32 devices in a mesh: lvl: 4 (over y, x), prow: 4 (over z), pcol: 2 (over core).
Axes of the slice: x: 2, y: 2, z: 4, core: 2. Of those that a mesh axis runs over, the one named last changes fastest.
Arguments:
- rhs: float32 [4, 2, 1024, 256], P('lvl', 'pcol'), may hold values from -6 to 6
- diag_inverse: bfloat16 [4, 2, 1024, 1024], P('lvl', 'pcol', 'prow'), may hold values from -0.1875 to 0.1875
- off_tiles: bfloat16 [4, 2, 32, 32, 1024], P('lvl', 'pcol', 'prow'), may hold values from -0.625 to 0.625
- panel_super: int32 [4, 2, 8], P('lvl', 'pcol'), may hold values from 0 to 7, as said below
- off_device: int32 [4, 2, 32], P('lvl', 'pcol', 'prow'), may hold values from 0 to 7, as said below
- off_block: int32 [4, 2, 32], P('lvl', 'pcol', 'prow'), may hold values from 0 to 47, as said below
- offdiag_block_panel: int32 [4, 2, 32], P('lvl', 'pcol', 'prow'), may hold values from 0 to 7
Outputs:
- solution: float32 [4, 2, 1024, 256], P('lvl', 'pcol', 'prow')
- outer: float32 [4, 2, 512, 256], P('lvl', 'pcol')
The draws below stay inside these ranges and needn't reach their ends.
Inputs may be any that keep to these rules, and one draw needn't show every extreme that they name: `panel_super`: within a group ids start at 0 and rise by 0 or 1 from panel to panel; panels of one id form one supernode. `off_device`: one device sends at most 2 block rows to any one target group; some group receives 2 from every device. `off_block`: A block under 1024 / 32 (a window row) goes only to a group on a higher level than the sender's; the others are rows above the window.
All inputs are finite; a program needn't handle non-finite values.
Results may differ from the reference program's by a relative error of at most 0.0055.
Values may be sent and summed in bfloat16 or wider, within the bound.
No kernel may reach another device: no remote copies, remote signals or barrier semaphores. Data moves between devices by JAX's collectives and lax.ppermute only.
A program may use at most 64 MiB of HBM per device.

```python
import jax
import jax.numpy as jnp
from jax import lax

R = 256
PANEL = 128
NPANEL = 8
BR = 32
CW = 1024
ABOVE = 512
NT = 48
GROUPS = 8
OFF = 8
N_LVL = 4
N_PROW = 4
N_PCOL = 2


def draw_panel_super(key, part):
    offset_starts = jax.random.randint(jax.random.fold_in(key, 3), (N_LVL, N_PCOL, NPANEL), 0, 2)
    chosen = jax.random.randint(jax.random.fold_in(key, 4), (), 0, GROUPS)
    group_ids = jnp.arange(GROUPS, dtype=jnp.int32).reshape(N_LVL, N_PCOL)
    offset_starts = jnp.where((group_ids == chosen)[:, :, None], 1, offset_starts)
    offset_starts = offset_starts.at[:, :, 0].set(0)
    return jnp.cumsum(offset_starts, axis=-1).astype(jnp.int32)


def route_draw(key):
    base = jax.random.fold_in(key, 11)
    sending_supernodes = N_LVL * N_PCOL * N_PROW
    star = jax.random.randint(jax.random.fold_in(base, 1), (), 0, GROUPS)
    scores = jax.random.randint(jax.random.fold_in(base, 2), (sending_supernodes, GROUPS - 1), 0, 1 << 20) * GROUPS
    scores = scores + jnp.arange(GROUPS - 1, dtype=jnp.int32)[None, :]
    order = jnp.argsort(scores, axis=-1).astype(jnp.int32)
    others = (star + 1 + order) % GROUPS
    listing = jnp.concatenate([jnp.full((sending_supernodes, 1), star, jnp.int32), others.astype(jnp.int32)], axis=1)
    tile_ids = jnp.arange(OFF, dtype=jnp.int32)
    position = jnp.where(tile_ids < OFF // 2, tile_ids // 2, tile_ids - OFF // 4)
    targets = listing[:, position]
    mixing = jax.random.randint(jax.random.fold_in(base, 3), (sending_supernodes, OFF), 0, 1 << 20) * OFF
    mixing = mixing + tile_ids[None, :]
    shuffle = jnp.argsort(mixing, axis=-1)
    targets = jnp.take_along_axis(targets, shuffle, axis=-1)
    sender_level = jnp.arange(sending_supernodes, dtype=jnp.int32) // (N_PCOL * N_PROW)
    any_block = jax.random.randint(jax.random.fold_in(base, 4), (sending_supernodes, OFF), 0, NT)
    upper_block = CW // BR + jax.random.randint(jax.random.fold_in(base, 5), (sending_supernodes, OFF), 0, ABOVE // BR)
    blocks = jnp.where(targets // N_PCOL > sender_level[:, None], any_block, upper_block)
    targets = targets.reshape(N_LVL, N_PCOL, N_PROW * OFF).astype(jnp.int32)
    blocks = blocks.reshape(N_LVL, N_PCOL, N_PROW * OFF).astype(jnp.int32)
    return (targets, blocks)


def draw_off_device(key, part):
    return route_draw(key)[0]


def draw_off_block(key, part):
    return route_draw(key)[1]


def plant(array, key, least, high):
    longest = array.shape.index(max(array.shape))
    spots = []
    for shift in (0, 1):
        where = [jax.random.randint(jax.random.fold_in(key, axis), (), 0, length) for axis, length in enumerate(array.shape)]
        where[longest] = (where[longest] + shift) % array.shape[longest]
        spots.append(tuple(where))
    return array.at[spots[0]].set(least).at[spots[1]].set(high)


def block_levels(own_key, dims, shards, least, largest):
    level, own = 1.0, jax.random.fold_in(own_key, 6)
    for dim, shards_of in shards:
        steps = jnp.exp(jax.random.uniform(jax.random.fold_in(own, dim), (shards_of,), jnp.float32, least / len(shards), largest / len(shards)))
        level = level * jnp.repeat(steps, dims[dim] // shards_of).reshape([-1 if axis == dim else 1 for axis in range(len(dims))])
    return level


def normal_values(own_key, dims, deviation, bound, split=(), kind=jnp.bfloat16):
    array = deviation * jax.random.normal(own_key, dims, jnp.float32)
    if split:
        array = array * block_levels(own_key, dims, split, -0.22, 0.18)
    return jnp.clip(array, -bound, bound).astype(kind)


def setup_inputs(seed: int = 0) -> dict:
    key_list = jax.random.split(jax.random.key(seed), 8)
    return {
        "rhs": normal_values(key_list[0], (N_LVL, N_PCOL, CW, R), 1.0, 6.0, ((0, 4), (1, 2)), jnp.float32),
        "diag_inverse": normal_values(key_list[1], (N_LVL, N_PCOL, CW, CW), CW ** -0.5, 0.1875, ((0, 4), (1, 2), (2, 4))),
        "off_tiles": normal_values(key_list[2], (N_LVL, N_PCOL, N_PROW * OFF, BR, CW), (CW // 12) ** -0.5, 0.625, ((0, 4), (1, 2), (2, 4))),
        "panel_super": draw_panel_super(jax.random.fold_in(key_list[7], 71), 0),
        "off_device": draw_off_device(jax.random.fold_in(key_list[7], 71), 0),
        "off_block": draw_off_block(jax.random.fold_in(key_list[7], 71), 0),
        "offdiag_block_panel": plant(jax.random.randint(key_list[6], (N_LVL, N_PCOL, N_PROW * OFF), 0, NPANEL), jax.random.fold_in(key_list[6], 1), 0, NPANEL - 1).astype(jnp.int32),
    }


def reference(rhs, diag_inverse, off_tiles, panel_super, off_device, off_block, offdiag_block_panel):
    col_super = jnp.repeat(panel_super, PANEL, axis=-1)
    right = rhs
    outer = jnp.zeros((N_LVL, N_PCOL, ABOVE, R), jnp.float32)
    solution = jnp.zeros((N_LVL, N_PCOL, CW, R), jnp.float32)
    for current in range(N_LVL):
        group_super = col_super[current]
        same = group_super[:, :, None] == group_super[:, None, :]
        inverse_used = jnp.where(same, diag_inverse[current], jnp.zeros((), jnp.bfloat16))
        rounded = right[current].astype(jnp.bfloat16)
        solved = jnp.einsum("qij,qjr->qir", inverse_used.astype(jnp.float32), rounded.astype(jnp.float32))
        solution = solution.at[current].set(solved)
        solved_half = solved.astype(jnp.bfloat16)
        tile_supernode = jnp.take_along_axis(panel_super[current], offdiag_block_panel[current], axis=1)
        tile_mask = group_super[:, None, :] == tile_supernode[:, :, None]

        def single_group_entry(items):
            tiles, mask, vector = items
            used = jnp.where(mask[:, None, :], tiles, jnp.zeros((), jnp.bfloat16))
            product = jnp.einsum("kbc,cr->kbr", used.astype(jnp.float32), vector.astype(jnp.float32))
            return product.astype(jnp.bfloat16)

        updates = lax.map(single_group_entry, (off_tiles[current], tile_mask, solved_half))
        updates = lax.optimization_barrier(updates).astype(jnp.float32)
        target = off_device[current]
        target_block = off_block[current]
        summed = jnp.zeros((GROUPS, NT, BR, R), jnp.float32)
        summed = summed.at[target, target_block].add(updates)
        summed = summed.reshape(N_LVL, N_PCOL, NT * BR, R)
        right = right - summed[:, :, :CW, :]
        outer = outer + summed[:, :, CW:, :]
    return solution, outer
```

```python
import jax
import jax.numpy as jnp
from jax import lax
from jax.sharding import PartitionSpec as P

CAP = 2
ABOVE = 512
NT = 48


def per_device(
    rhs, diag_inverse, off_tiles, panel_super, off_device, off_block, offdiag_block_panel
):
    n_lvl = lax.axis_size("lvl")
    n_pcol = lax.axis_size("pcol")
    n_prow = lax.axis_size("prow")
    groups = n_lvl * n_pcol
    level_index = lax.axis_index("lvl")
    row_index = lax.axis_index("prow")
    col_index = lax.axis_index("pcol")
    my_group = level_index * n_pcol + col_index
    width = rhs.shape[2]
    columns_all = rhs.shape[3]
    cols = columns_all // n_prow
    row_count = diag_inverse.shape[2]
    tile_count = off_tiles.shape[2]
    block_rows = off_tiles.shape[3]
    group_tiles = n_prow * tile_count
    slots = n_prow * CAP

    panels = panel_super[0, 0]
    panel_cols = width // panels.shape[0]
    col_super = jnp.repeat(panels, panel_cols)
    row_ids = row_index * row_count + jnp.arange(row_count, dtype=jnp.int32)
    row_super = jnp.take(col_super, row_ids)
    inverse = jnp.where(
        row_super[:, None] == col_super[None, :], diag_inverse[0, 0], jnp.zeros((), jnp.bfloat16)
    )
    tile_supernode = jnp.take(panels, offdiag_block_panel[0, 0])
    tiles_used = jnp.where(
        col_super[None, None, :] == tile_supernode[:, None, None],
        off_tiles[0, 0],
        jnp.zeros((), jnp.bfloat16),
    ).reshape(tile_count * block_rows, width)

    both = jnp.concatenate([inverse, tiles_used], axis=0)
    gathered = lax.all_gather(both, "prow", axis=0)
    inv_full = gathered[:, :row_count].reshape(n_prow * row_count, width)
    tiles_full = gathered[:, row_count:].reshape(group_tiles * block_rows, width)

    meta = jnp.stack([off_device[0, 0], off_block[0, 0]], axis=0)
    meta = lax.all_gather(meta, ("lvl", "pcol", "prow"), axis=0)
    meta = meta.reshape(groups, n_prow, 2, tile_count)
    target = jnp.transpose(meta[:, :, 0, :], (0, 1, 2)).reshape(groups, group_tiles)
    block = meta[:, :, 1, :].reshape(groups, group_tiles)
    tile_ids = jnp.arange(group_tiles, dtype=jnp.int32)
    source_row = tile_ids // tile_count
    earlier = (
        (target[:, :, None] == target[:, None, :])
        & (source_row[:, None] == source_row[None, :])[None]
        & (tile_ids[:, None] > tile_ids[None, :])[None]
    )
    position = jnp.sum(earlier.astype(jnp.int32), axis=2)
    local_slot = source_row[None, :] * CAP + position

    my_target = jnp.take(target, my_group, axis=0)
    my_slot = my_target * slots + jnp.take(local_slot, my_group, axis=0)
    send_pick = (
        my_slot[None, :] == jnp.arange(groups * slots, dtype=jnp.int32)[:, None]
    ).astype(jnp.bfloat16)

    to_me = target == my_group
    block_ids = jnp.arange(NT, dtype=jnp.int32)
    slot_ids = jnp.arange(slots, dtype=jnp.int32)
    pick = (
        to_me[:, None, None, :]
        & (local_slot[:, None, None, :] == slot_ids[None, None, :, None])
        & (block[:, None, None, :] == block_ids[None, :, None, None])
    )
    recv_pick = jnp.any(pick, axis=3).astype(jnp.bfloat16)
    recv_pick = recv_pick.reshape(n_lvl, n_pcol, NT, slots)
    recv_pick = jnp.transpose(recv_pick, (0, 2, 1, 3)).reshape(n_lvl, NT, n_pcol * slots)

    right = lax.dynamic_slice_in_dim(rhs[0, 0], row_index * cols, cols, axis=1)
    outer = jnp.zeros((ABOVE, cols), jnp.float32)
    solved = jnp.zeros((width, cols), jnp.float32)
    for section in range(n_lvl):
        solved_now = jnp.dot(
            inv_full, right.astype(jnp.bfloat16), preferred_element_type=jnp.float32
        )
        solved = jnp.where(level_index == section, solved_now, solved)
        updates = jnp.dot(
            tiles_full, solved_now.astype(jnp.bfloat16), preferred_element_type=jnp.float32
        ).astype(jnp.bfloat16)
        updates = updates.reshape(group_tiles, block_rows * cols)
        sending = jnp.dot(send_pick, updates, preferred_element_type=jnp.float32)
        sending = sending.astype(jnp.bfloat16).reshape(groups * slots, block_rows, cols)
        incoming = lax.all_to_all(
            sending, ("lvl", "pcol"), split_axis=0, concat_axis=0, tiled=True
        )
        incoming = incoming.reshape(n_lvl, n_pcol * slots, block_rows * cols)[section]
        summed = jnp.dot(recv_pick[section], incoming, preferred_element_type=jnp.float32)
        summed = summed.reshape(NT * block_rows, cols)
        right = right - summed[:width]
        outer = outer + summed[width:]

    rows_out = width // n_prow
    final = jnp.concatenate(
        [
            solved.reshape(n_prow, rows_out, cols),
            jnp.broadcast_to(outer[None], (n_prow, ABOVE, cols)),
        ],
        axis=1,
    )
    final = lax.all_to_all(final, "prow", split_axis=0, concat_axis=0, tiled=True)
    solution_rows = jnp.transpose(final[:, :rows_out], (1, 0, 2)).reshape(rows_out, columns_all)
    outer_all = jnp.transpose(final[:, rows_out:], (1, 0, 2)).reshape(ABOVE, columns_all)
    return (solution_rows[None, None], outer_all[None, None])


def solution(mesh):
    placed = (
        P("lvl", "pcol", None, None),
        P("lvl", "pcol", "prow", None),
        P("lvl", "pcol", "prow", None, None),
        P("lvl", "pcol", None),
        P("lvl", "pcol", "prow"),
        P("lvl", "pcol", "prow"),
        P("lvl", "pcol", "prow"),
    )
    return jax.shard_map(
        per_device,
        mesh=mesh,
        in_specs=placed,
        out_specs=(P("lvl", "pcol", "prow", None), P("lvl", "pcol", None, None)),
        check_vma=False,
    )
```

```python
import jax
import jax.numpy as jnp
from jax import lax
from jax.sharding import PartitionSpec as P

CAP = 2
ABOVE = 512
NT = 48


def per_device(
    rhs, diag_inverse, off_tiles, panel_super, off_device, off_block, offdiag_block_panel
):
    n_lvl = lax.axis_size("lvl")
    n_pcol = lax.axis_size("pcol")
    n_prow = lax.axis_size("prow")
    groups = n_lvl * n_pcol
    level_index = lax.axis_index("lvl")
    row_index = lax.axis_index("prow")
    col_index = lax.axis_index("pcol")
    my_group = level_index * n_pcol + col_index
    width = rhs.shape[2]
    columns_all = rhs.shape[3]
    cols = columns_all // n_prow
    row_count = diag_inverse.shape[2]
    tile_count = off_tiles.shape[2]
    block_rows = off_tiles.shape[3]
    group_tiles = n_prow * tile_count
    slots = n_prow * CAP

    panels = panel_super[0, 0]
    panel_cols = width // panels.shape[0]
    col_super = jnp.repeat(panels, panel_cols)
    row_ids = row_index * row_count + jnp.arange(row_count, dtype=jnp.int32)
    row_super = jnp.take(col_super, row_ids)
    inverse = jnp.where(
        row_super[:, None] == col_super[None, :], diag_inverse[0, 0], jnp.zeros((), jnp.bfloat16)
    )
    tile_supernode = jnp.take(panels, offdiag_block_panel[0, 0])
    tiles_used = jnp.where(
        col_super[None, None, :] == tile_supernode[:, None, None],
        off_tiles[0, 0],
        jnp.zeros((), jnp.bfloat16),
    ).reshape(tile_count * block_rows, width)

    both = jnp.concatenate([inverse, tiles_used], axis=0)
    gathered = lax.all_gather(both, "prow", axis=0)
    inv_full = gathered[:, :row_count].reshape(n_prow * row_count, width)
    tiles_full = gathered[:, row_count:].reshape(group_tiles * block_rows, width)
    tiles_full = jnp.concatenate(
        [tiles_full, jnp.zeros((block_rows, width), jnp.bfloat16)], axis=0
    )

    meta = jnp.stack([off_device[0, 0], off_block[0, 0]], axis=0)
    meta = lax.all_gather(meta, ("lvl", "prow", "pcol"), axis=0)
    meta = meta.reshape(n_lvl, n_prow, n_pcol, 2, tile_count)
    meta = jnp.transpose(meta, (0, 2, 1, 3, 4)).reshape(groups, n_prow, 2, tile_count)
    target = meta[:, :, 0, :].reshape(groups, group_tiles)
    block = meta[:, :, 1, :].reshape(groups, group_tiles)
    tile_ids = jnp.arange(group_tiles, dtype=jnp.int32)
    source_row = tile_ids // tile_count
    earlier = (
        (target[:, :, None] == target[:, None, :])
        & (source_row[:, None] == source_row[None, :])[None]
        & (tile_ids[:, None] > tile_ids[None, :])[None]
    )
    position = jnp.sum(earlier.astype(jnp.int32), axis=2)
    local_slot = source_row[None, :] * CAP + position

    my_target = jnp.take(target, my_group, axis=0)
    my_slot = my_target * slots + jnp.take(local_slot, my_group, axis=0)
    send_match = my_slot[None, :] == jnp.arange(groups * slots, dtype=jnp.int32)[:, None]
    send_index = jnp.where(
        jnp.any(send_match, axis=1),
        jnp.sum(jnp.where(send_match, tile_ids[None, :], 0), axis=1),
        group_tiles,
    )

    to_me = target == my_group
    slot_ids = jnp.arange(slots, dtype=jnp.int32)
    pick = to_me[:, None, :] & (local_slot[:, None, :] == slot_ids[None, :, None])
    recv_block = jnp.where(
        jnp.any(pick, axis=2), jnp.sum(jnp.where(pick, block[:, None, :], 0), axis=2), NT
    )
    recv_block = recv_block.reshape(n_lvl, n_pcol * slots)

    right = lax.dynamic_slice_in_dim(rhs[0, 0], row_index * cols, cols, axis=1)
    outer = jnp.zeros((ABOVE, cols), jnp.float32)
    solved = jnp.zeros((width, cols), jnp.float32)
    for section in range(n_lvl):
        solved_now = jnp.dot(
            inv_full, right.astype(jnp.bfloat16), preferred_element_type=jnp.float32
        )
        solved = jnp.where(level_index == section, solved_now, solved)
        updates = jnp.dot(
            tiles_full, solved_now.astype(jnp.bfloat16), preferred_element_type=jnp.float32
        ).astype(jnp.bfloat16)
        updates = updates.reshape(group_tiles + 1, block_rows, cols)
        sending = jnp.take(updates, send_index, axis=0)
        incoming = lax.all_to_all(
            sending, ("lvl", "pcol"), split_axis=0, concat_axis=0, tiled=True
        )
        incoming = incoming.reshape(n_lvl, n_pcol * slots, block_rows, cols)[section]
        summed = jnp.zeros((NT + 1, block_rows, cols), jnp.float32)
        summed = summed.at[recv_block[section]].add(incoming.astype(jnp.float32))
        summed = summed[:NT].reshape(NT * block_rows, cols)
        right = right - summed[:width]
        outer = outer + summed[width:]

    rows_out = width // n_prow
    final = jnp.concatenate(
        [
            solved.reshape(n_prow, rows_out, cols),
            jnp.broadcast_to(outer[None], (n_prow, ABOVE, cols)),
        ],
        axis=1,
    )
    final = lax.all_to_all(final, "prow", split_axis=0, concat_axis=0, tiled=True)
    solution_rows = jnp.transpose(final[:, :rows_out], (1, 0, 2)).reshape(rows_out, columns_all)
    outer_all = jnp.transpose(final[:, rows_out:], (1, 0, 2)).reshape(ABOVE, columns_all)
    return (solution_rows[None, None], outer_all[None, None])


def solution(mesh):
    placed = (
        P("lvl", "pcol", None, None),
        P("lvl", "pcol", "prow", None),
        P("lvl", "pcol", "prow", None, None),
        P("lvl", "pcol", None),
        P("lvl", "pcol", "prow"),
        P("lvl", "pcol", "prow"),
        P("lvl", "pcol", "prow"),
    )
    return jax.shard_map(
        per_device,
        mesh=mesh,
        in_specs=placed,
        out_specs=(P("lvl", "pcol", "prow", None), P("lvl", "pcol", None, None)),
        check_vma=False,
    )
```

```python
import jax
import jax.numpy as jnp
from jax import lax
from jax.sharding import PartitionSpec as P

CAP = 2
ABOVE = 512
NT = 48


def per_device(
    rhs, diag_inverse, off_tiles, panel_super, off_device, off_block, offdiag_block_panel
):
    n_lvl = lax.axis_size("lvl")
    n_pcol = lax.axis_size("pcol")
    n_prow = lax.axis_size("prow")
    groups = n_lvl * n_pcol
    level_index = lax.axis_index("lvl")
    row_index = lax.axis_index("prow")
    col_index = lax.axis_index("pcol")
    my_group = level_index * n_pcol + col_index
    width = rhs.shape[2]
    columns_all = rhs.shape[3]
    cols = columns_all // n_prow
    row_count = diag_inverse.shape[2]
    tile_count = off_tiles.shape[2]
    block_rows = off_tiles.shape[3]
    group_tiles = n_prow * tile_count
    slots = n_prow * CAP

    panels = panel_super[0, 0]
    panel_cols = width // panels.shape[0]
    col_super = jnp.repeat(panels, panel_cols)
    row_ids = row_index * row_count + jnp.arange(row_count, dtype=jnp.int32)
    row_super = jnp.take(col_super, row_ids)
    inverse = jnp.where(
        row_super[:, None] == col_super[None, :], diag_inverse[0, 0], jnp.zeros((), jnp.bfloat16)
    )
    tile_supernode = jnp.take(panels, offdiag_block_panel[0, 0])
    tiles_used = jnp.where(
        col_super[None, None, :] == tile_supernode[:, None, None],
        off_tiles[0, 0],
        jnp.zeros((), jnp.bfloat16),
    ).reshape(tile_count * block_rows, width)

    inv_full = lax.all_gather(inverse, "prow", axis=0, tiled=True)
    tiles_full = lax.all_to_all(
        jnp.broadcast_to(tiles_used[None], (n_prow,) + tiles_used.shape),
        "prow",
        split_axis=0,
        concat_axis=0,
        tiled=True,
    ).reshape(group_tiles * block_rows, width)
    tiles_full = jnp.concatenate(
        [tiles_full, jnp.zeros((block_rows, width), jnp.bfloat16)], axis=0
    )

    meta = jnp.stack([off_device[0, 0], off_block[0, 0]], axis=0)
    meta = lax.all_gather(meta, ("lvl", "prow", "pcol"), axis=0)
    meta = meta.reshape(n_lvl, n_prow, n_pcol, 2, tile_count)
    meta = jnp.transpose(meta, (0, 2, 1, 3, 4)).reshape(groups, n_prow, 2, tile_count)
    target = meta[:, :, 0, :].reshape(groups, group_tiles)
    block = meta[:, :, 1, :].reshape(groups, group_tiles)
    tile_ids = jnp.arange(group_tiles, dtype=jnp.int32)
    source_row = tile_ids // tile_count
    earlier = (
        (target[:, :, None] == target[:, None, :])
        & (source_row[:, None] == source_row[None, :])[None]
        & (tile_ids[:, None] > tile_ids[None, :])[None]
    )
    position = jnp.sum(earlier.astype(jnp.int32), axis=2)
    local_slot = source_row[None, :] * CAP + position

    my_target = jnp.take(target, my_group, axis=0)
    my_slot = my_target * slots + jnp.take(local_slot, my_group, axis=0)
    send_match = my_slot[None, :] == jnp.arange(groups * slots, dtype=jnp.int32)[:, None]
    send_index = jnp.where(
        jnp.any(send_match, axis=1),
        jnp.sum(jnp.where(send_match, tile_ids[None, :], 0), axis=1),
        group_tiles,
    )

    to_me = target == my_group
    slot_ids = jnp.arange(slots, dtype=jnp.int32)
    pick = to_me[:, None, :] & (local_slot[:, None, :] == slot_ids[None, :, None])
    recv_block = jnp.where(
        jnp.any(pick, axis=2), jnp.sum(jnp.where(pick, block[:, None, :], 0), axis=2), NT
    )
    recv_block = recv_block.reshape(n_lvl, n_pcol * slots)

    right = lax.dynamic_slice_in_dim(rhs[0, 0], row_index * cols, cols, axis=1)
    outer = jnp.zeros((ABOVE, cols), jnp.float32)
    solved = jnp.zeros((width, cols), jnp.float32)
    for section in range(n_lvl):
        solved_now = jnp.dot(
            inv_full, right.astype(jnp.bfloat16), preferred_element_type=jnp.float32
        )
        solved = jnp.where(level_index == section, solved_now, solved)
        updates = jnp.dot(
            tiles_full, solved_now.astype(jnp.bfloat16), preferred_element_type=jnp.float32
        ).astype(jnp.bfloat16)
        updates = updates.reshape(group_tiles + 1, block_rows, cols)
        sending = jnp.take(updates, send_index, axis=0)
        incoming = lax.all_to_all(
            sending, ("lvl", "pcol"), split_axis=0, concat_axis=0, tiled=True
        )
        incoming = incoming.reshape(n_lvl, n_pcol * slots, block_rows, cols)[section]
        summed = jnp.zeros((NT + 1, block_rows, cols), jnp.float32)
        summed = summed.at[recv_block[section]].add(incoming.astype(jnp.float32))
        summed = summed[:NT].reshape(NT * block_rows, cols)
        right = right - summed[:width]
        outer = outer + summed[width:]

    rows_out = width // n_prow
    final = jnp.concatenate(
        [
            solved.reshape(n_prow, rows_out, cols),
            jnp.broadcast_to(outer[None], (n_prow, ABOVE, cols)),
        ],
        axis=1,
    )
    final = lax.all_to_all(final, "prow", split_axis=0, concat_axis=0, tiled=True)
    solution_rows = jnp.transpose(final[:, :rows_out], (1, 0, 2)).reshape(rows_out, columns_all)
    outer_all = jnp.transpose(final[:, rows_out:], (1, 0, 2)).reshape(ABOVE, columns_all)
    return (solution_rows[None, None], outer_all[None, None])


def solution(mesh):
    placed = (
        P("lvl", "pcol", None, None),
        P("lvl", "pcol", "prow", None),
        P("lvl", "pcol", "prow", None, None),
        P("lvl", "pcol", None),
        P("lvl", "pcol", "prow"),
        P("lvl", "pcol", "prow"),
        P("lvl", "pcol", "prow"),
    )
    return jax.shard_map(
        per_device,
        mesh=mesh,
        in_specs=placed,
        out_specs=(P("lvl", "pcol", "prow", None), P("lvl", "pcol", None, None)),
        check_vma=False,
    )
```

```python
import jax
import jax.numpy as jnp
from jax import lax
from jax.sharding import PartitionSpec as P

CAP = 2
ABOVE = 512
NT = 48


def per_device(
    rhs, diag_inverse, off_tiles, panel_super, off_device, off_block, offdiag_block_panel
):
    n_lvl = lax.axis_size("lvl")
    n_pcol = lax.axis_size("pcol")
    n_prow = lax.axis_size("prow")
    groups = n_lvl * n_pcol
    level_index = lax.axis_index("lvl")
    row_index = lax.axis_index("prow")
    col_index = lax.axis_index("pcol")
    my_group = level_index * n_pcol + col_index
    width = rhs.shape[2]
    columns_all = rhs.shape[3]
    cols = columns_all // n_prow
    row_count = diag_inverse.shape[2]
    tile_count = off_tiles.shape[2]
    block_rows = off_tiles.shape[3]
    group_tiles = n_prow * tile_count
    slots = n_prow * CAP

    panels = panel_super[0, 0]
    panel_cols = width // panels.shape[0]
    col_super = jnp.repeat(panels, panel_cols)
    row_ids = row_index * row_count + jnp.arange(row_count, dtype=jnp.int32)
    row_super = jnp.take(col_super, row_ids)
    inverse = jnp.where(
        row_super[:, None] == col_super[None, :], diag_inverse[0, 0], jnp.zeros((), jnp.bfloat16)
    )
    tile_supernode = jnp.take(panels, offdiag_block_panel[0, 0])
    tiles_used = jnp.where(
        col_super[None, None, :] == tile_supernode[:, None, None],
        off_tiles[0, 0],
        jnp.zeros((), jnp.bfloat16),
    ).reshape(tile_count * block_rows, width)

    meta_rows = jnp.zeros((16, width), jnp.bfloat16)
    meta_rows = meta_rows.at[0, :tile_count].set(off_device[0, 0].astype(jnp.bfloat16))
    meta_rows = meta_rows.at[1, :tile_count].set(off_block[0, 0].astype(jnp.bfloat16))
    both = jnp.concatenate([inverse, tiles_used, meta_rows], axis=0)
    gathered = lax.all_gather(both, "prow", axis=0)
    inv_full = gathered[:, :row_count].reshape(n_prow * row_count, width)
    tile_end = row_count + tile_count * block_rows
    tiles_full = gathered[:, row_count:tile_end].reshape(group_tiles * block_rows, width)
    tiles_full = jnp.concatenate(
        [tiles_full, jnp.zeros((block_rows, width), jnp.bfloat16)], axis=0
    )
    meta = gathered[:, tile_end : tile_end + 2, :tile_count].astype(jnp.int32)
    target = meta[:, 0, :].reshape(group_tiles)
    block = meta[:, 1, :].reshape(group_tiles)

    tile_ids = jnp.arange(group_tiles, dtype=jnp.int32)
    source_row = tile_ids // tile_count
    earlier = (
        (target[:, None] == target[None, :])
        & (source_row[:, None] == source_row[None, :])
        & (tile_ids[:, None] > tile_ids[None, :])
    )
    position = jnp.sum(earlier.astype(jnp.int32), axis=1)
    my_slot = target * slots + source_row * CAP + position

    send_match = my_slot[None, :] == jnp.arange(groups * slots, dtype=jnp.int32)[:, None]
    filled = jnp.any(send_match, axis=1)
    send_index = jnp.where(
        filled, jnp.sum(jnp.where(send_match, tile_ids[None, :], 0), axis=1), group_tiles
    )
    slot_block = jnp.where(filled, jnp.take(block, jnp.minimum(send_index, group_tiles - 1)), NT)
    recv_block = lax.all_to_all(
        slot_block.reshape(groups, slots), ("lvl", "pcol"), split_axis=0, concat_axis=0, tiled=True
    )
    recv_block = recv_block.reshape(n_lvl, n_pcol * slots)

    right = lax.dynamic_slice_in_dim(rhs[0, 0], row_index * cols, cols, axis=1)
    outer = jnp.zeros((ABOVE, cols), jnp.float32)
    solved = jnp.zeros((width, cols), jnp.float32)
    for section in range(n_lvl):
        solved_now = jnp.dot(
            inv_full, right.astype(jnp.bfloat16), preferred_element_type=jnp.float32
        )
        solved = jnp.where(level_index == section, solved_now, solved)
        updates = jnp.dot(
            tiles_full, solved_now.astype(jnp.bfloat16), preferred_element_type=jnp.float32
        ).astype(jnp.bfloat16)
        updates = updates.reshape(group_tiles + 1, block_rows, cols)
        sending = jnp.take(updates, send_index, axis=0)
        incoming = lax.all_to_all(
            sending, ("lvl", "pcol"), split_axis=0, concat_axis=0, tiled=True
        )
        incoming = incoming.reshape(n_lvl, n_pcol * slots, block_rows, cols)[section]
        summed = jnp.zeros((NT + 1, block_rows, cols), jnp.float32)
        summed = summed.at[recv_block[section]].add(incoming.astype(jnp.float32))
        summed = summed[:NT].reshape(NT * block_rows, cols)
        right = right - summed[:width]
        outer = outer + summed[width:]

    rows_out = width // n_prow
    final = jnp.concatenate(
        [
            solved.reshape(n_prow, rows_out, cols),
            jnp.broadcast_to(outer[None], (n_prow, ABOVE, cols)),
        ],
        axis=1,
    )
    final = lax.all_to_all(final, "prow", split_axis=0, concat_axis=0, tiled=True)
    solution_rows = jnp.transpose(final[:, :rows_out], (1, 0, 2)).reshape(rows_out, columns_all)
    outer_all = jnp.transpose(final[:, rows_out:], (1, 0, 2)).reshape(ABOVE, columns_all)
    return (solution_rows[None, None], outer_all[None, None])


def solution(mesh):
    placed = (
        P("lvl", "pcol", None, None),
        P("lvl", "pcol", "prow", None),
        P("lvl", "pcol", "prow", None, None),
        P("lvl", "pcol", None),
        P("lvl", "pcol", "prow"),
        P("lvl", "pcol", "prow"),
        P("lvl", "pcol", "prow"),
    )
    return jax.shard_map(
        per_device,
        mesh=mesh,
        in_specs=placed,
        out_specs=(P("lvl", "pcol", "prow", None), P("lvl", "pcol", None, None)),
        check_vma=False,
    )
```

```python
import jax
import jax.numpy as jnp
from jax import lax
from jax.sharding import PartitionSpec as P

CAP = 2
ABOVE = 512
NT = 48


def per_device(
    rhs, diag_inverse, off_tiles, panel_super, off_device, off_block, offdiag_block_panel
):
    n_lvl = lax.axis_size("lvl")
    n_pcol = lax.axis_size("pcol")
    n_prow = lax.axis_size("prow")
    groups = n_lvl * n_pcol
    level_index = lax.axis_index("lvl")
    row_index = lax.axis_index("prow")
    col_index = lax.axis_index("pcol")
    my_group = level_index * n_pcol + col_index
    width = rhs.shape[2]
    columns_all = rhs.shape[3]
    cols = columns_all // n_prow
    row_count = diag_inverse.shape[2]
    tile_count = off_tiles.shape[2]
    block_rows = off_tiles.shape[3]
    group_tiles = n_prow * tile_count
    slots = n_prow * CAP

    panels = panel_super[0, 0]
    panel_count = panels.shape[0]
    panel_cols = width // panel_count
    panel_ids = jnp.arange(panel_count, dtype=jnp.int32)

    def super_of(panel):
        hit = panel[..., None] == panel_ids
        return jnp.sum(jnp.where(hit, panels, 0), axis=-1)

    col_super = super_of(jnp.arange(width, dtype=jnp.int32) // panel_cols)
    row_ids = row_index * row_count + jnp.arange(row_count, dtype=jnp.int32)
    row_super = super_of(row_ids // panel_cols)
    inverse = jnp.where(
        row_super[:, None] == col_super[None, :], diag_inverse[0, 0], jnp.zeros((), jnp.bfloat16)
    )
    tile_supernode = super_of(offdiag_block_panel[0, 0])
    tiles_used = jnp.where(
        col_super[None, None, :] == tile_supernode[:, None, None],
        off_tiles[0, 0],
        jnp.zeros((), jnp.bfloat16),
    ).reshape(tile_count * block_rows, width)

    both = jnp.concatenate([inverse, tiles_used], axis=0)
    gathered = lax.all_gather(both, "prow", axis=0)
    inv_full = gathered[:, :row_count].reshape(n_prow * row_count, width)
    tiles_full = gathered[:, row_count:].reshape(group_tiles * block_rows, width)
    tiles_full = jnp.concatenate(
        [tiles_full, jnp.zeros((block_rows, width), jnp.bfloat16)], axis=0
    )

    meta = jnp.stack([off_device[0, 0], off_block[0, 0]], axis=0)
    meta = lax.all_gather(meta, ("lvl", "prow", "pcol"), axis=0)
    meta = meta.reshape(n_lvl, n_prow, n_pcol, 2, tile_count)
    meta = jnp.transpose(meta, (0, 2, 1, 3, 4)).reshape(groups, n_prow, 2, tile_count)
    target = meta[:, :, 0, :].reshape(groups, group_tiles)
    block = meta[:, :, 1, :].reshape(groups, group_tiles)
    tile_ids = jnp.arange(group_tiles, dtype=jnp.int32)
    source_row = tile_ids // tile_count
    earlier = (
        (target[:, :, None] == target[:, None, :])
        & (source_row[:, None] == source_row[None, :])[None]
        & (tile_ids[:, None] > tile_ids[None, :])[None]
    )
    position = jnp.sum(earlier.astype(jnp.int32), axis=2)
    local_slot = source_row[None, :] * CAP + position

    my_target = jnp.take(target, my_group, axis=0)
    my_slot = my_target * slots + jnp.take(local_slot, my_group, axis=0)
    send_match = my_slot[None, :] == jnp.arange(groups * slots, dtype=jnp.int32)[:, None]
    send_index = jnp.where(
        jnp.any(send_match, axis=1),
        jnp.sum(jnp.where(send_match, tile_ids[None, :], 0), axis=1),
        group_tiles,
    )

    to_me = target == my_group
    slot_ids = jnp.arange(slots, dtype=jnp.int32)
    pick = to_me[:, None, :] & (local_slot[:, None, :] == slot_ids[None, :, None])
    recv_block = jnp.where(
        jnp.any(pick, axis=2), jnp.sum(jnp.where(pick, block[:, None, :], 0), axis=2), NT
    )
    recv_block = recv_block.reshape(n_lvl, n_pcol * slots)

    rhs_cols = lax.dynamic_slice_in_dim(rhs[0, 0], row_index * cols, cols, axis=1)
    window_blocks = width // block_rows
    acc = jnp.zeros((NT + 1, block_rows, cols), jnp.float32)
    solved = jnp.zeros((width, cols), jnp.float32)
    for section in range(n_lvl):
        right = rhs_cols - acc[:window_blocks].reshape(width, cols)
        solved_now = jnp.dot(
            inv_full, right.astype(jnp.bfloat16), preferred_element_type=jnp.float32
        )
        solved = jnp.where(level_index == section, solved_now, solved)
        updates = jnp.dot(
            tiles_full, solved_now.astype(jnp.bfloat16), preferred_element_type=jnp.float32
        ).astype(jnp.bfloat16)
        updates = updates.reshape(group_tiles + 1, block_rows, cols)
        sending = jnp.take(updates, send_index, axis=0, mode="clip")
        incoming = lax.all_to_all(
            sending, ("lvl", "pcol"), split_axis=0, concat_axis=0, tiled=True
        )
        incoming = incoming.reshape(n_lvl, n_pcol * slots, block_rows, cols)[section]
        acc = acc.at[recv_block[section]].add(incoming.astype(jnp.float32), mode="clip")
    outer = acc[window_blocks:NT].reshape(ABOVE, cols)

    rows_out = width // n_prow
    final = jnp.concatenate(
        [
            solved.reshape(n_prow, rows_out, cols),
            jnp.broadcast_to(outer[None], (n_prow, ABOVE, cols)),
        ],
        axis=1,
    )
    final = lax.all_to_all(final, "prow", split_axis=0, concat_axis=0, tiled=True)
    solution_rows = jnp.transpose(final[:, :rows_out], (1, 0, 2)).reshape(rows_out, columns_all)
    outer_all = jnp.transpose(final[:, rows_out:], (1, 0, 2)).reshape(ABOVE, columns_all)
    return (solution_rows[None, None], outer_all[None, None])


def solution(mesh):
    placed = (
        P("lvl", "pcol", None, None),
        P("lvl", "pcol", "prow", None),
        P("lvl", "pcol", "prow", None, None),
        P("lvl", "pcol", None),
        P("lvl", "pcol", "prow"),
        P("lvl", "pcol", "prow"),
        P("lvl", "pcol", "prow"),
    )
    return jax.shard_map(
        per_device,
        mesh=mesh,
        in_specs=placed,
        out_specs=(P("lvl", "pcol", "prow", None), P("lvl", "pcol", None, None)),
        check_vma=False,
    )
```

```python
import jax
import jax.numpy as jnp
from jax import lax
from jax.sharding import PartitionSpec as P

CAP = 2
ABOVE = 512
NT = 48


def per_device(
    rhs, diag_inverse, off_tiles, panel_super, off_device, off_block, offdiag_block_panel
):
    n_lvl = lax.axis_size("lvl")
    n_pcol = lax.axis_size("pcol")
    n_prow = lax.axis_size("prow")
    groups = n_lvl * n_pcol
    level_index = lax.axis_index("lvl")
    row_index = lax.axis_index("prow")
    col_index = lax.axis_index("pcol")
    my_group = level_index * n_pcol + col_index
    width = rhs.shape[2]
    columns_all = rhs.shape[3]
    cols = columns_all // n_prow
    row_count = diag_inverse.shape[2]
    tile_count = off_tiles.shape[2]
    block_rows = off_tiles.shape[3]
    group_tiles = n_prow * tile_count
    slots = n_prow * CAP

    panels = panel_super[0, 0]
    panel_count = panels.shape[0]
    panel_cols = width // panel_count
    panel_ids = jnp.arange(panel_count, dtype=jnp.int32)

    def super_of(panel):
        hit = panel[..., None] == panel_ids
        return jnp.sum(jnp.where(hit, panels, 0), axis=-1)

    col_super = super_of(jnp.arange(width, dtype=jnp.int32) // panel_cols)
    row_ids = row_index * row_count + jnp.arange(row_count, dtype=jnp.int32)
    row_super = super_of(row_ids // panel_cols)
    inverse = jnp.where(
        row_super[:, None] == col_super[None, :], diag_inverse[0, 0], jnp.zeros((), jnp.bfloat16)
    )
    tile_supernode = super_of(offdiag_block_panel[0, 0])
    tiles_used = jnp.where(
        col_super[None, None, :] == tile_supernode[:, None, None],
        off_tiles[0, 0],
        jnp.zeros((), jnp.bfloat16),
    ).reshape(tile_count * block_rows, width)

    tiles_full = lax.all_gather(tiles_used, "prow", axis=0, tiled=True)
    inverse, tiles_full = lax.optimization_barrier((inverse, tiles_full))
    inv_full = lax.all_gather(inverse, "prow", axis=0, tiled=True)
    tiles_full = jnp.concatenate(
        [tiles_full, jnp.zeros((block_rows, width), jnp.bfloat16)], axis=0
    )

    meta = jnp.stack([off_device[0, 0], off_block[0, 0]], axis=0)
    meta = lax.all_gather(meta, ("lvl", "prow", "pcol"), axis=0)
    meta = meta.reshape(n_lvl, n_prow, n_pcol, 2, tile_count)
    meta = jnp.transpose(meta, (0, 2, 1, 3, 4)).reshape(groups, n_prow, 2, tile_count)
    target = meta[:, :, 0, :].reshape(groups, group_tiles)
    block = meta[:, :, 1, :].reshape(groups, group_tiles)
    tile_ids = jnp.arange(group_tiles, dtype=jnp.int32)
    source_row = tile_ids // tile_count
    earlier = (
        (target[:, :, None] == target[:, None, :])
        & (source_row[:, None] == source_row[None, :])[None]
        & (tile_ids[:, None] > tile_ids[None, :])[None]
    )
    position = jnp.sum(earlier.astype(jnp.int32), axis=2)
    local_slot = source_row[None, :] * CAP + position

    my_target = jnp.take(target, my_group, axis=0)
    my_slot = my_target * slots + jnp.take(local_slot, my_group, axis=0)
    send_match = my_slot[None, :] == jnp.arange(groups * slots, dtype=jnp.int32)[:, None]
    send_index = jnp.where(
        jnp.any(send_match, axis=1),
        jnp.sum(jnp.where(send_match, tile_ids[None, :], 0), axis=1),
        group_tiles,
    )

    to_me = target == my_group
    slot_ids = jnp.arange(slots, dtype=jnp.int32)
    pick = to_me[:, None, :] & (local_slot[:, None, :] == slot_ids[None, :, None])
    recv_block = jnp.where(
        jnp.any(pick, axis=2), jnp.sum(jnp.where(pick, block[:, None, :], 0), axis=2), NT
    )
    recv_block = recv_block.reshape(n_lvl, n_pcol * slots)

    rhs_cols = lax.dynamic_slice_in_dim(rhs[0, 0], row_index * cols, cols, axis=1)
    window_blocks = width // block_rows
    acc = jnp.zeros((NT + 1, block_rows, cols), jnp.float32)
    solved = jnp.zeros((width, cols), jnp.float32)
    rows_out = width // n_prow
    first_rows = jnp.dot(
        inverse, rhs[0, 0].astype(jnp.bfloat16), preferred_element_type=jnp.float32
    )
    first_half = first_rows.astype(jnp.bfloat16).reshape(rows_out, n_prow, cols)
    first_cols = lax.all_to_all(
        jnp.transpose(first_half, (1, 0, 2)), "prow", split_axis=0, concat_axis=0, tiled=True
    ).reshape(width, cols)
    for section in range(n_lvl):
        if section == 0:
            solved_half = first_cols
        else:
            right = rhs_cols - acc[:window_blocks].reshape(width, cols)
            solved_now = jnp.dot(
                inv_full, right.astype(jnp.bfloat16), preferred_element_type=jnp.float32
            )
            solved = jnp.where(level_index == section, solved_now, solved)
            solved_half = solved_now.astype(jnp.bfloat16)
        updates = jnp.dot(
            tiles_full, solved_half, preferred_element_type=jnp.float32
        ).astype(jnp.bfloat16)
        updates = updates.reshape(group_tiles + 1, block_rows, cols)
        sending = jnp.take(updates, send_index, axis=0, mode="clip")
        incoming = lax.all_to_all(
            sending, ("lvl", "pcol"), split_axis=0, concat_axis=0, tiled=True
        )
        incoming = incoming.reshape(n_lvl, n_pcol * slots, block_rows, cols)[section]
        acc = acc.at[recv_block[section]].add(incoming.astype(jnp.float32), mode="clip")
    outer = acc[window_blocks:NT].reshape(ABOVE, cols)

    final = jnp.concatenate(
        [
            solved.reshape(n_prow, rows_out, cols),
            jnp.broadcast_to(outer[None], (n_prow, ABOVE, cols)),
        ],
        axis=1,
    )
    final = lax.all_to_all(final, "prow", split_axis=0, concat_axis=0, tiled=True)
    solution_rows = jnp.transpose(final[:, :rows_out], (1, 0, 2)).reshape(rows_out, columns_all)
    solution_rows = jnp.where(level_index == 0, first_rows, solution_rows)
    outer_all = jnp.transpose(final[:, rows_out:], (1, 0, 2)).reshape(ABOVE, columns_all)
    return (solution_rows[None, None], outer_all[None, None])


def solution(mesh):
    placed = (
        P("lvl", "pcol", None, None),
        P("lvl", "pcol", "prow", None),
        P("lvl", "pcol", "prow", None, None),
        P("lvl", "pcol", None),
        P("lvl", "pcol", "prow"),
        P("lvl", "pcol", "prow"),
        P("lvl", "pcol", "prow"),
    )
    return jax.shard_map(
        per_device,
        mesh=mesh,
        in_specs=placed,
        out_specs=(P("lvl", "pcol", "prow", None), P("lvl", "pcol", None, None)),
        check_vma=False,
    )
```

```python
import jax
import jax.numpy as jnp
from jax import lax
from jax.sharding import PartitionSpec as P

CAP = 2
ABOVE = 512
NT = 48


def per_device(
    rhs, diag_inverse, off_tiles, panel_super, off_device, off_block, offdiag_block_panel
):
    n_lvl = lax.axis_size("lvl")
    n_pcol = lax.axis_size("pcol")
    n_prow = lax.axis_size("prow")
    groups = n_lvl * n_pcol
    level_index = lax.axis_index("lvl")
    row_index = lax.axis_index("prow")
    col_index = lax.axis_index("pcol")
    my_group = level_index * n_pcol + col_index
    width = rhs.shape[2]
    columns_all = rhs.shape[3]
    cols = columns_all // n_prow
    row_count = diag_inverse.shape[2]
    tile_count = off_tiles.shape[2]
    block_rows = off_tiles.shape[3]
    group_tiles = n_prow * tile_count
    slots = n_prow * CAP

    panels = panel_super[0, 0]
    panel_count = panels.shape[0]
    panel_cols = width // panel_count
    panel_ids = jnp.arange(panel_count, dtype=jnp.int32)

    def super_of(panel):
        hit = panel[..., None] == panel_ids
        return jnp.sum(jnp.where(hit, panels, 0), axis=-1)

    col_super = super_of(jnp.arange(width, dtype=jnp.int32) // panel_cols)
    row_ids = row_index * row_count + jnp.arange(row_count, dtype=jnp.int32)
    row_super = super_of(row_ids // panel_cols)
    inverse = jnp.where(
        row_super[:, None] == col_super[None, :], diag_inverse[0, 0], jnp.zeros((), jnp.bfloat16)
    )
    tile_supernode = super_of(offdiag_block_panel[0, 0])
    tiles_used = jnp.where(
        col_super[None, None, :] == tile_supernode[:, None, None],
        off_tiles[0, 0],
        jnp.zeros((), jnp.bfloat16),
    ).reshape(tile_count * block_rows, width)

    tiles_full = lax.all_gather(tiles_used, "prow", axis=0, tiled=True)
    rows_out = width // n_prow
    first_rows = jnp.dot(
        inverse, rhs[0, 0].astype(jnp.bfloat16), preferred_element_type=jnp.float32
    )
    first_half = first_rows.astype(jnp.bfloat16).reshape(rows_out, n_prow, cols)
    first_cols = lax.all_to_all(
        jnp.transpose(first_half, (1, 0, 2)), "prow", split_axis=0, concat_axis=0, tiled=True
    ).reshape(width, cols)
    inverse, tiles_full, first_cols = lax.optimization_barrier((inverse, tiles_full, first_cols))
    inv_full = lax.all_gather(inverse, "prow", axis=0, tiled=True)
    tiles_full = jnp.concatenate(
        [tiles_full, jnp.zeros((block_rows, width), jnp.bfloat16)], axis=0
    )

    meta = jnp.stack([off_device[0, 0], off_block[0, 0]], axis=0)
    devices = n_lvl * n_prow * n_pcol
    meta = lax.all_to_all(
        jnp.broadcast_to(meta[None], (devices,) + meta.shape),
        ("lvl", "prow", "pcol"),
        split_axis=0,
        concat_axis=0,
        tiled=True,
    )
    meta = meta.reshape(n_lvl, n_prow, n_pcol, 2, tile_count)
    meta = jnp.transpose(meta, (0, 2, 1, 3, 4)).reshape(groups, n_prow, 2, tile_count)
    target = meta[:, :, 0, :].reshape(groups, group_tiles)
    block = meta[:, :, 1, :].reshape(groups, group_tiles)
    tile_ids = jnp.arange(group_tiles, dtype=jnp.int32)
    source_row = tile_ids // tile_count
    earlier = (
        (target[:, :, None] == target[:, None, :])
        & (source_row[:, None] == source_row[None, :])[None]
        & (tile_ids[:, None] > tile_ids[None, :])[None]
    )
    position = jnp.sum(earlier.astype(jnp.int32), axis=2)
    local_slot = source_row[None, :] * CAP + position

    my_target = jnp.take(target, my_group, axis=0)
    my_slot = my_target * slots + jnp.take(local_slot, my_group, axis=0)
    send_match = my_slot[None, :] == jnp.arange(groups * slots, dtype=jnp.int32)[:, None]
    send_index = jnp.where(
        jnp.any(send_match, axis=1),
        jnp.sum(jnp.where(send_match, tile_ids[None, :], 0), axis=1),
        group_tiles,
    )

    to_me = target == my_group
    slot_ids = jnp.arange(slots, dtype=jnp.int32)
    pick = to_me[:, None, :] & (local_slot[:, None, :] == slot_ids[None, :, None])
    recv_block = jnp.where(
        jnp.any(pick, axis=2), jnp.sum(jnp.where(pick, block[:, None, :], 0), axis=2), NT
    )
    recv_block = recv_block.reshape(n_lvl, n_pcol * slots)

    rhs_cols = lax.dynamic_slice_in_dim(rhs[0, 0], row_index * cols, cols, axis=1)
    window_blocks = width // block_rows
    acc = jnp.zeros((NT + 1, block_rows, cols), jnp.float32)
    solved = jnp.zeros((width, cols), jnp.float32)
    for section in range(n_lvl):
        if section == 0:
            solved_half = first_cols
        else:
            right = rhs_cols - acc[:window_blocks].reshape(width, cols)
            solved_now = jnp.dot(
                inv_full, right.astype(jnp.bfloat16), preferred_element_type=jnp.float32
            )
            solved = jnp.where(level_index == section, solved_now, solved)
            solved_half = solved_now.astype(jnp.bfloat16)
        updates = jnp.dot(
            tiles_full, solved_half, preferred_element_type=jnp.float32
        ).astype(jnp.bfloat16)
        updates = updates.reshape(group_tiles + 1, block_rows, cols)
        sending = jnp.take(updates, send_index, axis=0, mode="clip")
        incoming = lax.all_to_all(
            sending, ("lvl", "pcol"), split_axis=0, concat_axis=0, tiled=True
        )
        incoming = incoming.reshape(n_lvl, n_pcol * slots, block_rows, cols)[section]
        acc = acc.at[recv_block[section]].add(incoming.astype(jnp.float32), mode="clip")
    outer = acc[window_blocks:NT].reshape(ABOVE, cols)

    final = jnp.concatenate(
        [
            solved.reshape(n_prow, rows_out, cols),
            jnp.broadcast_to(outer[None], (n_prow, ABOVE, cols)),
        ],
        axis=1,
    )
    final = lax.all_to_all(final, "prow", split_axis=0, concat_axis=0, tiled=True)
    solution_rows = jnp.transpose(final[:, :rows_out], (1, 0, 2)).reshape(rows_out, columns_all)
    solution_rows = jnp.where(level_index == 0, first_rows, solution_rows)
    outer_all = jnp.transpose(final[:, rows_out:], (1, 0, 2)).reshape(ABOVE, columns_all)
    return (solution_rows[None, None], outer_all[None, None])


def solution(mesh):
    placed = (
        P("lvl", "pcol", None, None),
        P("lvl", "pcol", "prow", None),
        P("lvl", "pcol", "prow", None, None),
        P("lvl", "pcol", None),
        P("lvl", "pcol", "prow"),
        P("lvl", "pcol", "prow"),
        P("lvl", "pcol", "prow"),
    )
    return jax.shard_map(
        per_device,
        mesh=mesh,
        in_specs=placed,
        out_specs=(P("lvl", "pcol", "prow", None), P("lvl", "pcol", None, None)),
        check_vma=False,
    )
```

```python
import jax
import jax.numpy as jnp
from jax import lax
from jax.sharding import PartitionSpec as P

CAP = 2
ABOVE = 512
NT = 48


def per_device(
    rhs, diag_inverse, off_tiles, panel_super, off_device, off_block, offdiag_block_panel
):
    n_lvl = lax.axis_size("lvl")
    n_pcol = lax.axis_size("pcol")
    n_prow = lax.axis_size("prow")
    groups = n_lvl * n_pcol
    level_index = lax.axis_index("lvl")
    row_index = lax.axis_index("prow")
    col_index = lax.axis_index("pcol")
    my_group = level_index * n_pcol + col_index
    width = rhs.shape[2]
    columns_all = rhs.shape[3]
    cols = columns_all // n_prow
    row_count = diag_inverse.shape[2]
    tile_count = off_tiles.shape[2]
    block_rows = off_tiles.shape[3]
    group_tiles = n_prow * tile_count
    slots = n_prow * CAP

    panels = panel_super[0, 0]
    panel_count = panels.shape[0]
    panel_cols = width // panel_count
    panel_ids = jnp.arange(panel_count, dtype=jnp.int32)

    def super_of(panel):
        hit = panel[..., None] == panel_ids
        return jnp.sum(jnp.where(hit, panels, 0), axis=-1)

    col_super = super_of(jnp.arange(width, dtype=jnp.int32) // panel_cols)
    row_ids = row_index * row_count + jnp.arange(row_count, dtype=jnp.int32)
    row_super = super_of(row_ids // panel_cols)
    inverse = jnp.where(
        row_super[:, None] == col_super[None, :], diag_inverse[0, 0], jnp.zeros((), jnp.bfloat16)
    )
    tile_supernode = super_of(offdiag_block_panel[0, 0])
    tiles_used = jnp.where(
        col_super[None, None, :] == tile_supernode[:, None, None],
        off_tiles[0, 0],
        jnp.zeros((), jnp.bfloat16),
    ).reshape(tile_count * block_rows, width)

    both = jnp.concatenate([inverse, tiles_used], axis=0)
    gathered = lax.all_gather(both, "prow", axis=0)
    inv_full = gathered[:, :row_count].reshape(n_prow * row_count, width)
    tiles_full = gathered[:, row_count:].reshape(group_tiles * block_rows, width)
    tiles_full = jnp.concatenate(
        [tiles_full, jnp.zeros((block_rows, width), jnp.bfloat16)], axis=0
    )

    all_axes = ("lvl", "prow", "pcol")

    def level0_shift(x, shift):
        pairs = [
            (p * n_pcol + c, ((p + shift) % n_prow) * n_pcol + c)
            for p in range(n_prow)
            for c in range(n_pcol)
        ]
        return lax.ppermute(x, all_axes, pairs)

    def by_source(chunks):
        stacked = jnp.stack(chunks)
        order = (row_index - jnp.arange(n_prow, dtype=jnp.int32)) % n_prow
        return jnp.take(stacked, order, axis=0, mode="clip")

    rows_out = width // n_prow
    first_rows = jnp.dot(
        inverse, rhs[0, 0].astype(jnp.bfloat16), preferred_element_type=jnp.float32
    )
    first_half = first_rows.astype(jnp.bfloat16)
    first_all = by_source(
        [first_half] + [level0_shift(first_half, k) for k in range(1, n_prow)]
    ).reshape(width, columns_all)
    first_updates = jnp.dot(
        tiles_used, first_all, preferred_element_type=jnp.float32
    ).astype(jnp.bfloat16)

    def column_block(k):
        start = ((row_index + k) % n_prow) * cols
        return lax.dynamic_slice_in_dim(first_updates, start, cols, axis=1)

    first_cols = by_source(
        [column_block(0)] + [level0_shift(column_block(k), k) for k in range(1, n_prow)]
    ).reshape(group_tiles * block_rows, cols)
    first_cols = jnp.concatenate(
        [first_cols, jnp.zeros((block_rows, cols), jnp.bfloat16)], axis=0
    )

    meta = jnp.stack([off_device[0, 0], off_block[0, 0]], axis=0)
    devices = n_lvl * n_prow * n_pcol
    meta = lax.all_to_all(
        jnp.broadcast_to(meta[None], (devices,) + meta.shape),
        ("lvl", "prow", "pcol"),
        split_axis=0,
        concat_axis=0,
        tiled=True,
    )
    meta = meta.reshape(n_lvl, n_prow, n_pcol, 2, tile_count)
    meta = jnp.transpose(meta, (0, 2, 1, 3, 4)).reshape(groups, n_prow, 2, tile_count)
    target = meta[:, :, 0, :].reshape(groups, group_tiles)
    block = meta[:, :, 1, :].reshape(groups, group_tiles)
    tile_ids = jnp.arange(group_tiles, dtype=jnp.int32)
    source_row = tile_ids // tile_count
    earlier = (
        (target[:, :, None] == target[:, None, :])
        & (source_row[:, None] == source_row[None, :])[None]
        & (tile_ids[:, None] > tile_ids[None, :])[None]
    )
    position = jnp.sum(earlier.astype(jnp.int32), axis=2)
    local_slot = source_row[None, :] * CAP + position

    my_target = jnp.take(target, my_group, axis=0)
    my_slot = my_target * slots + jnp.take(local_slot, my_group, axis=0)
    send_match = my_slot[None, :] == jnp.arange(groups * slots, dtype=jnp.int32)[:, None]
    send_index = jnp.where(
        jnp.any(send_match, axis=1),
        jnp.sum(jnp.where(send_match, tile_ids[None, :], 0), axis=1),
        group_tiles,
    )

    to_me = target == my_group
    slot_ids = jnp.arange(slots, dtype=jnp.int32)
    pick = to_me[:, None, :] & (local_slot[:, None, :] == slot_ids[None, :, None])
    recv_block = jnp.where(
        jnp.any(pick, axis=2), jnp.sum(jnp.where(pick, block[:, None, :], 0), axis=2), NT
    )
    recv_block = recv_block.reshape(n_lvl, n_pcol * slots)

    rhs_cols = lax.dynamic_slice_in_dim(rhs[0, 0], row_index * cols, cols, axis=1)
    window_blocks = width // block_rows
    acc = jnp.zeros((NT + 1, block_rows, cols), jnp.float32)
    solved = jnp.zeros((width, cols), jnp.float32)
    for section in range(n_lvl):
        if section == 0:
            updates = first_cols
        else:
            right = rhs_cols - acc[:window_blocks].reshape(width, cols)
            solved_now = jnp.dot(
                inv_full, right.astype(jnp.bfloat16), preferred_element_type=jnp.float32
            )
            solved = jnp.where(level_index == section, solved_now, solved)
            updates = jnp.dot(
                tiles_full, solved_now.astype(jnp.bfloat16), preferred_element_type=jnp.float32
            ).astype(jnp.bfloat16)
        updates = updates.reshape(group_tiles + 1, block_rows, cols)
        sending = jnp.take(updates, send_index, axis=0, mode="clip")
        incoming = lax.all_to_all(
            sending, ("lvl", "pcol"), split_axis=0, concat_axis=0, tiled=True
        )
        incoming = incoming.reshape(n_lvl, n_pcol * slots, block_rows, cols)[section]
        acc = acc.at[recv_block[section]].add(incoming.astype(jnp.float32), mode="clip")
    outer = acc[window_blocks:NT].reshape(ABOVE, cols)

    final = jnp.concatenate(
        [
            solved.reshape(n_prow, rows_out, cols),
            jnp.broadcast_to(outer[None], (n_prow, ABOVE, cols)),
        ],
        axis=1,
    )
    final = lax.all_to_all(final, "prow", split_axis=0, concat_axis=0, tiled=True)
    solution_rows = jnp.transpose(final[:, :rows_out], (1, 0, 2)).reshape(rows_out, columns_all)
    solution_rows = jnp.where(level_index == 0, first_rows, solution_rows)
    outer_all = jnp.transpose(final[:, rows_out:], (1, 0, 2)).reshape(ABOVE, columns_all)
    return (solution_rows[None, None], outer_all[None, None])


def solution(mesh):
    placed = (
        P("lvl", "pcol", None, None),
        P("lvl", "pcol", "prow", None),
        P("lvl", "pcol", "prow", None, None),
        P("lvl", "pcol", None),
        P("lvl", "pcol", "prow"),
        P("lvl", "pcol", "prow"),
        P("lvl", "pcol", "prow"),
    )
    return jax.shard_map(
        per_device,
        mesh=mesh,
        in_specs=placed,
        out_specs=(P("lvl", "pcol", "prow", None), P("lvl", "pcol", None, None)),
        check_vma=False,
    )
```

```python
import jax
import jax.numpy as jnp
from jax import lax
from jax.sharding import PartitionSpec as P

CAP = 2
ABOVE = 512
NT = 48


def per_device(
    rhs, diag_inverse, off_tiles, panel_super, off_device, off_block, offdiag_block_panel
):
    n_lvl = lax.axis_size("lvl")
    n_pcol = lax.axis_size("pcol")
    n_prow = lax.axis_size("prow")
    groups = n_lvl * n_pcol
    level_index = lax.axis_index("lvl")
    row_index = lax.axis_index("prow")
    col_index = lax.axis_index("pcol")
    my_group = level_index * n_pcol + col_index
    width = rhs.shape[2]
    columns_all = rhs.shape[3]
    cols = columns_all // n_prow
    row_count = diag_inverse.shape[2]
    tile_count = off_tiles.shape[2]
    block_rows = off_tiles.shape[3]
    group_tiles = n_prow * tile_count
    slots = n_prow * CAP

    panels = panel_super[0, 0]
    panel_count = panels.shape[0]
    panel_cols = width // panel_count
    panel_ids = jnp.arange(panel_count, dtype=jnp.int32)

    def super_of(panel):
        hit = panel[..., None] == panel_ids
        return jnp.sum(jnp.where(hit, panels, 0), axis=-1)

    col_super = super_of(jnp.arange(width, dtype=jnp.int32) // panel_cols)
    row_ids = row_index * row_count + jnp.arange(row_count, dtype=jnp.int32)
    row_super = super_of(row_ids // panel_cols)
    inverse = jnp.where(
        row_super[:, None] == col_super[None, :], diag_inverse[0, 0], jnp.zeros((), jnp.bfloat16)
    )
    tile_supernode = super_of(offdiag_block_panel[0, 0])
    tiles_used = jnp.where(
        col_super[None, None, :] == tile_supernode[:, None, None],
        off_tiles[0, 0],
        jnp.zeros((), jnp.bfloat16),
    ).reshape(tile_count * block_rows, width)

    both = jnp.concatenate([inverse, tiles_used], axis=0)
    gathered = lax.all_gather(both, "prow", axis=0)
    inv_full = gathered[:, :row_count].reshape(n_prow * row_count, width)
    tiles_full = gathered[:, row_count:].reshape(group_tiles * block_rows, width)
    tiles_full = jnp.concatenate(
        [tiles_full, jnp.zeros((block_rows, width), jnp.bfloat16)], axis=0
    )

    all_axes = ("lvl", "prow", "pcol")

    def level0_shift(x, shift):
        pairs = [
            (p * n_pcol + c, ((p + shift) % n_prow) * n_pcol + c)
            for p in range(n_prow)
            for c in range(n_pcol)
        ]
        return lax.ppermute(x, all_axes, pairs)

    def by_source(chunks):
        stacked = jnp.stack(chunks)
        order = (row_index - jnp.arange(n_prow, dtype=jnp.int32)) % n_prow
        return jnp.take(stacked, order, axis=0, mode="clip")

    rows_out = width // n_prow
    first_rows = jnp.dot(
        inverse, rhs[0, 0].astype(jnp.bfloat16), preferred_element_type=jnp.float32
    )
    first_half = first_rows.astype(jnp.bfloat16)
    first_all = by_source(
        [first_half] + [level0_shift(first_half, k) for k in range(1, n_prow)]
    ).reshape(width, columns_all)
    first_updates = jnp.dot(
        tiles_used, first_all, preferred_element_type=jnp.float32
    ).astype(jnp.bfloat16)

    def column_block(k):
        start = ((row_index + k) % n_prow) * cols
        return lax.dynamic_slice_in_dim(first_updates, start, cols, axis=1)

    first_cols = by_source(
        [column_block(0)] + [level0_shift(column_block(k), k) for k in range(1, n_prow)]
    ).reshape(group_tiles * block_rows, cols)
    first_cols = jnp.concatenate(
        [first_cols, jnp.zeros((block_rows, cols), jnp.bfloat16)], axis=0
    )

    meta = jnp.stack([off_device[0, 0], off_block[0, 0]], axis=0)
    devices = n_lvl * n_prow * n_pcol
    meta = lax.all_to_all(
        jnp.broadcast_to(meta[None], (devices,) + meta.shape),
        ("lvl", "prow", "pcol"),
        split_axis=0,
        concat_axis=0,
        tiled=True,
    )
    meta = meta.reshape(n_lvl, n_prow, n_pcol, 2, tile_count)
    meta = jnp.transpose(meta, (0, 2, 1, 3, 4)).reshape(groups, n_prow, 2, tile_count)
    target = meta[:, :, 0, :].reshape(groups, group_tiles)
    block = meta[:, :, 1, :].reshape(groups, group_tiles)
    tile_ids = jnp.arange(group_tiles, dtype=jnp.int32)
    source_row = tile_ids // tile_count
    earlier = (
        (target[:, :, None] == target[:, None, :])
        & (source_row[:, None] == source_row[None, :])[None]
        & (tile_ids[:, None] > tile_ids[None, :])[None]
    )
    position = jnp.sum(earlier.astype(jnp.int32), axis=2)
    local_slot = source_row[None, :] * CAP + position

    my_target = jnp.take(target, my_group, axis=0)
    my_slot = my_target * slots + jnp.take(local_slot, my_group, axis=0)
    send_match = my_slot[None, :] == jnp.arange(groups * slots, dtype=jnp.int32)[:, None]
    send_index = jnp.where(
        jnp.any(send_match, axis=1),
        jnp.sum(jnp.where(send_match, tile_ids[None, :], 0), axis=1),
        group_tiles,
    )

    to_me = target == my_group
    slot_ids = jnp.arange(slots, dtype=jnp.int32)
    pick = to_me[:, None, :] & (local_slot[:, None, :] == slot_ids[None, :, None])
    recv_block = jnp.where(
        jnp.any(pick, axis=2), jnp.sum(jnp.where(pick, block[:, None, :], 0), axis=2), NT
    )
    recv_block = recv_block.reshape(n_lvl, n_pcol * slots)

    rhs_cols = lax.dynamic_slice_in_dim(rhs[0, 0], row_index * cols, cols, axis=1)
    window_blocks = width // block_rows
    acc = jnp.zeros((NT + 1, block_rows, cols), jnp.float32)
    solved = jnp.zeros((width, cols), jnp.float32)
    slot_rows = groups * slots * block_rows
    direct = slot_rows * width * 2 <= (8 << 20)
    if direct:
        tiles_slots = jnp.take(
            tiles_full.reshape(group_tiles + 1, block_rows, width), send_index, axis=0, mode="clip"
        ).reshape(slot_rows, width)
    for section in range(n_lvl):
        if section == 0:
            updates = first_cols
        if section > 0:
            right = rhs_cols - acc[:window_blocks].reshape(width, cols)
            solved_now = jnp.dot(
                inv_full, right.astype(jnp.bfloat16), preferred_element_type=jnp.float32
            )
            solved = jnp.where(level_index == section, solved_now, solved)
        if section > 0 and direct:
            sending = jnp.dot(
                tiles_slots, solved_now.astype(jnp.bfloat16), preferred_element_type=jnp.float32
            ).astype(jnp.bfloat16)
            sending = sending.reshape(groups * slots, block_rows, cols)
        else:
            if section > 0:
                updates = jnp.dot(
                    tiles_full,
                    solved_now.astype(jnp.bfloat16),
                    preferred_element_type=jnp.float32,
                ).astype(jnp.bfloat16)
            updates = updates.reshape(group_tiles + 1, block_rows, cols)
            sending = jnp.take(updates, send_index, axis=0, mode="clip")
        incoming = lax.all_to_all(
            sending, ("lvl", "pcol"), split_axis=0, concat_axis=0, tiled=True
        )
        incoming = incoming.reshape(n_lvl, n_pcol * slots, block_rows, cols)[section]
        acc = acc.at[recv_block[section]].add(incoming.astype(jnp.float32), mode="clip")
    outer = acc[window_blocks:NT].reshape(ABOVE, cols)

    final = jnp.concatenate(
        [
            solved.reshape(n_prow, rows_out, cols),
            jnp.broadcast_to(outer[None], (n_prow, ABOVE, cols)),
        ],
        axis=1,
    )
    final = lax.all_to_all(final, "prow", split_axis=0, concat_axis=0, tiled=True)
    solution_rows = jnp.transpose(final[:, :rows_out], (1, 0, 2)).reshape(rows_out, columns_all)
    solution_rows = jnp.where(level_index == 0, first_rows, solution_rows)
    outer_all = jnp.transpose(final[:, rows_out:], (1, 0, 2)).reshape(ABOVE, columns_all)
    return (solution_rows[None, None], outer_all[None, None])


def solution(mesh):
    placed = (
        P("lvl", "pcol", None, None),
        P("lvl", "pcol", "prow", None),
        P("lvl", "pcol", "prow", None, None),
        P("lvl", "pcol", None),
        P("lvl", "pcol", "prow"),
        P("lvl", "pcol", "prow"),
        P("lvl", "pcol", "prow"),
    )
    return jax.shard_map(
        per_device,
        mesh=mesh,
        in_specs=placed,
        out_specs=(P("lvl", "pcol", "prow", None), P("lvl", "pcol", None, None)),
        check_vma=False,
    )
```

```python
import jax
import jax.numpy as jnp
from jax import lax
from jax.sharding import PartitionSpec as P

CAP = 2
ABOVE = 512
NT = 48


def per_device(
    rhs, diag_inverse, off_tiles, panel_super, off_device, off_block, offdiag_block_panel
):
    n_lvl = lax.axis_size("lvl")
    n_pcol = lax.axis_size("pcol")
    n_prow = lax.axis_size("prow")
    groups = n_lvl * n_pcol
    level_index = lax.axis_index("lvl")
    row_index = lax.axis_index("prow")
    col_index = lax.axis_index("pcol")
    my_group = level_index * n_pcol + col_index
    width = rhs.shape[2]
    columns_all = rhs.shape[3]
    cols = columns_all // n_prow
    row_count = diag_inverse.shape[2]
    tile_count = off_tiles.shape[2]
    block_rows = off_tiles.shape[3]
    group_tiles = n_prow * tile_count
    slots = n_prow * CAP

    panels = panel_super[0, 0]
    panel_count = panels.shape[0]
    panel_cols = width // panel_count
    panel_ids = jnp.arange(panel_count, dtype=jnp.int32)

    def super_of(panel):
        hit = panel[..., None] == panel_ids
        return jnp.sum(jnp.where(hit, panels, 0), axis=-1)

    col_super = super_of(jnp.arange(width, dtype=jnp.int32) // panel_cols)
    row_ids = row_index * row_count + jnp.arange(row_count, dtype=jnp.int32)
    row_super = super_of(row_ids // panel_cols)
    inverse = jnp.where(
        row_super[:, None] == col_super[None, :], diag_inverse[0, 0], jnp.zeros((), jnp.bfloat16)
    )
    tile_supernode = super_of(offdiag_block_panel[0, 0])
    tiles_used = jnp.where(
        col_super[None, None, :] == tile_supernode[:, None, None],
        off_tiles[0, 0],
        jnp.zeros((), jnp.bfloat16),
    ).reshape(tile_count * block_rows, width)

    both = jnp.concatenate([inverse, tiles_used], axis=0)
    gathered = lax.all_gather(both, "prow", axis=0)
    inv_full = gathered[:, :row_count].reshape(n_prow * row_count, width)
    tiles_full = gathered[:, row_count:].reshape(group_tiles * block_rows, width)
    tiles_full = jnp.concatenate(
        [tiles_full, jnp.zeros((block_rows, width), jnp.bfloat16)], axis=0
    )

    all_axes = ("lvl", "prow", "pcol")

    def level0_shift(x, shift):
        pairs = [
            (p * n_pcol + c, ((p + shift) % n_prow) * n_pcol + c)
            for p in range(n_prow)
            for c in range(n_pcol)
        ]
        return lax.ppermute(x, all_axes, pairs)

    def prow_shift(x, shift):
        return lax.ppermute(x, "prow", [(p, (p + shift) % n_prow) for p in range(n_prow)])

    def by_source(chunks):
        stacked = jnp.stack(chunks)
        order = (row_index - jnp.arange(n_prow, dtype=jnp.int32)) % n_prow
        return jnp.take(stacked, order, axis=0, mode="clip")

    rows_out = width // n_prow
    first_rows = jnp.dot(
        inverse, rhs[0, 0].astype(jnp.bfloat16), preferred_element_type=jnp.float32
    )
    first_half = first_rows.astype(jnp.bfloat16)
    first_all = by_source(
        [first_half] + [level0_shift(first_half, k) for k in range(1, n_prow)]
    ).reshape(width, columns_all)
    first_updates = jnp.dot(
        tiles_used, first_all, preferred_element_type=jnp.float32
    ).astype(jnp.bfloat16)

    def column_block(k):
        start = ((row_index + k) % n_prow) * cols
        return lax.dynamic_slice_in_dim(first_updates, start, cols, axis=1)

    first_cols = by_source(
        [column_block(0)] + [level0_shift(column_block(k), k) for k in range(1, n_prow)]
    ).reshape(group_tiles * block_rows, cols)
    first_cols = jnp.concatenate(
        [first_cols, jnp.zeros((block_rows, cols), jnp.bfloat16)], axis=0
    )

    meta = jnp.stack([off_device[0, 0], off_block[0, 0]], axis=0)
    devices = n_lvl * n_prow * n_pcol
    meta = lax.all_to_all(
        jnp.broadcast_to(meta[None], (devices,) + meta.shape),
        ("lvl", "prow", "pcol"),
        split_axis=0,
        concat_axis=0,
        tiled=True,
    )
    meta = meta.reshape(n_lvl, n_prow, n_pcol, 2, tile_count)
    meta = jnp.transpose(meta, (0, 2, 1, 3, 4)).reshape(groups, n_prow, 2, tile_count)
    target = meta[:, :, 0, :].reshape(groups, group_tiles)
    block = meta[:, :, 1, :].reshape(groups, group_tiles)
    tile_ids = jnp.arange(group_tiles, dtype=jnp.int32)
    source_row = tile_ids // tile_count
    earlier = (
        (target[:, :, None] == target[:, None, :])
        & (source_row[:, None] == source_row[None, :])[None]
        & (tile_ids[:, None] > tile_ids[None, :])[None]
    )
    position = jnp.sum(earlier.astype(jnp.int32), axis=2)
    local_slot = source_row[None, :] * CAP + position

    my_target = jnp.take(target, my_group, axis=0)
    my_slot = my_target * slots + jnp.take(local_slot, my_group, axis=0)
    send_match = my_slot[None, :] == jnp.arange(groups * slots, dtype=jnp.int32)[:, None]
    send_index = jnp.where(
        jnp.any(send_match, axis=1),
        jnp.sum(jnp.where(send_match, tile_ids[None, :], 0), axis=1),
        group_tiles,
    )

    to_me = target == my_group
    slot_ids = jnp.arange(slots, dtype=jnp.int32)
    pick = to_me[:, None, :] & (local_slot[:, None, :] == slot_ids[None, :, None])
    recv_block = jnp.where(
        jnp.any(pick, axis=2), jnp.sum(jnp.where(pick, block[:, None, :], 0), axis=2), NT
    )
    recv_block = recv_block.reshape(n_lvl, n_pcol * slots)

    rhs_cols = lax.dynamic_slice_in_dim(rhs[0, 0], row_index * cols, cols, axis=1)
    window_blocks = width // block_rows
    acc = jnp.zeros((NT + 1, block_rows, cols), jnp.float32)
    solved = jnp.zeros((width, cols), jnp.float32)
    last = n_lvl - 1
    for section in range(n_lvl):
        if section == last:
            partial = acc[window_blocks:NT].reshape(ABOVE, cols)
            partial = by_source([partial] + [prow_shift(partial, k) for k in range(1, n_prow)])
        if section == 0:
            updates = first_cols
        else:
            right = rhs_cols - acc[:window_blocks].reshape(width, cols)
            solved_now = jnp.dot(
                inv_full, right.astype(jnp.bfloat16), preferred_element_type=jnp.float32
            )
            solved = jnp.where(level_index == section, solved_now, solved)
            updates = jnp.dot(
                tiles_full, solved_now.astype(jnp.bfloat16), preferred_element_type=jnp.float32
            ).astype(jnp.bfloat16)
        updates = updates.reshape(group_tiles + 1, block_rows, cols)
        sending = jnp.take(updates, send_index, axis=0, mode="clip")
        incoming = lax.all_to_all(
            sending, ("lvl", "pcol"), split_axis=0, concat_axis=0, tiled=True
        )
        incoming = incoming.reshape(n_lvl, n_pcol * slots, block_rows, cols)[section]
        if section < last:
            acc = acc.at[recv_block[section]].add(incoming.astype(jnp.float32), mode="clip")

    final = lax.all_to_all(
        solved.reshape(n_prow, rows_out, cols), "prow", split_axis=0, concat_axis=0, tiled=True
    )
    solution_rows = jnp.transpose(final, (1, 0, 2)).reshape(rows_out, columns_all)
    solution_rows = jnp.where(level_index == 0, first_rows, solution_rows)
    last_slots = by_source([incoming] + [prow_shift(incoming, k) for k in range(1, n_prow)])
    last_slots = jnp.transpose(last_slots, (1, 2, 0, 3)).reshape(
        n_pcol * slots, block_rows, columns_all
    )
    outer_last = jnp.zeros((NT + 1, block_rows, columns_all), jnp.float32)
    outer_last = outer_last.at[recv_block[last]].add(last_slots.astype(jnp.float32), mode="clip")
    outer_all = jnp.transpose(partial, (1, 0, 2)).reshape(ABOVE, columns_all)
    outer_all = outer_all + outer_last[window_blocks:NT].reshape(ABOVE, columns_all)
    return (solution_rows[None, None], outer_all[None, None])


def solution(mesh):
    placed = (
        P("lvl", "pcol", None, None),
        P("lvl", "pcol", "prow", None),
        P("lvl", "pcol", "prow", None, None),
        P("lvl", "pcol", None),
        P("lvl", "pcol", "prow"),
        P("lvl", "pcol", "prow"),
        P("lvl", "pcol", "prow"),
    )
    return jax.shard_map(
        per_device,
        mesh=mesh,
        in_specs=placed,
        out_specs=(P("lvl", "pcol", "prow", None), P("lvl", "pcol", None, None)),
        check_vma=False,
    )
```

```python
import jax
import jax.numpy as jnp
from jax import lax
from jax.sharding import PartitionSpec as P

CAP = 2
ABOVE = 512
NT = 48


def per_device(
    rhs, diag_inverse, off_tiles, panel_super, off_device, off_block, offdiag_block_panel
):
    n_lvl = lax.axis_size("lvl")
    n_pcol = lax.axis_size("pcol")
    n_prow = lax.axis_size("prow")
    groups = n_lvl * n_pcol
    level_index = lax.axis_index("lvl")
    row_index = lax.axis_index("prow")
    col_index = lax.axis_index("pcol")
    my_group = level_index * n_pcol + col_index
    width = rhs.shape[2]
    columns_all = rhs.shape[3]
    cols = columns_all // n_prow
    row_count = diag_inverse.shape[2]
    tile_count = off_tiles.shape[2]
    block_rows = off_tiles.shape[3]
    group_tiles = n_prow * tile_count
    slots = n_prow * CAP

    panels = panel_super[0, 0]
    panel_count = panels.shape[0]
    panel_cols = width // panel_count
    panel_ids = jnp.arange(panel_count, dtype=jnp.int32)

    def super_of(panel):
        hit = panel[..., None] == panel_ids
        return jnp.sum(jnp.where(hit, panels, 0), axis=-1)

    col_super = super_of(jnp.arange(width, dtype=jnp.int32) // panel_cols)
    row_ids = row_index * row_count + jnp.arange(row_count, dtype=jnp.int32)
    row_super = super_of(row_ids // panel_cols)
    inverse = jnp.where(
        row_super[:, None] == col_super[None, :], diag_inverse[0, 0], jnp.zeros((), jnp.bfloat16)
    )
    tile_supernode = super_of(offdiag_block_panel[0, 0])
    tiles_used = jnp.where(
        col_super[None, None, :] == tile_supernode[:, None, None],
        off_tiles[0, 0],
        jnp.zeros((), jnp.bfloat16),
    ).reshape(tile_count * block_rows, width)

    both = jnp.concatenate([inverse, tiles_used], axis=0)
    if both.size * 2 <= (2 << 20):
        to_right = [(p, p + 1) for p in range(n_prow - 1)]
        to_left = [(p + 1, p) for p in range(n_prow - 1)]
        chunks = [both]
        from_left = from_right = both
        for _ in range(n_prow - 1):
            from_left = lax.ppermute(from_left, "prow", to_right)
            from_right = lax.ppermute(from_right, "prow", to_left)
            chunks += [from_left, from_right]
        offsets = jnp.arange(n_prow, dtype=jnp.int32) - row_index
        chunk_of = jnp.where(offsets < 0, -2 * offsets - 1, 2 * offsets)
        gathered = jnp.take(jnp.stack(chunks), chunk_of, axis=0, mode="clip")
    else:
        gathered = lax.all_gather(both, "prow", axis=0)
    inv_full = gathered[:, :row_count].reshape(n_prow * row_count, width)
    tiles_full = gathered[:, row_count:].reshape(group_tiles * block_rows, width)
    tiles_full = jnp.concatenate(
        [tiles_full, jnp.zeros((block_rows, width), jnp.bfloat16)], axis=0
    )

    all_axes = ("lvl", "prow", "pcol")

    def level0_shift(x, shift):
        pairs = [
            (p * n_pcol + c, ((p + shift) % n_prow) * n_pcol + c)
            for p in range(n_prow)
            for c in range(n_pcol)
        ]
        return lax.ppermute(x, all_axes, pairs)

    def by_source(chunks):
        stacked = jnp.stack(chunks)
        order = (row_index - jnp.arange(n_prow, dtype=jnp.int32)) % n_prow
        return jnp.take(stacked, order, axis=0, mode="clip")

    rows_out = width // n_prow
    first_rows = jnp.dot(
        inverse, rhs[0, 0].astype(jnp.bfloat16), preferred_element_type=jnp.float32
    )
    first_half = first_rows.astype(jnp.bfloat16)
    first_all = by_source(
        [first_half] + [level0_shift(first_half, k) for k in range(1, n_prow)]
    ).reshape(width, columns_all)
    first_updates = jnp.dot(
        tiles_used, first_all, preferred_element_type=jnp.float32
    ).astype(jnp.bfloat16)

    def column_block(k):
        start = ((row_index + k) % n_prow) * cols
        return lax.dynamic_slice_in_dim(first_updates, start, cols, axis=1)

    first_cols = by_source(
        [column_block(0)] + [level0_shift(column_block(k), k) for k in range(1, n_prow)]
    ).reshape(group_tiles * block_rows, cols)
    first_cols = jnp.concatenate(
        [first_cols, jnp.zeros((block_rows, cols), jnp.bfloat16)], axis=0
    )

    meta = jnp.stack([off_device[0, 0], off_block[0, 0]], axis=0)
    devices = n_lvl * n_prow * n_pcol
    meta = lax.all_to_all(
        jnp.broadcast_to(meta[None], (devices,) + meta.shape),
        ("lvl", "prow", "pcol"),
        split_axis=0,
        concat_axis=0,
        tiled=True,
    )
    meta = meta.reshape(n_lvl, n_prow, n_pcol, 2, tile_count)
    meta = jnp.transpose(meta, (0, 2, 1, 3, 4)).reshape(groups, n_prow, 2, tile_count)
    target = meta[:, :, 0, :].reshape(groups, group_tiles)
    block = meta[:, :, 1, :].reshape(groups, group_tiles)
    tile_ids = jnp.arange(group_tiles, dtype=jnp.int32)
    source_row = tile_ids // tile_count
    earlier = (
        (target[:, :, None] == target[:, None, :])
        & (source_row[:, None] == source_row[None, :])[None]
        & (tile_ids[:, None] > tile_ids[None, :])[None]
    )
    position = jnp.sum(earlier.astype(jnp.int32), axis=2)
    local_slot = source_row[None, :] * CAP + position

    my_target = jnp.take(target, my_group, axis=0)
    my_slot = my_target * slots + jnp.take(local_slot, my_group, axis=0)
    send_match = my_slot[None, :] == jnp.arange(groups * slots, dtype=jnp.int32)[:, None]
    send_index = jnp.where(
        jnp.any(send_match, axis=1),
        jnp.sum(jnp.where(send_match, tile_ids[None, :], 0), axis=1),
        group_tiles,
    )

    to_me = target == my_group
    slot_ids = jnp.arange(slots, dtype=jnp.int32)
    pick = to_me[:, None, :] & (local_slot[:, None, :] == slot_ids[None, :, None])
    recv_block = jnp.where(
        jnp.any(pick, axis=2), jnp.sum(jnp.where(pick, block[:, None, :], 0), axis=2), NT
    )
    recv_block = recv_block.reshape(n_lvl, n_pcol * slots)

    rhs_cols = lax.dynamic_slice_in_dim(rhs[0, 0], row_index * cols, cols, axis=1)
    window_blocks = width // block_rows
    acc = jnp.zeros((NT + 1, block_rows, cols), jnp.float32)
    solved = jnp.zeros((width, cols), jnp.float32)
    for section in range(n_lvl):
        if section == 0:
            updates = first_cols
        else:
            right = rhs_cols - acc[:window_blocks].reshape(width, cols)
            solved_now = jnp.dot(
                inv_full, right.astype(jnp.bfloat16), preferred_element_type=jnp.float32
            )
            solved = jnp.where(level_index == section, solved_now, solved)
            updates = jnp.dot(
                tiles_full, solved_now.astype(jnp.bfloat16), preferred_element_type=jnp.float32
            ).astype(jnp.bfloat16)
        updates = updates.reshape(group_tiles + 1, block_rows, cols)
        sending = jnp.take(updates, send_index, axis=0, mode="clip")
        incoming = lax.all_to_all(
            sending, ("lvl", "pcol"), split_axis=0, concat_axis=0, tiled=True
        )
        incoming = incoming.reshape(n_lvl, n_pcol * slots, block_rows, cols)[section]
        acc = acc.at[recv_block[section]].add(incoming.astype(jnp.float32), mode="clip")
    outer = acc[window_blocks:NT].reshape(ABOVE, cols)

    final = jnp.concatenate(
        [
            solved.reshape(n_prow, rows_out, cols),
            jnp.broadcast_to(outer[None], (n_prow, ABOVE, cols)),
        ],
        axis=1,
    )
    final = lax.all_to_all(final, "prow", split_axis=0, concat_axis=0, tiled=True)
    solution_rows = jnp.transpose(final[:, :rows_out], (1, 0, 2)).reshape(rows_out, columns_all)
    solution_rows = jnp.where(level_index == 0, first_rows, solution_rows)
    outer_all = jnp.transpose(final[:, rows_out:], (1, 0, 2)).reshape(ABOVE, columns_all)
    return (solution_rows[None, None], outer_all[None, None])


def solution(mesh):
    placed = (
        P("lvl", "pcol", None, None),
        P("lvl", "pcol", "prow", None),
        P("lvl", "pcol", "prow", None, None),
        P("lvl", "pcol", None),
        P("lvl", "pcol", "prow"),
        P("lvl", "pcol", "prow"),
        P("lvl", "pcol", "prow"),
    )
    return jax.shard_map(
        per_device,
        mesh=mesh,
        in_specs=placed,
        out_specs=(P("lvl", "pcol", "prow", None), P("lvl", "pcol", None, None)),
        check_vma=False,
    )
```

```python
import jax
import jax.numpy as jnp
from jax import lax
from jax.sharding import PartitionSpec as P

CAP = 2
ABOVE = 512
NT = 48


def per_device(
    rhs, diag_inverse, off_tiles, panel_super, off_device, off_block, offdiag_block_panel
):
    n_lvl = lax.axis_size("lvl")
    n_pcol = lax.axis_size("pcol")
    n_prow = lax.axis_size("prow")
    groups = n_lvl * n_pcol
    level_index = lax.axis_index("lvl")
    row_index = lax.axis_index("prow")
    col_index = lax.axis_index("pcol")
    my_group = level_index * n_pcol + col_index
    width = rhs.shape[2]
    columns_all = rhs.shape[3]
    cols = columns_all // n_prow
    row_count = diag_inverse.shape[2]
    tile_count = off_tiles.shape[2]
    block_rows = off_tiles.shape[3]
    group_tiles = n_prow * tile_count
    slots = n_prow * CAP

    panels = panel_super[0, 0]
    panel_count = panels.shape[0]
    panel_cols = width // panel_count
    panel_ids = jnp.arange(panel_count, dtype=jnp.int32)

    def super_of(panel):
        hit = panel[..., None] == panel_ids
        return jnp.sum(jnp.where(hit, panels, 0), axis=-1)

    col_super = super_of(jnp.arange(width, dtype=jnp.int32) // panel_cols)
    row_ids = row_index * row_count + jnp.arange(row_count, dtype=jnp.int32)
    row_super = super_of(row_ids // panel_cols)
    inverse = jnp.where(
        row_super[:, None] == col_super[None, :], diag_inverse[0, 0], jnp.zeros((), jnp.bfloat16)
    )
    tile_supernode = super_of(offdiag_block_panel[0, 0])
    tiles_used = jnp.where(
        col_super[None, None, :] == tile_supernode[:, None, None],
        off_tiles[0, 0],
        jnp.zeros((), jnp.bfloat16),
    ).reshape(tile_count * block_rows, width)

    both = jnp.concatenate([inverse, tiles_used], axis=0)
    if both.size * 2 <= (2 << 20):
        to_right = [(p, p + 1) for p in range(n_prow - 1)]
        to_left = [(p + 1, p) for p in range(n_prow - 1)]
        chunks = [both]
        from_left = from_right = both
        for _ in range(n_prow - 1):
            from_left = lax.ppermute(from_left, "prow", to_right)
            from_right = lax.ppermute(from_right, "prow", to_left)
            chunks += [from_left, from_right]
        offsets = jnp.arange(n_prow, dtype=jnp.int32) - row_index
        chunk_of = jnp.where(offsets < 0, -2 * offsets - 1, 2 * offsets)
        gathered = jnp.take(jnp.stack(chunks), chunk_of, axis=0, mode="clip")
    else:
        gathered = lax.all_gather(both, "prow", axis=0)
    inv_full = gathered[:, :row_count].reshape(n_prow * row_count, width)
    tiles_full = gathered[:, row_count:].reshape(group_tiles * block_rows, width)
    tiles_full = jnp.concatenate(
        [tiles_full, jnp.zeros((block_rows, width), jnp.bfloat16)], axis=0
    )

    meta = jnp.stack([off_device[0, 0], off_block[0, 0]], axis=0)
    devices = n_lvl * n_prow * n_pcol
    meta = lax.all_to_all(
        jnp.broadcast_to(meta[None], (devices,) + meta.shape),
        ("lvl", "prow", "pcol"),
        split_axis=0,
        concat_axis=0,
        tiled=True,
    )
    meta = meta.reshape(n_lvl, n_prow, n_pcol, 2, tile_count)
    meta = jnp.transpose(meta, (0, 2, 1, 3, 4)).reshape(groups, n_prow, 2, tile_count)
    target = meta[:, :, 0, :].reshape(groups, group_tiles)
    block = meta[:, :, 1, :].reshape(groups, group_tiles)
    tile_ids = jnp.arange(group_tiles, dtype=jnp.int32)
    source_row = tile_ids // tile_count
    earlier = (
        (target[:, :, None] == target[:, None, :])
        & (source_row[:, None] == source_row[None, :])[None]
        & (tile_ids[:, None] > tile_ids[None, :])[None]
    )
    position = jnp.sum(earlier.astype(jnp.int32), axis=2)
    local_slot = source_row[None, :] * CAP + position

    my_target = jnp.take(target, my_group, axis=0)
    my_slot = my_target * slots + jnp.take(local_slot, my_group, axis=0)
    send_match = my_slot[None, :] == jnp.arange(groups * slots, dtype=jnp.int32)[:, None]
    send_index = jnp.where(
        jnp.any(send_match, axis=1),
        jnp.sum(jnp.where(send_match, tile_ids[None, :], 0), axis=1),
        group_tiles,
    )

    to_me = target == my_group
    slot_ids = jnp.arange(slots, dtype=jnp.int32)
    pick = to_me[:, None, :] & (local_slot[:, None, :] == slot_ids[None, :, None])
    recv_block = jnp.where(
        jnp.any(pick, axis=2), jnp.sum(jnp.where(pick, block[:, None, :], 0), axis=2), NT
    )
    recv_block = recv_block.reshape(n_lvl, n_pcol * slots)

    rhs_cols = lax.dynamic_slice_in_dim(rhs[0, 0], row_index * cols, cols, axis=1)
    window_blocks = width // block_rows
    acc = jnp.zeros((NT + 1, block_rows, cols), jnp.float32)
    solved = jnp.zeros((width, cols), jnp.float32)
    for section in range(n_lvl):
        right = rhs_cols - acc[:window_blocks].reshape(width, cols)
        solved_now = jnp.dot(
            inv_full, right.astype(jnp.bfloat16), preferred_element_type=jnp.float32
        )
        solved = jnp.where(level_index == section, solved_now, solved)
        updates = jnp.dot(
            tiles_full, solved_now.astype(jnp.bfloat16), preferred_element_type=jnp.float32
        ).astype(jnp.bfloat16)
        updates = updates.reshape(group_tiles + 1, block_rows, cols)
        sending = jnp.take(updates, send_index, axis=0, mode="clip")
        incoming = lax.all_to_all(
            sending, ("lvl", "pcol"), split_axis=0, concat_axis=0, tiled=True
        )
        incoming = incoming.reshape(n_lvl, n_pcol * slots, block_rows, cols)[section]
        acc = acc.at[recv_block[section]].add(incoming.astype(jnp.float32), mode="clip")
    outer = acc[window_blocks:NT].reshape(ABOVE, cols)

    rows_out = width // n_prow
    final = jnp.concatenate(
        [
            solved.reshape(n_prow, rows_out, cols),
            jnp.broadcast_to(outer[None], (n_prow, ABOVE, cols)),
        ],
        axis=1,
    )
    final = lax.all_to_all(final, "prow", split_axis=0, concat_axis=0, tiled=True)
    solution_rows = jnp.transpose(final[:, :rows_out], (1, 0, 2)).reshape(rows_out, columns_all)
    outer_all = jnp.transpose(final[:, rows_out:], (1, 0, 2)).reshape(ABOVE, columns_all)
    return (solution_rows[None, None], outer_all[None, None])


def solution(mesh):
    placed = (
        P("lvl", "pcol", None, None),
        P("lvl", "pcol", "prow", None),
        P("lvl", "pcol", "prow", None, None),
        P("lvl", "pcol", None),
        P("lvl", "pcol", "prow"),
        P("lvl", "pcol", "prow"),
        P("lvl", "pcol", "prow"),
    )
    return jax.shard_map(
        per_device,
        mesh=mesh,
        in_specs=placed,
        out_specs=(P("lvl", "pcol", "prow", None), P("lvl", "pcol", None, None)),
        check_vma=False,
    )
```

```python
import jax
import jax.numpy as jnp
from jax import lax
from jax.sharding import PartitionSpec as P

CAP = 2
ABOVE = 512
NT = 48


def per_device(
    rhs, diag_inverse, off_tiles, panel_super, off_device, off_block, offdiag_block_panel
):
    n_lvl = lax.axis_size("lvl")
    n_pcol = lax.axis_size("pcol")
    n_prow = lax.axis_size("prow")
    groups = n_lvl * n_pcol
    level_index = lax.axis_index("lvl")
    row_index = lax.axis_index("prow")
    col_index = lax.axis_index("pcol")
    my_group = level_index * n_pcol + col_index
    width = rhs.shape[2]
    columns_all = rhs.shape[3]
    cols = columns_all // n_prow
    row_count = diag_inverse.shape[2]
    tile_count = off_tiles.shape[2]
    block_rows = off_tiles.shape[3]
    group_tiles = n_prow * tile_count
    slots = n_prow * CAP

    panels = panel_super[0, 0]
    panel_count = panels.shape[0]
    panel_cols = width // panel_count
    panel_ids = jnp.arange(panel_count, dtype=jnp.int32)

    def super_of(panel):
        hit = panel[..., None] == panel_ids
        return jnp.sum(jnp.where(hit, panels, 0), axis=-1)

    col_super = super_of(jnp.arange(width, dtype=jnp.int32) // panel_cols)
    row_ids = row_index * row_count + jnp.arange(row_count, dtype=jnp.int32)
    row_super = super_of(row_ids // panel_cols)
    inverse = jnp.where(
        row_super[:, None] == col_super[None, :], diag_inverse[0, 0], jnp.zeros((), jnp.bfloat16)
    )
    tile_supernode = super_of(offdiag_block_panel[0, 0])
    tiles_used = jnp.where(
        col_super[None, None, :] == tile_supernode[:, None, None],
        off_tiles[0, 0],
        jnp.zeros((), jnp.bfloat16),
    ).reshape(tile_count * block_rows, width)

    both = jnp.concatenate([inverse, tiles_used], axis=0)
    gathered = lax.all_gather(both, "prow", axis=0)
    inv_full = gathered[:, :row_count].reshape(n_prow * row_count, width)
    tiles_full = gathered[:, row_count:].reshape(group_tiles * block_rows, width)
    tiles_full = jnp.concatenate(
        [tiles_full, jnp.zeros((block_rows, width), jnp.bfloat16)], axis=0
    )

    all_axes = ("lvl", "prow", "pcol")

    def level0_shift(x, shift):
        pairs = [
            (p * n_pcol + c, ((p + shift) % n_prow) * n_pcol + c)
            for p in range(n_prow)
            for c in range(n_pcol)
        ]
        return lax.ppermute(x, all_axes, pairs)

    def by_source(chunks):
        stacked = jnp.stack(chunks)
        order = (row_index - jnp.arange(n_prow, dtype=jnp.int32)) % n_prow
        return jnp.take(stacked, order, axis=0, mode="clip")

    rows_out = width // n_prow
    first_rows = jnp.dot(
        inverse, rhs[0, 0].astype(jnp.bfloat16), preferred_element_type=jnp.float32
    )
    first_half = first_rows.astype(jnp.bfloat16)
    first_all = by_source(
        [first_half] + [level0_shift(first_half, k) for k in range(1, n_prow)]
    ).reshape(width, columns_all)
    first_updates = jnp.dot(
        tiles_used, first_all, preferred_element_type=jnp.float32
    ).astype(jnp.bfloat16)

    def column_block(k):
        start = ((row_index + k) % n_prow) * cols
        return lax.dynamic_slice_in_dim(first_updates, start, cols, axis=1)

    first_cols = by_source(
        [column_block(0)] + [level0_shift(column_block(k), k) for k in range(1, n_prow)]
    ).reshape(group_tiles * block_rows, cols)
    first_cols = jnp.concatenate(
        [first_cols, jnp.zeros((block_rows, cols), jnp.bfloat16)], axis=0
    )

    meta = jnp.stack([off_device[0, 0], off_block[0, 0]], axis=0)
    devices = n_lvl * n_prow * n_pcol
    meta = lax.all_to_all(
        jnp.broadcast_to(meta[None], (devices,) + meta.shape),
        ("lvl", "prow", "pcol"),
        split_axis=0,
        concat_axis=0,
        tiled=True,
    )
    meta = meta.reshape(n_lvl, n_prow, n_pcol, 2, tile_count)
    meta = jnp.transpose(meta, (0, 2, 1, 3, 4)).reshape(groups, n_prow, 2, tile_count)
    target = meta[:, :, 0, :].reshape(groups, group_tiles)
    block = meta[:, :, 1, :].reshape(groups, group_tiles)
    tile_ids = jnp.arange(group_tiles, dtype=jnp.int32)
    source_row = tile_ids // tile_count
    earlier = (
        (target[:, :, None] == target[:, None, :])
        & (source_row[:, None] == source_row[None, :])[None]
        & (tile_ids[:, None] > tile_ids[None, :])[None]
    )
    position = jnp.sum(earlier.astype(jnp.int32), axis=2)
    local_slot = source_row[None, :] * CAP + position

    my_target = jnp.take(target, my_group, axis=0)
    my_slot = my_target * slots + jnp.take(local_slot, my_group, axis=0)
    send_match = my_slot[None, :] == jnp.arange(groups * slots, dtype=jnp.int32)[:, None]
    send_index = jnp.where(
        jnp.any(send_match, axis=1),
        jnp.sum(jnp.where(send_match, tile_ids[None, :], 0), axis=1),
        group_tiles,
    )

    to_me = target == my_group
    slot_ids = jnp.arange(slots, dtype=jnp.int32)
    pick = to_me[:, None, :] & (local_slot[:, None, :] == slot_ids[None, :, None])
    recv_block = jnp.where(
        jnp.any(pick, axis=2), jnp.sum(jnp.where(pick, block[:, None, :], 0), axis=2), NT
    )
    recv_block = recv_block.reshape(n_lvl, n_pcol * slots)

    rhs_cols = lax.dynamic_slice_in_dim(rhs[0, 0], row_index * cols, cols, axis=1)
    window_blocks = width // block_rows
    acc = jnp.zeros((NT + 1, block_rows, cols), jnp.float32)
    solved = jnp.zeros((width, cols), jnp.float32)
    for section in range(n_lvl):
        if section == 0:
            updates = first_cols
        else:
            right = rhs_cols - acc[:window_blocks].reshape(width, cols)
            solved_now = jnp.dot(
                inv_full, right.astype(jnp.bfloat16), preferred_element_type=jnp.float32
            )
            solved = jnp.where(level_index == section, solved_now, solved)
            updates = jnp.dot(
                tiles_full, solved_now.astype(jnp.bfloat16), preferred_element_type=jnp.float32
            ).astype(jnp.bfloat16)
        updates = updates.reshape(group_tiles + 1, block_rows, cols)
        sending = jnp.take(updates, send_index, axis=0, mode="clip")
        incoming = lax.all_to_all(
            sending, ("lvl", "pcol"), split_axis=0, concat_axis=0, tiled=True
        )
        incoming = incoming.reshape(n_lvl, n_pcol * slots, block_rows, cols)[section]
        acc = acc.at[recv_block[section]].add(incoming.astype(jnp.float32), mode="clip")
    outer = acc[window_blocks:NT].reshape(ABOVE, cols)

    solved_blocks = solved.reshape(n_prow, rows_out, cols)
    solved_high = lax.reduce_precision(solved_blocks, exponent_bits=8, mantissa_bits=7)
    solved_low = solved_blocks - solved_high
    final = jnp.concatenate(
        [
            solved_high.astype(jnp.bfloat16),
            solved_low.astype(jnp.bfloat16),
            jnp.broadcast_to(outer.astype(jnp.bfloat16)[None], (n_prow, ABOVE, cols)),
        ],
        axis=1,
    )
    final = lax.all_to_all(final, "prow", split_axis=0, concat_axis=0, tiled=True)
    final = final.astype(jnp.float32)
    solution_cols = final[:, :rows_out] + final[:, rows_out : 2 * rows_out]
    solution_rows = jnp.transpose(solution_cols, (1, 0, 2)).reshape(rows_out, columns_all)
    solution_rows = jnp.where(level_index == 0, first_rows, solution_rows)
    outer_all = jnp.transpose(final[:, 2 * rows_out :], (1, 0, 2)).reshape(ABOVE, columns_all)
    return (solution_rows[None, None], outer_all[None, None])


def solution(mesh):
    placed = (
        P("lvl", "pcol", None, None),
        P("lvl", "pcol", "prow", None),
        P("lvl", "pcol", "prow", None, None),
        P("lvl", "pcol", None),
        P("lvl", "pcol", "prow"),
        P("lvl", "pcol", "prow"),
        P("lvl", "pcol", "prow"),
    )
    return jax.shard_map(
        per_device,
        mesh=mesh,
        in_specs=placed,
        out_specs=(P("lvl", "pcol", "prow", None), P("lvl", "pcol", None, None)),
        check_vma=False,
    )
```

```python
import jax
import jax.numpy as jnp
from jax import lax
from jax.sharding import PartitionSpec as P

CAP = 2
ABOVE = 512
NT = 48


def per_device(
    rhs, diag_inverse, off_tiles, panel_super, off_device, off_block, offdiag_block_panel
):
    n_lvl = lax.axis_size("lvl")
    n_pcol = lax.axis_size("pcol")
    n_prow = lax.axis_size("prow")
    groups = n_lvl * n_pcol
    level_index = lax.axis_index("lvl")
    row_index = lax.axis_index("prow")
    col_index = lax.axis_index("pcol")
    my_group = level_index * n_pcol + col_index
    width = rhs.shape[2]
    columns_all = rhs.shape[3]
    cols = columns_all // n_prow
    row_count = diag_inverse.shape[2]
    tile_count = off_tiles.shape[2]
    block_rows = off_tiles.shape[3]
    group_tiles = n_prow * tile_count
    slots = n_prow * CAP

    panels = panel_super[0, 0]
    panel_count = panels.shape[0]
    panel_cols = width // panel_count
    panel_ids = jnp.arange(panel_count, dtype=jnp.int32)

    def super_of(panel):
        hit = panel[..., None] == panel_ids
        return jnp.sum(jnp.where(hit, panels, 0), axis=-1)

    col_super = super_of(jnp.arange(width, dtype=jnp.int32) // panel_cols)
    row_ids = row_index * row_count + jnp.arange(row_count, dtype=jnp.int32)
    row_super = super_of(row_ids // panel_cols)
    inverse = jnp.where(
        row_super[:, None] == col_super[None, :], diag_inverse[0, 0], jnp.zeros((), jnp.bfloat16)
    )
    tile_supernode = super_of(offdiag_block_panel[0, 0])
    tiles_used = jnp.where(
        col_super[None, None, :] == tile_supernode[:, None, None],
        off_tiles[0, 0],
        jnp.zeros((), jnp.bfloat16),
    ).reshape(tile_count * block_rows, width)

    if inverse.shape == tiles_used.shape:
        gathered = lax.all_gather(jnp.stack([inverse, tiles_used]), "prow", axis=1)
        inv_full = gathered[0].reshape(n_prow * row_count, width)
        tiles_full = gathered[1].reshape(group_tiles * block_rows, width)
    else:
        both = jnp.concatenate([inverse, tiles_used], axis=0)
        gathered = lax.all_gather(both, "prow", axis=0)
        inv_full = gathered[:, :row_count].reshape(n_prow * row_count, width)
        tiles_full = gathered[:, row_count:].reshape(group_tiles * block_rows, width)
    tiles_full = jnp.concatenate(
        [tiles_full, jnp.zeros((block_rows, width), jnp.bfloat16)], axis=0
    )

    all_axes = ("lvl", "prow", "pcol")

    def level0_shift(x, shift):
        pairs = [
            (p * n_pcol + c, ((p + shift) % n_prow) * n_pcol + c)
            for p in range(n_prow)
            for c in range(n_pcol)
        ]
        return lax.ppermute(x, all_axes, pairs)

    def by_source(chunks):
        stacked = jnp.stack(chunks)
        order = (row_index - jnp.arange(n_prow, dtype=jnp.int32)) % n_prow
        return jnp.take(stacked, order, axis=0, mode="clip")

    rows_out = width // n_prow
    first_rows = jnp.dot(
        inverse, rhs[0, 0].astype(jnp.bfloat16), preferred_element_type=jnp.float32
    )
    first_half = first_rows.astype(jnp.bfloat16)
    first_all = by_source(
        [first_half] + [level0_shift(first_half, k) for k in range(1, n_prow)]
    ).reshape(width, columns_all)
    first_updates = jnp.dot(
        tiles_used, first_all, preferred_element_type=jnp.float32
    ).astype(jnp.bfloat16)

    def column_block(k):
        start = ((row_index + k) % n_prow) * cols
        return lax.dynamic_slice_in_dim(first_updates, start, cols, axis=1)

    first_cols = by_source(
        [column_block(0)] + [level0_shift(column_block(k), k) for k in range(1, n_prow)]
    ).reshape(group_tiles * block_rows, cols)
    first_cols = jnp.concatenate(
        [first_cols, jnp.zeros((block_rows, cols), jnp.bfloat16)], axis=0
    )

    meta = jnp.stack([off_device[0, 0], off_block[0, 0]], axis=0)
    devices = n_lvl * n_prow * n_pcol
    meta = lax.all_to_all(
        jnp.broadcast_to(meta[None], (devices,) + meta.shape),
        ("lvl", "prow", "pcol"),
        split_axis=0,
        concat_axis=0,
        tiled=True,
    )
    meta = meta.reshape(n_lvl, n_prow, n_pcol, 2, tile_count)
    meta = jnp.transpose(meta, (0, 2, 1, 3, 4)).reshape(groups, n_prow, 2, tile_count)
    target = meta[:, :, 0, :].reshape(groups, group_tiles)
    block = meta[:, :, 1, :].reshape(groups, group_tiles)
    tile_ids = jnp.arange(group_tiles, dtype=jnp.int32)
    source_row = tile_ids // tile_count
    earlier = (
        (target[:, :, None] == target[:, None, :])
        & (source_row[:, None] == source_row[None, :])[None]
        & (tile_ids[:, None] > tile_ids[None, :])[None]
    )
    position = jnp.sum(earlier.astype(jnp.int32), axis=2)
    local_slot = source_row[None, :] * CAP + position

    my_target = jnp.take(target, my_group, axis=0)
    my_slot = my_target * slots + jnp.take(local_slot, my_group, axis=0)
    send_match = my_slot[None, :] == jnp.arange(groups * slots, dtype=jnp.int32)[:, None]
    send_index = jnp.where(
        jnp.any(send_match, axis=1),
        jnp.sum(jnp.where(send_match, tile_ids[None, :], 0), axis=1),
        group_tiles,
    )

    to_me = target == my_group
    slot_ids = jnp.arange(slots, dtype=jnp.int32)
    pick = to_me[:, None, :] & (local_slot[:, None, :] == slot_ids[None, :, None])
    recv_block = jnp.where(
        jnp.any(pick, axis=2), jnp.sum(jnp.where(pick, block[:, None, :], 0), axis=2), NT
    )
    recv_block = recv_block.reshape(n_lvl, n_pcol * slots)

    rhs_cols = lax.dynamic_slice_in_dim(rhs[0, 0], row_index * cols, cols, axis=1)
    window_blocks = width // block_rows
    acc = jnp.zeros((NT + 1, block_rows, cols), jnp.float32)
    solved = jnp.zeros((width, cols), jnp.float32)
    for section in range(n_lvl):
        if section == 0:
            updates = first_cols
        else:
            right = rhs_cols - acc[:window_blocks].reshape(width, cols)
            solved_now = jnp.dot(
                inv_full, right.astype(jnp.bfloat16), preferred_element_type=jnp.float32
            )
            solved = jnp.where(level_index == section, solved_now, solved)
            updates = jnp.dot(
                tiles_full, solved_now.astype(jnp.bfloat16), preferred_element_type=jnp.float32
            ).astype(jnp.bfloat16)
        updates = updates.reshape(group_tiles + 1, block_rows, cols)
        sending = jnp.take(updates, send_index, axis=0, mode="clip")
        incoming = lax.all_to_all(
            sending, ("lvl", "pcol"), split_axis=0, concat_axis=0, tiled=True
        )
        incoming = incoming.reshape(n_lvl, n_pcol * slots, block_rows, cols)[section]
        acc = acc.at[recv_block[section]].add(incoming.astype(jnp.float32), mode="clip")
    outer = acc[window_blocks:NT].reshape(ABOVE, cols)

    solved_blocks = solved.reshape(n_prow, rows_out, cols)
    solved_high = lax.reduce_precision(solved_blocks, exponent_bits=8, mantissa_bits=7)
    solved_low = solved_blocks - solved_high
    final = jnp.concatenate(
        [
            solved_high.astype(jnp.bfloat16),
            solved_low.astype(jnp.bfloat16),
            jnp.broadcast_to(outer.astype(jnp.bfloat16)[None], (n_prow, ABOVE, cols)),
        ],
        axis=1,
    )
    final = lax.all_to_all(final, "prow", split_axis=0, concat_axis=0, tiled=True)
    final = final.astype(jnp.float32)
    solution_cols = final[:, :rows_out] + final[:, rows_out : 2 * rows_out]
    solution_rows = jnp.transpose(solution_cols, (1, 0, 2)).reshape(rows_out, columns_all)
    solution_rows = jnp.where(level_index == 0, first_rows, solution_rows)
    outer_all = jnp.transpose(final[:, 2 * rows_out :], (1, 0, 2)).reshape(ABOVE, columns_all)
    return (solution_rows[None, None], outer_all[None, None])


def solution(mesh):
    placed = (
        P("lvl", "pcol", None, None),
        P("lvl", "pcol", "prow", None),
        P("lvl", "pcol", "prow", None, None),
        P("lvl", "pcol", None),
        P("lvl", "pcol", "prow"),
        P("lvl", "pcol", "prow"),
        P("lvl", "pcol", "prow"),
    )
    return jax.shard_map(
        per_device,
        mesh=mesh,
        in_specs=placed,
        out_specs=(P("lvl", "pcol", "prow", None), P("lvl", "pcol", None, None)),
        check_vma=False,
    )
```

```python
import jax
import jax.numpy as jnp
from jax import lax
from jax.sharding import PartitionSpec as P

CAP = 2
ABOVE = 512
NT = 48


def per_device(
    rhs, diag_inverse, off_tiles, panel_super, off_device, off_block, offdiag_block_panel
):
    n_lvl = lax.axis_size("lvl")
    n_pcol = lax.axis_size("pcol")
    n_prow = lax.axis_size("prow")
    groups = n_lvl * n_pcol
    level_index = lax.axis_index("lvl")
    row_index = lax.axis_index("prow")
    col_index = lax.axis_index("pcol")
    my_group = level_index * n_pcol + col_index
    width = rhs.shape[2]
    columns_all = rhs.shape[3]
    cols = columns_all // n_prow
    row_count = diag_inverse.shape[2]
    tile_count = off_tiles.shape[2]
    block_rows = off_tiles.shape[3]
    group_tiles = n_prow * tile_count
    slots = n_prow * CAP

    panels = panel_super[0, 0]
    panel_count = panels.shape[0]
    panel_cols = width // panel_count
    panel_ids = jnp.arange(panel_count, dtype=jnp.int32)

    def super_of(panel):
        hit = panel[..., None] == panel_ids
        return jnp.sum(jnp.where(hit, panels, 0), axis=-1)

    col_super = super_of(jnp.arange(width, dtype=jnp.int32) // panel_cols)
    row_ids = row_index * row_count + jnp.arange(row_count, dtype=jnp.int32)
    row_super = super_of(row_ids // panel_cols)
    inverse = jnp.where(
        row_super[:, None] == col_super[None, :], diag_inverse[0, 0], jnp.zeros((), jnp.bfloat16)
    )
    tile_supernode = super_of(offdiag_block_panel[0, 0])
    tiles_used = jnp.where(
        col_super[None, None, :] == tile_supernode[:, None, None],
        off_tiles[0, 0],
        jnp.zeros((), jnp.bfloat16),
    ).reshape(tile_count * block_rows, width)

    both = jnp.concatenate([inverse, tiles_used], axis=0)
    gathered = lax.all_gather(both, "prow", axis=0)
    inv_full = gathered[:, :row_count].reshape(n_prow * row_count, width)
    tiles_full = gathered[:, row_count:].reshape(group_tiles * block_rows, width)
    tiles_full = jnp.concatenate(
        [tiles_full, jnp.zeros((block_rows, width), jnp.bfloat16)], axis=0
    )

    all_axes = ("lvl", "prow", "pcol")

    def level0_shift(x, shift):
        pairs = [
            (p * n_pcol + c, ((p + shift) % n_prow) * n_pcol + c)
            for p in range(n_prow)
            for c in range(n_pcol)
        ]
        return lax.ppermute(x, all_axes, pairs)

    def by_source(chunks):
        stacked = jnp.stack(chunks)
        order = (row_index - jnp.arange(n_prow, dtype=jnp.int32)) % n_prow
        return jnp.take(stacked, order, axis=0, mode="clip")

    rows_out = width // n_prow
    first_rows = jnp.dot(
        inverse, rhs[0, 0].astype(jnp.bfloat16), preferred_element_type=jnp.float32
    )
    first_half = first_rows.astype(jnp.bfloat16)
    first_all = by_source(
        [first_half] + [level0_shift(first_half, k) for k in range(1, n_prow)]
    ).reshape(width, columns_all)
    first_updates = jnp.dot(
        tiles_used, first_all, preferred_element_type=jnp.float32
    ).astype(jnp.bfloat16)

    def column_block(k):
        start = ((row_index + k) % n_prow) * cols
        return lax.dynamic_slice_in_dim(first_updates, start, cols, axis=1)

    first_cols = by_source(
        [column_block(0)] + [level0_shift(column_block(k), k) for k in range(1, n_prow)]
    ).reshape(group_tiles * block_rows, cols)
    first_cols = jnp.concatenate(
        [first_cols, jnp.zeros((block_rows, cols), jnp.bfloat16)], axis=0
    )

    meta = jnp.stack([off_device[0, 0], off_block[0, 0]], axis=0)
    devices = n_lvl * n_prow * n_pcol
    meta = lax.all_to_all(
        jnp.broadcast_to(meta[None], (devices,) + meta.shape),
        ("lvl", "prow", "pcol"),
        split_axis=0,
        concat_axis=0,
        tiled=True,
    )
    meta = meta.reshape(n_lvl, n_prow, n_pcol, 2, tile_count)
    meta = jnp.transpose(meta, (0, 2, 1, 3, 4)).reshape(groups, n_prow, 2, tile_count)
    target = meta[:, :, 0, :].reshape(groups, group_tiles)
    block = meta[:, :, 1, :].reshape(groups, group_tiles)
    tile_ids = jnp.arange(group_tiles, dtype=jnp.int32)
    source_row = tile_ids // tile_count
    earlier = (
        (target[:, :, None] == target[:, None, :])
        & (source_row[:, None] == source_row[None, :])[None]
        & (tile_ids[:, None] > tile_ids[None, :])[None]
    )
    position = jnp.sum(earlier.astype(jnp.int32), axis=2)
    local_slot = source_row[None, :] * CAP + position

    my_target = jnp.take(target, my_group, axis=0)
    my_slot = my_target * slots + jnp.take(local_slot, my_group, axis=0)
    send_match = my_slot[None, :] == jnp.arange(groups * slots, dtype=jnp.int32)[:, None]
    send_index = jnp.where(
        jnp.any(send_match, axis=1),
        jnp.sum(jnp.where(send_match, tile_ids[None, :], 0), axis=1),
        group_tiles,
    )

    to_me = target == my_group
    slot_ids = jnp.arange(slots, dtype=jnp.int32)
    pick = to_me[:, None, :] & (local_slot[:, None, :] == slot_ids[None, :, None])
    recv_block = jnp.where(
        jnp.any(pick, axis=2), jnp.sum(jnp.where(pick, block[:, None, :], 0), axis=2), NT
    )
    recv_block = recv_block.reshape(n_lvl, n_pcol * slots)

    rhs_cols = lax.dynamic_slice_in_dim(rhs[0, 0], row_index * cols, cols, axis=1)
    window_blocks = width // block_rows
    acc = jnp.zeros((NT + 1, block_rows, cols), jnp.float32)
    solved = jnp.zeros((width, cols), jnp.float32)
    for section in range(n_lvl):
        if section == 0:
            updates = first_cols
        else:
            right = rhs_cols - acc[:window_blocks].reshape(width, cols)
            solved_now = jnp.dot(
                inv_full, right.astype(jnp.bfloat16), preferred_element_type=jnp.float32
            )
            solved = jnp.where(level_index == section, solved_now, solved)
            updates = jnp.dot(
                tiles_full, solved_now.astype(jnp.bfloat16), preferred_element_type=jnp.float32
            ).astype(jnp.bfloat16)
        updates = updates.reshape(group_tiles + 1, block_rows, cols)
        sending = jnp.take(updates, send_index, axis=0, mode="clip")
        incoming = lax.all_to_all(
            sending, ("lvl", "pcol"), split_axis=0, concat_axis=0, tiled=True
        )
        incoming = incoming.reshape(n_lvl, n_pcol * slots, block_rows, cols)[section]
        acc = acc.at[recv_block[section]].add(incoming.astype(jnp.float32), mode="clip")
    outer = acc[window_blocks:NT].reshape(ABOVE, cols)

    solved_blocks = solved.reshape(n_prow, rows_out, cols)
    final = jnp.concatenate(
        [
            solved_blocks.astype(jnp.bfloat16),
            jnp.broadcast_to(outer.astype(jnp.bfloat16)[None], (n_prow, ABOVE, cols)),
        ],
        axis=1,
    )
    final = lax.all_to_all(final, "prow", split_axis=0, concat_axis=0, tiled=True)
    final = final.astype(jnp.float32)
    solution_rows = jnp.transpose(final[:, :rows_out], (1, 0, 2)).reshape(rows_out, columns_all)
    solution_rows = jnp.where(level_index == 0, first_rows, solution_rows)
    outer_all = jnp.transpose(final[:, rows_out:], (1, 0, 2)).reshape(ABOVE, columns_all)
    return (solution_rows[None, None], outer_all[None, None])


def solution(mesh):
    placed = (
        P("lvl", "pcol", None, None),
        P("lvl", "pcol", "prow", None),
        P("lvl", "pcol", "prow", None, None),
        P("lvl", "pcol", None),
        P("lvl", "pcol", "prow"),
        P("lvl", "pcol", "prow"),
        P("lvl", "pcol", "prow"),
    )
    return jax.shard_map(
        per_device,
        mesh=mesh,
        in_specs=placed,
        out_specs=(P("lvl", "pcol", "prow", None), P("lvl", "pcol", None, None)),
        check_vma=False,
    )
```

```python
import jax
import jax.numpy as jnp
from jax import lax
from jax.sharding import PartitionSpec as P

CAP = 2
ABOVE = 512
NT = 48


def per_device(
    rhs, diag_inverse, off_tiles, panel_super, off_device, off_block, offdiag_block_panel
):
    n_lvl = lax.axis_size("lvl")
    n_pcol = lax.axis_size("pcol")
    n_prow = lax.axis_size("prow")
    groups = n_lvl * n_pcol
    level_index = lax.axis_index("lvl")
    row_index = lax.axis_index("prow")
    col_index = lax.axis_index("pcol")
    my_group = level_index * n_pcol + col_index
    width = rhs.shape[2]
    columns_all = rhs.shape[3]
    cols = columns_all // n_prow
    row_count = diag_inverse.shape[2]
    tile_count = off_tiles.shape[2]
    block_rows = off_tiles.shape[3]
    group_tiles = n_prow * tile_count
    slots = n_prow * CAP

    panels = panel_super[0, 0]
    panel_count = panels.shape[0]
    panel_cols = width // panel_count
    panel_ids = jnp.arange(panel_count, dtype=jnp.int32)

    def super_of(panel):
        hit = panel[..., None] == panel_ids
        return jnp.sum(jnp.where(hit, panels, 0), axis=-1)

    col_super = super_of(jnp.arange(width, dtype=jnp.int32) // panel_cols)
    row_ids = row_index * row_count + jnp.arange(row_count, dtype=jnp.int32)
    row_super = super_of(row_ids // panel_cols)
    inverse = jnp.where(
        row_super[:, None] == col_super[None, :], diag_inverse[0, 0], jnp.zeros((), jnp.bfloat16)
    )
    tile_supernode = super_of(offdiag_block_panel[0, 0])
    tiles_used = jnp.where(
        col_super[None, None, :] == tile_supernode[:, None, None],
        off_tiles[0, 0],
        jnp.zeros((), jnp.bfloat16),
    ).reshape(tile_count * block_rows, width)

    both = jnp.concatenate([inverse, tiles_used], axis=0)
    gathered = lax.all_gather(both, "prow", axis=0)
    inv_full = gathered[:, :row_count].reshape(n_prow * row_count, width)
    tiles_full = gathered[:, row_count:].reshape(group_tiles * block_rows, width)
    tiles_full = jnp.concatenate(
        [tiles_full, jnp.zeros((block_rows, width), jnp.bfloat16)], axis=0
    )

    all_axes = ("lvl", "prow", "pcol")

    def level0_shift(x, shift):
        pairs = [
            (p * n_pcol + c, ((p + shift) % n_prow) * n_pcol + c)
            for p in range(n_prow)
            for c in range(n_pcol)
        ]
        return lax.ppermute(x, all_axes, pairs)

    def by_source(chunks):
        stacked = jnp.stack(chunks)
        order = (row_index - jnp.arange(n_prow, dtype=jnp.int32)) % n_prow
        return jnp.take(stacked, order, axis=0, mode="clip")

    rows_out = width // n_prow
    first_rows = jnp.dot(
        inverse, rhs[0, 0].astype(jnp.bfloat16), preferred_element_type=jnp.float32
    )
    first_half = first_rows.astype(jnp.bfloat16)
    first_all = by_source(
        [first_half] + [level0_shift(first_half, k) for k in range(1, n_prow)]
    ).reshape(width, columns_all)
    first_updates = jnp.dot(
        tiles_used, first_all, preferred_element_type=jnp.float32
    ).astype(jnp.bfloat16)

    def column_block(k):
        start = ((row_index + k) % n_prow) * cols
        return lax.dynamic_slice_in_dim(first_updates, start, cols, axis=1)

    first_cols = by_source(
        [column_block(0)] + [level0_shift(column_block(k), k) for k in range(1, n_prow)]
    ).reshape(group_tiles * block_rows, cols)
    first_cols = jnp.concatenate(
        [first_cols, jnp.zeros((block_rows, cols), jnp.bfloat16)], axis=0
    )

    meta = jnp.stack([off_device[0, 0], off_block[0, 0]], axis=0)
    devices = n_lvl * n_prow * n_pcol
    meta = lax.all_to_all(
        jnp.broadcast_to(meta[None], (devices,) + meta.shape),
        ("lvl", "prow", "pcol"),
        split_axis=0,
        concat_axis=0,
        tiled=True,
    )
    meta = meta.reshape(n_lvl, n_prow, n_pcol, 2, tile_count)
    meta = jnp.transpose(meta, (0, 2, 1, 3, 4)).reshape(groups, n_prow, 2, tile_count)
    target = meta[:, :, 0, :].reshape(groups, group_tiles)
    block = meta[:, :, 1, :].reshape(groups, group_tiles)
    tile_ids = jnp.arange(group_tiles, dtype=jnp.int32)
    source_row = tile_ids // tile_count
    earlier = (
        (target[:, :, None] == target[:, None, :])
        & (source_row[:, None] == source_row[None, :])[None]
        & (tile_ids[:, None] > tile_ids[None, :])[None]
    )
    position = jnp.sum(earlier.astype(jnp.int32), axis=2)
    local_slot = source_row[None, :] * CAP + position

    my_target = jnp.take(target, my_group, axis=0)
    my_slot = my_target * slots + jnp.take(local_slot, my_group, axis=0)
    send_match = my_slot[None, :] == jnp.arange(groups * slots, dtype=jnp.int32)[:, None]
    send_index = jnp.where(
        jnp.any(send_match, axis=1),
        jnp.sum(jnp.where(send_match, tile_ids[None, :], 0), axis=1),
        group_tiles,
    )

    to_me = target == my_group
    slot_ids = jnp.arange(slots, dtype=jnp.int32)
    pick = to_me[:, None, :] & (local_slot[:, None, :] == slot_ids[None, :, None])
    recv_block = jnp.where(
        jnp.any(pick, axis=2), jnp.sum(jnp.where(pick, block[:, None, :], 0), axis=2), NT
    )
    recv_block = recv_block.reshape(n_lvl, n_pcol * slots)

    rhs_cols = lax.dynamic_slice_in_dim(rhs[0, 0], row_index * cols, cols, axis=1)
    window_blocks = width // block_rows
    acc = jnp.zeros((NT + 1, block_rows, cols), jnp.float32)
    solved = jnp.zeros((width, cols), jnp.bfloat16)
    for section in range(n_lvl):
        if section == 0:
            updates = first_cols
        else:
            right = rhs_cols - acc[:window_blocks].reshape(width, cols)
            solved_now = jnp.dot(
                inv_full, right.astype(jnp.bfloat16), preferred_element_type=jnp.float32
            )
            solved_half = solved_now.astype(jnp.bfloat16)
            solved = jnp.where(level_index == section, solved_half, solved)
            updates = jnp.dot(
                tiles_full, solved_half, preferred_element_type=jnp.float32
            ).astype(jnp.bfloat16)
        updates = updates.reshape(group_tiles + 1, block_rows, cols)
        sending = jnp.take(updates, send_index, axis=0, mode="clip")
        incoming = lax.all_to_all(
            sending, ("lvl", "pcol"), split_axis=0, concat_axis=0, tiled=True
        )
        incoming = incoming.reshape(n_lvl, n_pcol * slots, block_rows, cols)[section]
        acc = acc.at[recv_block[section]].add(incoming.astype(jnp.float32), mode="clip")
    outer = acc[window_blocks:NT].reshape(ABOVE, cols)

    solved_blocks = solved.reshape(n_prow, rows_out, cols)
    final = jnp.concatenate(
        [
            solved_blocks,
            jnp.broadcast_to(outer.astype(jnp.bfloat16)[None], (n_prow, ABOVE, cols)),
        ],
        axis=1,
    )
    final = lax.all_to_all(final, "prow", split_axis=0, concat_axis=0, tiled=True)
    final = final.astype(jnp.float32)
    solution_rows = jnp.transpose(final[:, :rows_out], (1, 0, 2)).reshape(rows_out, columns_all)
    solution_rows = jnp.where(level_index == 0, first_rows, solution_rows)
    outer_all = jnp.transpose(final[:, rows_out:], (1, 0, 2)).reshape(ABOVE, columns_all)
    return (solution_rows[None, None], outer_all[None, None])


def solution(mesh):
    placed = (
        P("lvl", "pcol", None, None),
        P("lvl", "pcol", "prow", None),
        P("lvl", "pcol", "prow", None, None),
        P("lvl", "pcol", None),
        P("lvl", "pcol", "prow"),
        P("lvl", "pcol", "prow"),
        P("lvl", "pcol", "prow"),
    )
    return jax.shard_map(
        per_device,
        mesh=mesh,
        in_specs=placed,
        out_specs=(P("lvl", "pcol", "prow", None), P("lvl", "pcol", None, None)),
        check_vma=False,
    )
```

```python
import jax
import jax.numpy as jnp
from jax import lax
from jax.sharding import PartitionSpec as P

CAP = 2
ABOVE = 512
NT = 48


def per_device(
    rhs, diag_inverse, off_tiles, panel_super, off_device, off_block, offdiag_block_panel
):
    n_lvl = lax.axis_size("lvl")
    n_pcol = lax.axis_size("pcol")
    n_prow = lax.axis_size("prow")
    groups = n_lvl * n_pcol
    level_index = lax.axis_index("lvl")
    row_index = lax.axis_index("prow")
    col_index = lax.axis_index("pcol")
    my_group = level_index * n_pcol + col_index
    width = rhs.shape[2]
    columns_all = rhs.shape[3]
    cols = columns_all // n_prow
    row_count = diag_inverse.shape[2]
    tile_count = off_tiles.shape[2]
    block_rows = off_tiles.shape[3]
    group_tiles = n_prow * tile_count
    slots = n_prow * CAP

    panels = panel_super[0, 0]
    panel_count = panels.shape[0]
    panel_cols = width // panel_count
    panel_ids = jnp.arange(panel_count, dtype=jnp.int32)

    def super_of(panel):
        hit = panel[..., None] == panel_ids
        return jnp.sum(jnp.where(hit, panels, 0), axis=-1)

    col_super = super_of(jnp.arange(width, dtype=jnp.int32) // panel_cols)
    row_ids = row_index * row_count + jnp.arange(row_count, dtype=jnp.int32)
    row_super = super_of(row_ids // panel_cols)
    inverse = jnp.where(
        row_super[:, None] == col_super[None, :], diag_inverse[0, 0], jnp.zeros((), jnp.bfloat16)
    )
    tile_supernode = super_of(offdiag_block_panel[0, 0])
    tiles_used = jnp.where(
        col_super[None, None, :] == tile_supernode[:, None, None],
        off_tiles[0, 0],
        jnp.zeros((), jnp.bfloat16),
    ).reshape(tile_count * block_rows, width)

    raw = jnp.concatenate(
        [diag_inverse[0, 0], off_tiles[0, 0].reshape(tile_count * block_rows, width)], axis=0
    )
    gathered = lax.all_gather(raw, "prow", axis=0)
    zero = jnp.zeros((), jnp.bfloat16)
    inv_full = jnp.where(
        col_super[:, None] == col_super[None, :],
        gathered[:, :row_count].reshape(n_prow * row_count, width),
        zero,
    )

    all_axes = ("lvl", "prow", "pcol")

    def level0_shift(x, shift):
        pairs = [
            (p * n_pcol + c, ((p + shift) % n_prow) * n_pcol + c)
            for p in range(n_prow)
            for c in range(n_pcol)
        ]
        return lax.ppermute(x, all_axes, pairs)

    def by_source(chunks):
        stacked = jnp.stack(chunks)
        order = (row_index - jnp.arange(n_prow, dtype=jnp.int32)) % n_prow
        return jnp.take(stacked, order, axis=0, mode="clip")

    rows_out = width // n_prow
    first_rows = jnp.dot(
        inverse, rhs[0, 0].astype(jnp.bfloat16), preferred_element_type=jnp.float32
    )
    first_half = first_rows.astype(jnp.bfloat16)
    first_all = by_source(
        [first_half] + [level0_shift(first_half, k) for k in range(1, n_prow)]
    ).reshape(width, columns_all)
    first_updates = jnp.dot(
        tiles_used, first_all, preferred_element_type=jnp.float32
    ).astype(jnp.bfloat16)

    def column_block(k):
        start = ((row_index + k) % n_prow) * cols
        return lax.dynamic_slice_in_dim(first_updates, start, cols, axis=1)

    first_cols = by_source(
        [column_block(0)] + [level0_shift(column_block(k), k) for k in range(1, n_prow)]
    ).reshape(group_tiles * block_rows, cols)
    first_cols = jnp.concatenate(
        [first_cols, jnp.zeros((block_rows, cols), jnp.bfloat16)], axis=0
    )

    meta = jnp.stack([off_device[0, 0], off_block[0, 0], offdiag_block_panel[0, 0]], axis=0)
    devices = n_lvl * n_prow * n_pcol
    meta = lax.all_to_all(
        jnp.broadcast_to(meta[None], (devices,) + meta.shape),
        ("lvl", "prow", "pcol"),
        split_axis=0,
        concat_axis=0,
        tiled=True,
    )
    meta = meta.reshape(n_lvl, n_prow, n_pcol, 3, tile_count)
    meta = jnp.transpose(meta, (0, 2, 1, 3, 4)).reshape(groups, n_prow, 3, tile_count)
    target = meta[:, :, 0, :].reshape(groups, group_tiles)
    group_panels = jnp.take(meta[:, :, 2, :].reshape(groups, group_tiles), my_group, axis=0)
    tiles_full = jnp.where(
        col_super[None, None, :] == super_of(group_panels)[:, None, None],
        gathered[:, row_count:].reshape(group_tiles, block_rows, width),
        zero,
    ).reshape(group_tiles * block_rows, width)
    tiles_full = jnp.concatenate(
        [tiles_full, jnp.zeros((block_rows, width), jnp.bfloat16)], axis=0
    )
    block = meta[:, :, 1, :].reshape(groups, group_tiles)
    tile_ids = jnp.arange(group_tiles, dtype=jnp.int32)
    source_row = tile_ids // tile_count
    earlier = (
        (target[:, :, None] == target[:, None, :])
        & (source_row[:, None] == source_row[None, :])[None]
        & (tile_ids[:, None] > tile_ids[None, :])[None]
    )
    position = jnp.sum(earlier.astype(jnp.int32), axis=2)
    local_slot = source_row[None, :] * CAP + position

    my_target = jnp.take(target, my_group, axis=0)
    my_slot = my_target * slots + jnp.take(local_slot, my_group, axis=0)
    send_match = my_slot[None, :] == jnp.arange(groups * slots, dtype=jnp.int32)[:, None]
    send_index = jnp.where(
        jnp.any(send_match, axis=1),
        jnp.sum(jnp.where(send_match, tile_ids[None, :], 0), axis=1),
        group_tiles,
    )

    to_me = target == my_group
    slot_ids = jnp.arange(slots, dtype=jnp.int32)
    pick = to_me[:, None, :] & (local_slot[:, None, :] == slot_ids[None, :, None])
    recv_block = jnp.where(
        jnp.any(pick, axis=2), jnp.sum(jnp.where(pick, block[:, None, :], 0), axis=2), NT
    )
    recv_block = recv_block.reshape(n_lvl, n_pcol * slots)

    rhs_cols = lax.dynamic_slice_in_dim(rhs[0, 0], row_index * cols, cols, axis=1)
    window_blocks = width // block_rows
    acc = jnp.zeros((NT + 1, block_rows, cols), jnp.float32)
    solved = jnp.zeros((width, cols), jnp.float32)
    for section in range(n_lvl):
        if section == 0:
            updates = first_cols
        else:
            right = rhs_cols - acc[:window_blocks].reshape(width, cols)
            solved_now = jnp.dot(
                inv_full, right.astype(jnp.bfloat16), preferred_element_type=jnp.float32
            )
            solved = jnp.where(level_index == section, solved_now, solved)
            updates = jnp.dot(
                tiles_full, solved_now.astype(jnp.bfloat16), preferred_element_type=jnp.float32
            ).astype(jnp.bfloat16)
        updates = updates.reshape(group_tiles + 1, block_rows, cols)
        sending = jnp.take(updates, send_index, axis=0, mode="clip")
        incoming = lax.all_to_all(
            sending, ("lvl", "pcol"), split_axis=0, concat_axis=0, tiled=True
        )
        incoming = incoming.reshape(n_lvl, n_pcol * slots, block_rows, cols)[section]
        acc = acc.at[recv_block[section]].add(incoming.astype(jnp.float32), mode="clip")
    outer = acc[window_blocks:NT].reshape(ABOVE, cols)

    solved_blocks = solved.reshape(n_prow, rows_out, cols)
    final = jnp.concatenate(
        [
            solved_blocks.astype(jnp.bfloat16),
            jnp.broadcast_to(outer.astype(jnp.bfloat16)[None], (n_prow, ABOVE, cols)),
        ],
        axis=1,
    )
    final = lax.all_to_all(final, "prow", split_axis=0, concat_axis=0, tiled=True)
    final = final.astype(jnp.float32)
    solution_rows = jnp.transpose(final[:, :rows_out], (1, 0, 2)).reshape(rows_out, columns_all)
    solution_rows = jnp.where(level_index == 0, first_rows, solution_rows)
    outer_all = jnp.transpose(final[:, rows_out:], (1, 0, 2)).reshape(ABOVE, columns_all)
    return (solution_rows[None, None], outer_all[None, None])


def solution(mesh):
    placed = (
        P("lvl", "pcol", None, None),
        P("lvl", "pcol", "prow", None),
        P("lvl", "pcol", "prow", None, None),
        P("lvl", "pcol", None),
        P("lvl", "pcol", "prow"),
        P("lvl", "pcol", "prow"),
        P("lvl", "pcol", "prow"),
    )
    return jax.shard_map(
        per_device,
        mesh=mesh,
        in_specs=placed,
        out_specs=(P("lvl", "pcol", "prow", None), P("lvl", "pcol", None, None)),
        check_vma=False,
    )
```

```python
import jax
import jax.numpy as jnp
from jax import lax
from jax.sharding import PartitionSpec as P

CAP = 2
ABOVE = 512
NT = 48


def per_device(
    rhs, diag_inverse, off_tiles, panel_super, off_device, off_block, offdiag_block_panel
):
    n_lvl = lax.axis_size("lvl")
    n_pcol = lax.axis_size("pcol")
    n_prow = lax.axis_size("prow")
    groups = n_lvl * n_pcol
    level_index = lax.axis_index("lvl")
    row_index = lax.axis_index("prow")
    col_index = lax.axis_index("pcol")
    my_group = level_index * n_pcol + col_index
    width = rhs.shape[2]
    columns_all = rhs.shape[3]
    cols = columns_all // n_prow
    row_count = diag_inverse.shape[2]
    tile_count = off_tiles.shape[2]
    block_rows = off_tiles.shape[3]
    group_tiles = n_prow * tile_count
    slots = n_prow * CAP

    panels = panel_super[0, 0]
    panel_count = panels.shape[0]
    panel_cols = width // panel_count
    panel_ids = jnp.arange(panel_count, dtype=jnp.int32)

    def super_of(panel):
        hit = panel[..., None] == panel_ids
        return jnp.sum(jnp.where(hit, panels, 0), axis=-1)

    col_super = super_of(jnp.arange(width, dtype=jnp.int32) // panel_cols)
    row_ids = row_index * row_count + jnp.arange(row_count, dtype=jnp.int32)
    row_super = super_of(row_ids // panel_cols)
    inverse = jnp.where(
        row_super[:, None] == col_super[None, :], diag_inverse[0, 0], jnp.zeros((), jnp.bfloat16)
    )
    tile_supernode = super_of(offdiag_block_panel[0, 0])
    tiles_used = jnp.where(
        col_super[None, None, :] == tile_supernode[:, None, None],
        off_tiles[0, 0],
        jnp.zeros((), jnp.bfloat16),
    ).reshape(tile_count * block_rows, width)

    inv_raw, tiles_raw = lax.all_gather(
        (diag_inverse[0, 0], off_tiles[0, 0]), "prow", axis=0, tiled=True
    )
    zero = jnp.zeros((), jnp.bfloat16)
    inv_full = jnp.where(col_super[:, None] == col_super[None, :], inv_raw, zero)

    all_axes = ("lvl", "prow", "pcol")

    def level0_shift(x, shift):
        pairs = [
            (p * n_pcol + c, ((p + shift) % n_prow) * n_pcol + c)
            for p in range(n_prow)
            for c in range(n_pcol)
        ]
        return lax.ppermute(x, all_axes, pairs)

    def by_source(chunks):
        stacked = jnp.stack(chunks)
        order = (row_index - jnp.arange(n_prow, dtype=jnp.int32)) % n_prow
        return jnp.take(stacked, order, axis=0, mode="clip")

    rows_out = width // n_prow
    first_rows = jnp.dot(
        inverse, rhs[0, 0].astype(jnp.bfloat16), preferred_element_type=jnp.float32
    )
    first_half = first_rows.astype(jnp.bfloat16)
    first_all = by_source(
        [first_half] + [level0_shift(first_half, k) for k in range(1, n_prow)]
    ).reshape(width, columns_all)
    first_updates = jnp.dot(
        tiles_used, first_all, preferred_element_type=jnp.float32
    ).astype(jnp.bfloat16)

    def column_block(k):
        start = ((row_index + k) % n_prow) * cols
        return lax.dynamic_slice_in_dim(first_updates, start, cols, axis=1)

    first_cols = by_source(
        [column_block(0)] + [level0_shift(column_block(k), k) for k in range(1, n_prow)]
    ).reshape(group_tiles * block_rows, cols)
    first_cols = jnp.concatenate(
        [first_cols, jnp.zeros((block_rows, cols), jnp.bfloat16)], axis=0
    )

    meta = jnp.stack([off_device[0, 0], off_block[0, 0], offdiag_block_panel[0, 0]], axis=0)
    devices = n_lvl * n_prow * n_pcol
    meta = lax.all_to_all(
        jnp.broadcast_to(meta[None], (devices,) + meta.shape),
        ("lvl", "prow", "pcol"),
        split_axis=0,
        concat_axis=0,
        tiled=True,
    )
    meta = meta.reshape(n_lvl, n_prow, n_pcol, 3, tile_count)
    meta = jnp.transpose(meta, (0, 2, 1, 3, 4)).reshape(groups, n_prow, 3, tile_count)
    target = meta[:, :, 0, :].reshape(groups, group_tiles)
    group_panels = jnp.take(meta[:, :, 2, :].reshape(groups, group_tiles), my_group, axis=0)
    tiles_full = jnp.where(
        col_super[None, None, :] == super_of(group_panels)[:, None, None],
        tiles_raw,
        zero,
    ).reshape(group_tiles * block_rows, width)
    tiles_full = jnp.concatenate(
        [tiles_full, jnp.zeros((block_rows, width), jnp.bfloat16)], axis=0
    )
    block = meta[:, :, 1, :].reshape(groups, group_tiles)
    tile_ids = jnp.arange(group_tiles, dtype=jnp.int32)
    source_row = tile_ids // tile_count
    earlier = (
        (target[:, :, None] == target[:, None, :])
        & (source_row[:, None] == source_row[None, :])[None]
        & (tile_ids[:, None] > tile_ids[None, :])[None]
    )
    position = jnp.sum(earlier.astype(jnp.int32), axis=2)
    local_slot = source_row[None, :] * CAP + position

    my_target = jnp.take(target, my_group, axis=0)
    my_slot = my_target * slots + jnp.take(local_slot, my_group, axis=0)
    send_match = my_slot[None, :] == jnp.arange(groups * slots, dtype=jnp.int32)[:, None]
    send_index = jnp.where(
        jnp.any(send_match, axis=1),
        jnp.sum(jnp.where(send_match, tile_ids[None, :], 0), axis=1),
        group_tiles,
    )

    to_me = target == my_group
    slot_ids = jnp.arange(slots, dtype=jnp.int32)
    pick = to_me[:, None, :] & (local_slot[:, None, :] == slot_ids[None, :, None])
    recv_block = jnp.where(
        jnp.any(pick, axis=2), jnp.sum(jnp.where(pick, block[:, None, :], 0), axis=2), NT
    )
    recv_block = recv_block.reshape(n_lvl, n_pcol * slots)

    rhs_cols = lax.dynamic_slice_in_dim(rhs[0, 0], row_index * cols, cols, axis=1)
    window_blocks = width // block_rows
    acc = jnp.zeros((NT + 1, block_rows, cols), jnp.float32)
    solved = jnp.zeros((width, cols), jnp.float32)
    for section in range(n_lvl):
        if section == 0:
            updates = first_cols
        else:
            right = rhs_cols - acc[:window_blocks].reshape(width, cols)
            solved_now = jnp.dot(
                inv_full, right.astype(jnp.bfloat16), preferred_element_type=jnp.float32
            )
            solved = jnp.where(level_index == section, solved_now, solved)
            updates = jnp.dot(
                tiles_full, solved_now.astype(jnp.bfloat16), preferred_element_type=jnp.float32
            ).astype(jnp.bfloat16)
        updates = updates.reshape(group_tiles + 1, block_rows, cols)
        sending = jnp.take(updates, send_index, axis=0, mode="clip")
        incoming = lax.all_to_all(
            sending, ("lvl", "pcol"), split_axis=0, concat_axis=0, tiled=True
        )
        incoming = incoming.reshape(n_lvl, n_pcol * slots, block_rows, cols)[section]
        acc = acc.at[recv_block[section]].add(incoming.astype(jnp.float32), mode="clip")
    outer = acc[window_blocks:NT].reshape(ABOVE, cols)

    solved_blocks = solved.reshape(n_prow, rows_out, cols)
    final = jnp.concatenate(
        [
            solved_blocks.astype(jnp.bfloat16),
            jnp.broadcast_to(outer.astype(jnp.bfloat16)[None], (n_prow, ABOVE, cols)),
        ],
        axis=1,
    )
    final = lax.all_to_all(final, "prow", split_axis=0, concat_axis=0, tiled=True)
    final = final.astype(jnp.float32)
    solution_rows = jnp.transpose(final[:, :rows_out], (1, 0, 2)).reshape(rows_out, columns_all)
    solution_rows = jnp.where(level_index == 0, first_rows, solution_rows)
    outer_all = jnp.transpose(final[:, rows_out:], (1, 0, 2)).reshape(ABOVE, columns_all)
    return (solution_rows[None, None], outer_all[None, None])


def solution(mesh):
    placed = (
        P("lvl", "pcol", None, None),
        P("lvl", "pcol", "prow", None),
        P("lvl", "pcol", "prow", None, None),
        P("lvl", "pcol", None),
        P("lvl", "pcol", "prow"),
        P("lvl", "pcol", "prow"),
        P("lvl", "pcol", "prow"),
    )
    return jax.shard_map(
        per_device,
        mesh=mesh,
        in_specs=placed,
        out_specs=(P("lvl", "pcol", "prow", None), P("lvl", "pcol", None, None)),
        check_vma=False,
    )
```

```python
import jax
import jax.numpy as jnp
from jax import lax
from jax.sharding import PartitionSpec as P

CAP = 2
ABOVE = 512
NT = 48


def per_device(
    rhs, diag_inverse, off_tiles, panel_super, off_device, off_block, offdiag_block_panel
):
    n_lvl = lax.axis_size("lvl")
    n_pcol = lax.axis_size("pcol")
    n_prow = lax.axis_size("prow")
    groups = n_lvl * n_pcol
    level_index = lax.axis_index("lvl")
    row_index = lax.axis_index("prow")
    col_index = lax.axis_index("pcol")
    my_group = level_index * n_pcol + col_index
    width = rhs.shape[2]
    columns_all = rhs.shape[3]
    cols = columns_all // n_prow
    row_count = diag_inverse.shape[2]
    tile_count = off_tiles.shape[2]
    block_rows = off_tiles.shape[3]
    group_tiles = n_prow * tile_count
    slots = n_prow * CAP

    panels = panel_super[0, 0]
    panel_count = panels.shape[0]
    panel_cols = width // panel_count
    panel_ids = jnp.arange(panel_count, dtype=jnp.int32)

    def super_of(panel):
        hit = panel[..., None] == panel_ids
        return jnp.sum(jnp.where(hit, panels, 0), axis=-1)

    col_super = super_of(jnp.arange(width, dtype=jnp.int32) // panel_cols)
    row_ids = row_index * row_count + jnp.arange(row_count, dtype=jnp.int32)
    row_super = super_of(row_ids // panel_cols)
    inverse = jnp.where(
        row_super[:, None] == col_super[None, :], diag_inverse[0, 0], jnp.zeros((), jnp.bfloat16)
    )
    tile_supernode = super_of(offdiag_block_panel[0, 0])
    tiles_used = jnp.where(
        col_super[None, None, :] == tile_supernode[:, None, None],
        off_tiles[0, 0],
        jnp.zeros((), jnp.bfloat16),
    ).reshape(tile_count * block_rows, width)

    raw = jnp.concatenate(
        [diag_inverse[0, 0], off_tiles[0, 0].reshape(tile_count * block_rows, width)], axis=0
    )
    gathered = lax.all_gather(raw, "prow", axis=0)
    zero = jnp.zeros((), jnp.bfloat16)
    inv_full = jnp.where(
        col_super[:, None] == col_super[None, :],
        gathered[:, :row_count].reshape(n_prow * row_count, width),
        zero,
    )

    all_axes = ("lvl", "prow", "pcol")

    def level0_shift(x, shift):
        pairs = [
            (p * n_pcol + c, ((p + shift) % n_prow) * n_pcol + c)
            for p in range(n_prow)
            for c in range(n_pcol)
        ]
        return lax.ppermute(x, all_axes, pairs)

    def by_source(chunks):
        stacked = jnp.stack(chunks)
        order = (row_index - jnp.arange(n_prow, dtype=jnp.int32)) % n_prow
        return jnp.take(stacked, order, axis=0, mode="clip")

    rows_out = width // n_prow
    first_rows = jnp.dot(
        inverse, rhs[0, 0].astype(jnp.bfloat16), preferred_element_type=jnp.float32
    )
    first_half = first_rows.astype(jnp.bfloat16)
    first_all = by_source(
        [first_half] + [level0_shift(first_half, k) for k in range(1, n_prow)]
    ).reshape(width, columns_all)
    first_updates = jnp.dot(
        tiles_used, first_all, preferred_element_type=jnp.float32
    ).astype(jnp.bfloat16)

    def column_block(k):
        start = ((row_index + k) % n_prow) * cols
        return lax.dynamic_slice_in_dim(first_updates, start, cols, axis=1)

    first_cols = by_source(
        [column_block(0)] + [level0_shift(column_block(k), k) for k in range(1, n_prow)]
    ).reshape(group_tiles * block_rows, cols)
    first_cols = jnp.concatenate(
        [first_cols, jnp.zeros((block_rows, cols), jnp.bfloat16)], axis=0
    )

    meta = jnp.stack([off_device[0, 0], off_block[0, 0], offdiag_block_panel[0, 0]], axis=0)
    devices = n_lvl * n_prow * n_pcol
    meta = lax.all_to_all(
        jnp.broadcast_to(meta[None], (devices,) + meta.shape),
        ("lvl", "prow", "pcol"),
        split_axis=0,
        concat_axis=0,
        tiled=True,
    )
    meta = meta.reshape(n_lvl, n_prow, n_pcol, 3, tile_count)
    meta = jnp.transpose(meta, (0, 2, 1, 3, 4)).reshape(groups, n_prow, 3, tile_count)
    target = meta[:, :, 0, :].reshape(groups, group_tiles)
    group_panels = jnp.take(meta[:, :, 2, :].reshape(groups, group_tiles), my_group, axis=0)
    tiles_full = jnp.where(
        col_super[None, None, :] == super_of(group_panels)[:, None, None],
        gathered[:, row_count:].reshape(group_tiles, block_rows, width),
        zero,
    ).reshape(group_tiles * block_rows, width)
    tiles_full = jnp.concatenate(
        [tiles_full, jnp.zeros((block_rows, width), jnp.bfloat16)], axis=0
    )
    block = meta[:, :, 1, :].reshape(groups, group_tiles)
    tile_ids = jnp.arange(group_tiles, dtype=jnp.int32)
    source_row = tile_ids // tile_count
    earlier = (
        (target[:, :, None] == target[:, None, :])
        & (source_row[:, None] == source_row[None, :])[None]
        & (tile_ids[:, None] > tile_ids[None, :])[None]
    )
    position = jnp.sum(earlier.astype(jnp.int32), axis=2)
    local_slot = source_row[None, :] * CAP + position

    my_target = jnp.take(target, my_group, axis=0)
    my_slot = my_target * slots + jnp.take(local_slot, my_group, axis=0)
    send_match = my_slot[None, :] == jnp.arange(groups * slots, dtype=jnp.int32)[:, None]
    send_index = jnp.where(
        jnp.any(send_match, axis=1),
        jnp.sum(jnp.where(send_match, tile_ids[None, :], 0), axis=1),
        group_tiles,
    )

    to_me = target == my_group
    slot_ids = jnp.arange(slots, dtype=jnp.int32)
    pick = to_me[:, None, :] & (local_slot[:, None, :] == slot_ids[None, :, None])
    recv_block = jnp.where(
        jnp.any(pick, axis=2), jnp.sum(jnp.where(pick, block[:, None, :], 0), axis=2), NT
    )
    recv_block = recv_block.reshape(n_lvl, n_pcol * slots)

    rhs_cols = lax.dynamic_slice_in_dim(rhs[0, 0], row_index * cols, cols, axis=1)
    window_blocks = width // block_rows
    acc = jnp.zeros((NT + 1, block_rows, cols), jnp.float32)
    solved = jnp.zeros((width, cols), jnp.float32)
    for section in range(n_lvl):
        if section == 0:
            updates = first_cols
        else:
            right = rhs_cols - acc[:window_blocks].reshape(width, cols)
            solved_now = jnp.dot(
                inv_full, right.astype(jnp.bfloat16), preferred_element_type=jnp.float32
            )
            solved = jnp.where(level_index == section, solved_now, solved)
            updates = jnp.dot(
                tiles_full, solved_now.astype(jnp.bfloat16), preferred_element_type=jnp.float32
            ).astype(jnp.bfloat16)
        updates = updates.reshape(group_tiles + 1, block_rows, cols)
        sending = jnp.take(updates, send_index, axis=0, mode="clip")
        incoming = lax.all_to_all(
            sending, ("lvl", "pcol"), split_axis=0, concat_axis=0, tiled=True
        )
        incoming = incoming.reshape(n_lvl, n_pcol * slots, block_rows, cols)[section]
        acc = acc.at[recv_block[section]].add(incoming.astype(jnp.float32), mode="clip")
    outer = acc[window_blocks:NT].reshape(ABOVE, cols)

    solved_blocks = solved.reshape(n_prow, rows_out, cols)
    final = jnp.concatenate(
        [
            solved_blocks.astype(jnp.bfloat16),
            jnp.broadcast_to(outer.astype(jnp.bfloat16)[None], (n_prow, ABOVE, cols)),
        ],
        axis=1,
    )
    final_shape = final.shape
    final = lax.all_to_all(
        final.reshape(n_prow, -1), "prow", split_axis=0, concat_axis=0, tiled=True
    ).reshape(final_shape)
    final = final.astype(jnp.float32)
    solution_rows = jnp.transpose(final[:, :rows_out], (1, 0, 2)).reshape(rows_out, columns_all)
    solution_rows = jnp.where(level_index == 0, first_rows, solution_rows)
    outer_all = jnp.transpose(final[:, rows_out:], (1, 0, 2)).reshape(ABOVE, columns_all)
    return (solution_rows[None, None], outer_all[None, None])


def solution(mesh):
    placed = (
        P("lvl", "pcol", None, None),
        P("lvl", "pcol", "prow", None),
        P("lvl", "pcol", "prow", None, None),
        P("lvl", "pcol", None),
        P("lvl", "pcol", "prow"),
        P("lvl", "pcol", "prow"),
        P("lvl", "pcol", "prow"),
    )
    return jax.shard_map(
        per_device,
        mesh=mesh,
        in_specs=placed,
        out_specs=(P("lvl", "pcol", "prow", None), P("lvl", "pcol", None, None)),
        check_vma=False,
    )
```

```python
import jax
import jax.numpy as jnp
from jax import lax
from jax.sharding import PartitionSpec as P

CAP = 2
ABOVE = 512
NT = 48


def per_device(
    rhs, diag_inverse, off_tiles, panel_super, off_device, off_block, offdiag_block_panel
):
    n_lvl = lax.axis_size("lvl")
    n_pcol = lax.axis_size("pcol")
    n_prow = lax.axis_size("prow")
    groups = n_lvl * n_pcol
    level_index = lax.axis_index("lvl")
    row_index = lax.axis_index("prow")
    col_index = lax.axis_index("pcol")
    my_group = level_index * n_pcol + col_index
    width = rhs.shape[2]
    columns_all = rhs.shape[3]
    cols = columns_all // n_prow
    row_count = diag_inverse.shape[2]
    tile_count = off_tiles.shape[2]
    block_rows = off_tiles.shape[3]
    group_tiles = n_prow * tile_count
    slots = n_prow * CAP

    panels = panel_super[0, 0]
    panel_count = panels.shape[0]
    panel_cols = width // panel_count
    panel_ids = jnp.arange(panel_count, dtype=jnp.int32)

    def super_of(panel):
        hit = panel[..., None] == panel_ids
        return jnp.sum(jnp.where(hit, panels, 0), axis=-1)

    col_super = super_of(jnp.arange(width, dtype=jnp.int32) // panel_cols)
    row_ids = row_index * row_count + jnp.arange(row_count, dtype=jnp.int32)
    row_super = super_of(row_ids // panel_cols)
    inverse = jnp.where(
        row_super[:, None] == col_super[None, :], diag_inverse[0, 0], jnp.zeros((), jnp.bfloat16)
    )
    tile_supernode = super_of(offdiag_block_panel[0, 0])
    tiles_used = jnp.where(
        col_super[None, None, :] == tile_supernode[:, None, None],
        off_tiles[0, 0],
        jnp.zeros((), jnp.bfloat16),
    ).reshape(tile_count * block_rows, width)

    raw = jnp.concatenate(
        [diag_inverse[0, 0], off_tiles[0, 0].reshape(tile_count * block_rows, width)], axis=0
    )
    gathered = lax.all_gather(raw, "prow", axis=0)
    zero = jnp.zeros((), jnp.bfloat16)
    inv_full = jnp.where(
        col_super[:, None] == col_super[None, :],
        gathered[:, :row_count].reshape(n_prow * row_count, width),
        zero,
    )

    all_axes = ("lvl", "prow", "pcol")

    def level0_shift(x, shift):
        pairs = [
            (p * n_pcol + c, ((p + shift) % n_prow) * n_pcol + c)
            for p in range(n_prow)
            for c in range(n_pcol)
        ]
        return lax.ppermute(x, all_axes, pairs)

    def by_source(chunks):
        stacked = jnp.stack(chunks)
        order = (row_index - jnp.arange(n_prow, dtype=jnp.int32)) % n_prow
        return jnp.take(stacked, order, axis=0, mode="clip")

    rows_out = width // n_prow
    first_rows = jnp.dot(
        inverse, rhs[0, 0].astype(jnp.bfloat16), preferred_element_type=jnp.float32
    )
    first_half = first_rows.astype(jnp.bfloat16)
    first_all = by_source(
        [first_half] + [level0_shift(first_half, k) for k in range(1, n_prow)]
    ).reshape(width, columns_all)
    first_updates = jnp.dot(
        tiles_used, first_all, preferred_element_type=jnp.float32
    ).astype(jnp.bfloat16)

    def column_block(k):
        start = ((row_index + k) % n_prow) * cols
        return lax.dynamic_slice_in_dim(first_updates, start, cols, axis=1)

    first_cols = by_source(
        [column_block(0)] + [level0_shift(column_block(k), k) for k in range(1, n_prow)]
    ).reshape(group_tiles * block_rows, cols)
    first_cols = jnp.concatenate(
        [first_cols, jnp.zeros((block_rows, cols), jnp.bfloat16)], axis=0
    )

    meta = jnp.stack([off_device[0, 0], off_block[0, 0], offdiag_block_panel[0, 0]], axis=0)
    devices = n_lvl * n_prow * n_pcol
    meta = lax.all_to_all(
        jnp.broadcast_to(meta[None], (devices,) + meta.shape),
        ("lvl", "prow", "pcol"),
        split_axis=0,
        concat_axis=0,
        tiled=True,
    )
    meta = meta.reshape(n_lvl, n_prow, n_pcol, 3, tile_count)
    meta = jnp.transpose(meta, (0, 2, 1, 3, 4)).reshape(groups, n_prow, 3, tile_count)
    target = meta[:, :, 0, :].reshape(groups, group_tiles)
    group_panels = jnp.take(meta[:, :, 2, :].reshape(groups, group_tiles), my_group, axis=0)
    tiles_full = jnp.where(
        col_super[None, None, :] == super_of(group_panels)[:, None, None],
        gathered[:, row_count:].reshape(group_tiles, block_rows, width),
        zero,
    ).reshape(group_tiles * block_rows, width)
    tiles_full = jnp.concatenate(
        [tiles_full, jnp.zeros((block_rows, width), jnp.bfloat16)], axis=0
    )
    block = meta[:, :, 1, :].reshape(groups, group_tiles)
    tile_ids = jnp.arange(group_tiles, dtype=jnp.int32)
    source_row = tile_ids // tile_count
    earlier = (
        (target[:, :, None] == target[:, None, :])
        & (source_row[:, None] == source_row[None, :])[None]
        & (tile_ids[:, None] > tile_ids[None, :])[None]
    )
    position = jnp.sum(earlier.astype(jnp.int32), axis=2)
    local_slot = source_row[None, :] * CAP + position

    my_target = jnp.take(target, my_group, axis=0)
    my_slot = my_target * slots + jnp.take(local_slot, my_group, axis=0)
    send_match = my_slot[None, :] == jnp.arange(groups * slots, dtype=jnp.int32)[:, None]
    send_index = jnp.where(
        jnp.any(send_match, axis=1),
        jnp.sum(jnp.where(send_match, tile_ids[None, :], 0), axis=1),
        group_tiles,
    )

    to_me = target == my_group
    slot_ids = jnp.arange(slots, dtype=jnp.int32)
    pick = to_me[:, None, :] & (local_slot[:, None, :] == slot_ids[None, :, None])
    recv_block = jnp.where(
        jnp.any(pick, axis=2), jnp.sum(jnp.where(pick, block[:, None, :], 0), axis=2), NT
    )
    recv_block = recv_block.reshape(n_lvl, n_pcol * slots)

    rhs_cols = lax.dynamic_slice_in_dim(rhs[0, 0], row_index * cols, cols, axis=1)
    window_blocks = width // block_rows
    acc = jnp.zeros((NT + 1, block_rows, cols), jnp.float32)
    solved = jnp.zeros((width, cols), jnp.float32)
    for section in range(n_lvl):
        if section == 0:
            updates = first_cols
        else:
            right = rhs_cols - acc[:window_blocks].reshape(width, cols)
            solved_now = jnp.dot(
                inv_full, right.astype(jnp.bfloat16), preferred_element_type=jnp.float32
            )
            solved = jnp.where(level_index == section, solved_now, solved)
            updates = jnp.dot(
                tiles_full, solved_now.astype(jnp.bfloat16), preferred_element_type=jnp.float32
            ).astype(jnp.bfloat16)
        updates = updates.reshape(group_tiles + 1, block_rows * cols)
        sending = jnp.take(updates, send_index, axis=0, mode="clip")
        incoming = lax.all_to_all(
            sending.reshape(groups, slots * block_rows * cols),
            ("lvl", "pcol"),
            split_axis=0,
            concat_axis=0,
            tiled=True,
        )
        incoming = incoming.reshape(n_lvl, n_pcol * slots, block_rows, cols)[section]
        acc = acc.at[recv_block[section]].add(incoming.astype(jnp.float32), mode="clip")
    outer = acc[window_blocks:NT].reshape(ABOVE, cols)

    solved_blocks = solved.reshape(n_prow, rows_out, cols)
    final = jnp.concatenate(
        [
            solved_blocks.astype(jnp.bfloat16),
            jnp.broadcast_to(outer.astype(jnp.bfloat16)[None], (n_prow, ABOVE, cols)),
        ],
        axis=1,
    )
    final = lax.all_to_all(final, "prow", split_axis=0, concat_axis=0, tiled=True)
    final = final.astype(jnp.float32)
    solution_rows = jnp.transpose(final[:, :rows_out], (1, 0, 2)).reshape(rows_out, columns_all)
    solution_rows = jnp.where(level_index == 0, first_rows, solution_rows)
    outer_all = jnp.transpose(final[:, rows_out:], (1, 0, 2)).reshape(ABOVE, columns_all)
    return (solution_rows[None, None], outer_all[None, None])


def solution(mesh):
    placed = (
        P("lvl", "pcol", None, None),
        P("lvl", "pcol", "prow", None),
        P("lvl", "pcol", "prow", None, None),
        P("lvl", "pcol", None),
        P("lvl", "pcol", "prow"),
        P("lvl", "pcol", "prow"),
        P("lvl", "pcol", "prow"),
    )
    return jax.shard_map(
        per_device,
        mesh=mesh,
        in_specs=placed,
        out_specs=(P("lvl", "pcol", "prow", None), P("lvl", "pcol", None, None)),
        check_vma=False,
    )
```

```python
import jax
import jax.numpy as jnp
from jax import lax
from jax.sharding import PartitionSpec as P

CAP = 2
ABOVE = 512
NT = 48


def per_device(
    rhs, diag_inverse, off_tiles, panel_super, off_device, off_block, offdiag_block_panel
):
    n_lvl = lax.axis_size("lvl")
    n_pcol = lax.axis_size("pcol")
    n_prow = lax.axis_size("prow")
    groups = n_lvl * n_pcol
    level_index = lax.axis_index("lvl")
    row_index = lax.axis_index("prow")
    col_index = lax.axis_index("pcol")
    my_group = level_index * n_pcol + col_index
    width = rhs.shape[2]
    columns_all = rhs.shape[3]
    cols = columns_all // n_prow
    row_count = diag_inverse.shape[2]
    tile_count = off_tiles.shape[2]
    block_rows = off_tiles.shape[3]
    group_tiles = n_prow * tile_count
    slots = n_prow * CAP

    panels = panel_super[0, 0]
    panel_count = panels.shape[0]
    panel_cols = width // panel_count
    panel_ids = jnp.arange(panel_count, dtype=jnp.int32)

    def super_of(panel):
        hit = panel[..., None] == panel_ids
        return jnp.sum(jnp.where(hit, panels, 0), axis=-1)

    col_super = super_of(jnp.arange(width, dtype=jnp.int32) // panel_cols)
    row_ids = row_index * row_count + jnp.arange(row_count, dtype=jnp.int32)
    row_super = super_of(row_ids // panel_cols)
    inverse = jnp.where(
        row_super[:, None] == col_super[None, :], diag_inverse[0, 0], jnp.zeros((), jnp.bfloat16)
    )
    tile_supernode = super_of(offdiag_block_panel[0, 0])
    tiles_used = jnp.where(
        col_super[None, None, :] == tile_supernode[:, None, None],
        off_tiles[0, 0],
        jnp.zeros((), jnp.bfloat16),
    ).reshape(tile_count * block_rows, width)

    raw = jnp.concatenate(
        [diag_inverse[0, 0], off_tiles[0, 0].reshape(tile_count * block_rows, width)], axis=0
    )
    gathered = lax.all_gather(raw, "prow", axis=0)
    zero = jnp.zeros((), jnp.bfloat16)
    inv_full = jnp.where(
        col_super[:, None] == col_super[None, :],
        gathered[:, :row_count].reshape(n_prow * row_count, width),
        zero,
    )

    all_axes = ("lvl", "prow", "pcol")

    def level0_shift(x, shift):
        pairs = [
            (p * n_pcol + c, ((p + shift) % n_prow) * n_pcol + c)
            for p in range(n_prow)
            for c in range(n_pcol)
        ]
        return lax.ppermute(x, all_axes, pairs)

    def by_source(chunks):
        stacked = jnp.stack(chunks)
        order = (row_index - jnp.arange(n_prow, dtype=jnp.int32)) % n_prow
        return jnp.take(stacked, order, axis=0, mode="clip")

    rows_out = width // n_prow
    first_rows = jnp.dot(
        inverse, rhs[0, 0].astype(jnp.bfloat16), preferred_element_type=jnp.float32
    )
    first_half = first_rows.astype(jnp.bfloat16)
    first_all = by_source(
        [first_half] + [level0_shift(first_half, k) for k in range(1, n_prow)]
    ).reshape(width, columns_all)
    first_updates = jnp.dot(
        tiles_used, first_all, preferred_element_type=jnp.float32
    ).astype(jnp.bfloat16)

    def column_block(k):
        start = ((row_index + k) % n_prow) * cols
        return lax.dynamic_slice_in_dim(first_updates, start, cols, axis=1)

    first_cols = by_source(
        [column_block(0)] + [level0_shift(column_block(k), k) for k in range(1, n_prow)]
    ).reshape(group_tiles * block_rows, cols)
    first_cols = jnp.concatenate(
        [first_cols, jnp.zeros((block_rows, cols), jnp.bfloat16)], axis=0
    )

    meta = jnp.stack([off_device[0, 0], off_block[0, 0], offdiag_block_panel[0, 0]], axis=0)
    devices = n_lvl * n_prow * n_pcol
    meta = lax.all_to_all(
        jnp.broadcast_to(meta[None], (devices,) + meta.shape),
        ("lvl", "prow", "pcol"),
        split_axis=0,
        concat_axis=0,
        tiled=True,
    )
    meta = meta.reshape(n_lvl, n_prow, n_pcol, 3, tile_count)
    meta = jnp.transpose(meta, (0, 2, 1, 3, 4)).reshape(groups, n_prow, 3, tile_count)
    target = meta[:, :, 0, :].reshape(groups, group_tiles)
    group_panels = jnp.take(meta[:, :, 2, :].reshape(groups, group_tiles), my_group, axis=0)
    tiles_full = jnp.where(
        col_super[None, None, :] == super_of(group_panels)[:, None, None],
        gathered[:, row_count:].reshape(group_tiles, block_rows, width),
        zero,
    ).reshape(group_tiles * block_rows, width)
    tiles_full = jnp.concatenate(
        [tiles_full, jnp.zeros((block_rows, width), jnp.bfloat16)], axis=0
    )
    block = meta[:, :, 1, :].reshape(groups, group_tiles)
    tile_ids = jnp.arange(group_tiles, dtype=jnp.int32)
    source_row = tile_ids // tile_count
    earlier = (
        (target[:, :, None] == target[:, None, :])
        & (source_row[:, None] == source_row[None, :])[None]
        & (tile_ids[:, None] > tile_ids[None, :])[None]
    )
    position = jnp.sum(earlier.astype(jnp.int32), axis=2)
    local_slot = source_row[None, :] * CAP + position

    my_target = jnp.take(target, my_group, axis=0)
    my_slot = my_target * slots + jnp.take(local_slot, my_group, axis=0)
    send_match = my_slot[None, :] == jnp.arange(groups * slots, dtype=jnp.int32)[:, None]
    send_index = jnp.where(
        jnp.any(send_match, axis=1),
        jnp.sum(jnp.where(send_match, tile_ids[None, :], 0), axis=1),
        group_tiles,
    )

    to_me = target == my_group
    slot_ids = jnp.arange(slots, dtype=jnp.int32)
    pick = to_me[:, None, :] & (local_slot[:, None, :] == slot_ids[None, :, None])
    recv_block = jnp.where(
        jnp.any(pick, axis=2), jnp.sum(jnp.where(pick, block[:, None, :], 0), axis=2), NT
    )
    recv_block = recv_block.reshape(n_lvl, n_pcol * slots)

    rhs_cols = lax.dynamic_slice_in_dim(rhs[0, 0], row_index * cols, cols, axis=1)
    window_blocks = width // block_rows
    acc = jnp.zeros((NT + 1, block_rows, cols), jnp.float32)
    halves = []
    for section in range(n_lvl):
        if section == 0:
            updates = first_cols
        else:
            right = rhs_cols - acc[:window_blocks].reshape(width, cols)
            solved_now = jnp.dot(
                inv_full, right.astype(jnp.bfloat16), preferred_element_type=jnp.float32
            )
            halves.append(solved_now.astype(jnp.bfloat16))
            updates = jnp.dot(
                tiles_full, solved_now.astype(jnp.bfloat16), preferred_element_type=jnp.float32
            ).astype(jnp.bfloat16)
        updates = updates.reshape(group_tiles + 1, block_rows, cols)
        sending = jnp.take(updates, send_index, axis=0, mode="clip")
        incoming = lax.all_to_all(
            sending, ("lvl", "pcol"), split_axis=0, concat_axis=0, tiled=True
        )
        incoming = incoming.reshape(n_lvl, n_pcol * slots, block_rows, cols)[section]
        acc = acc.at[recv_block[section]].add(incoming.astype(jnp.float32), mode="clip")
    outer = acc[window_blocks:NT].reshape(ABOVE, cols)

    solved = halves[-1]
    for section in range(n_lvl - 2, 0, -1):
        solved = jnp.where(level_index == section, halves[section - 1], solved)
    solved_blocks = solved.reshape(n_prow, rows_out, cols)
    final = jnp.concatenate(
        [
            solved_blocks.astype(jnp.bfloat16),
            jnp.broadcast_to(outer.astype(jnp.bfloat16)[None], (n_prow, ABOVE, cols)),
        ],
        axis=1,
    )
    final = lax.all_to_all(final, "prow", split_axis=0, concat_axis=0, tiled=True)
    final = final.astype(jnp.float32)
    solution_rows = jnp.transpose(final[:, :rows_out], (1, 0, 2)).reshape(rows_out, columns_all)
    solution_rows = jnp.where(level_index == 0, first_rows, solution_rows)
    outer_all = jnp.transpose(final[:, rows_out:], (1, 0, 2)).reshape(ABOVE, columns_all)
    return (solution_rows[None, None], outer_all[None, None])


def solution(mesh):
    placed = (
        P("lvl", "pcol", None, None),
        P("lvl", "pcol", "prow", None),
        P("lvl", "pcol", "prow", None, None),
        P("lvl", "pcol", None),
        P("lvl", "pcol", "prow"),
        P("lvl", "pcol", "prow"),
        P("lvl", "pcol", "prow"),
    )
    return jax.shard_map(
        per_device,
        mesh=mesh,
        in_specs=placed,
        out_specs=(P("lvl", "pcol", "prow", None), P("lvl", "pcol", None, None)),
        check_vma=False,
    )
```

```python
import jax
import jax.numpy as jnp
from jax import lax
from jax.sharding import PartitionSpec as P

CAP = 2
ABOVE = 512
NT = 48


def per_device(
    rhs, diag_inverse, off_tiles, panel_super, off_device, off_block, offdiag_block_panel
):
    n_lvl = lax.axis_size("lvl")
    n_pcol = lax.axis_size("pcol")
    n_prow = lax.axis_size("prow")
    groups = n_lvl * n_pcol
    level_index = lax.axis_index("lvl")
    row_index = lax.axis_index("prow")
    col_index = lax.axis_index("pcol")
    my_group = level_index * n_pcol + col_index
    width = rhs.shape[2]
    columns_all = rhs.shape[3]
    cols = columns_all // n_prow
    row_count = diag_inverse.shape[2]
    tile_count = off_tiles.shape[2]
    block_rows = off_tiles.shape[3]
    group_tiles = n_prow * tile_count
    slots = n_prow * CAP

    panels = panel_super[0, 0]
    panel_count = panels.shape[0]
    panel_cols = width // panel_count
    panel_ids = jnp.arange(panel_count, dtype=jnp.int32)

    def super_of(panel):
        hit = panel[..., None] == panel_ids
        return jnp.sum(jnp.where(hit, panels, 0), axis=-1)

    col_super = super_of(jnp.arange(width, dtype=jnp.int32) // panel_cols)
    row_ids = row_index * row_count + jnp.arange(row_count, dtype=jnp.int32)
    row_super = super_of(row_ids // panel_cols)
    inverse = jnp.where(
        row_super[:, None] == col_super[None, :], diag_inverse[0, 0], jnp.zeros((), jnp.bfloat16)
    )
    tile_supernode = super_of(offdiag_block_panel[0, 0])
    tiles_used = jnp.where(
        col_super[None, None, :] == tile_supernode[:, None, None],
        off_tiles[0, 0],
        jnp.zeros((), jnp.bfloat16),
    ).reshape(tile_count * block_rows, width)

    raw = jnp.concatenate(
        [diag_inverse[0, 0], off_tiles[0, 0].reshape(tile_count * block_rows, width)], axis=0
    )
    gathered = lax.all_gather(raw, "prow", axis=0)
    zero = jnp.zeros((), jnp.bfloat16)
    inv_full = jnp.where(
        col_super[:, None] == col_super[None, :],
        gathered[:, :row_count].reshape(n_prow * row_count, width),
        zero,
    )

    all_axes = ("lvl", "prow", "pcol")

    def level0_shift(x, shift):
        pairs = [
            (p * n_pcol + c, ((p + shift) % n_prow) * n_pcol + c)
            for p in range(n_prow)
            for c in range(n_pcol)
        ]
        return lax.ppermute(x, all_axes, pairs)

    def by_source(chunks):
        stacked = jnp.stack(chunks)
        order = (row_index - jnp.arange(n_prow, dtype=jnp.int32)) % n_prow
        return jnp.take(stacked, order, axis=0, mode="clip")

    rows_out = width // n_prow
    first_rows = jnp.dot(
        inverse, rhs[0, 0].astype(jnp.bfloat16), preferred_element_type=jnp.float32
    )
    first_half = first_rows.astype(jnp.bfloat16)
    first_all = by_source(
        [first_half] + [level0_shift(first_half, k) for k in range(1, n_prow)]
    ).reshape(width, columns_all)
    first_updates = jnp.dot(
        tiles_used, first_all, preferred_element_type=jnp.float32
    ).astype(jnp.bfloat16)

    def column_block(k):
        start = ((row_index + k) % n_prow) * cols
        return lax.dynamic_slice_in_dim(first_updates, start, cols, axis=1)

    first_cols = by_source(
        [column_block(0)] + [level0_shift(column_block(k), k) for k in range(1, n_prow)]
    ).reshape(group_tiles * block_rows, cols)
    first_cols = jnp.concatenate(
        [first_cols, jnp.zeros((block_rows, cols), jnp.bfloat16)], axis=0
    )

    meta = jnp.stack([off_device[0, 0], off_block[0, 0], offdiag_block_panel[0, 0]], axis=0)
    meta = lax.all_gather(meta, ("lvl", "prow", "pcol"), axis=0)
    meta = meta.reshape(n_lvl, n_prow, n_pcol, 3, tile_count)
    meta = jnp.transpose(meta, (0, 2, 1, 3, 4)).reshape(groups, n_prow, 3, tile_count)
    target = meta[:, :, 0, :].reshape(groups, group_tiles)
    group_panels = jnp.take(meta[:, :, 2, :].reshape(groups, group_tiles), my_group, axis=0)
    tiles_full = jnp.where(
        col_super[None, None, :] == super_of(group_panels)[:, None, None],
        gathered[:, row_count:].reshape(group_tiles, block_rows, width),
        zero,
    ).reshape(group_tiles * block_rows, width)
    tiles_full = jnp.concatenate(
        [tiles_full, jnp.zeros((block_rows, width), jnp.bfloat16)], axis=0
    )
    block = meta[:, :, 1, :].reshape(groups, group_tiles)
    tile_ids = jnp.arange(group_tiles, dtype=jnp.int32)
    source_row = tile_ids // tile_count
    earlier = (
        (target[:, :, None] == target[:, None, :])
        & (source_row[:, None] == source_row[None, :])[None]
        & (tile_ids[:, None] > tile_ids[None, :])[None]
    )
    position = jnp.sum(earlier.astype(jnp.int32), axis=2)
    local_slot = source_row[None, :] * CAP + position

    my_target = jnp.take(target, my_group, axis=0)
    my_slot = my_target * slots + jnp.take(local_slot, my_group, axis=0)
    send_match = my_slot[None, :] == jnp.arange(groups * slots, dtype=jnp.int32)[:, None]
    send_index = jnp.where(
        jnp.any(send_match, axis=1),
        jnp.sum(jnp.where(send_match, tile_ids[None, :], 0), axis=1),
        group_tiles,
    )

    to_me = target == my_group
    slot_ids = jnp.arange(slots, dtype=jnp.int32)
    pick = to_me[:, None, :] & (local_slot[:, None, :] == slot_ids[None, :, None])
    recv_block = jnp.where(
        jnp.any(pick, axis=2), jnp.sum(jnp.where(pick, block[:, None, :], 0), axis=2), NT
    )
    recv_block = recv_block.reshape(n_lvl, n_pcol * slots)

    rhs_cols = lax.dynamic_slice_in_dim(rhs[0, 0], row_index * cols, cols, axis=1)
    window_blocks = width // block_rows
    acc = jnp.zeros((NT + 1, block_rows, cols), jnp.float32)
    solved = jnp.zeros((width, cols), jnp.float32)
    for section in range(n_lvl):
        if section == 0:
            updates = first_cols
        else:
            right = rhs_cols - acc[:window_blocks].reshape(width, cols)
            solved_now = jnp.dot(
                inv_full, right.astype(jnp.bfloat16), preferred_element_type=jnp.float32
            )
            solved = jnp.where(level_index == section, solved_now, solved)
            updates = jnp.dot(
                tiles_full, solved_now.astype(jnp.bfloat16), preferred_element_type=jnp.float32
            ).astype(jnp.bfloat16)
        updates = updates.reshape(group_tiles + 1, block_rows, cols)
        sending = jnp.take(updates, send_index, axis=0, mode="clip")
        incoming = lax.all_to_all(
            sending, ("lvl", "pcol"), split_axis=0, concat_axis=0, tiled=True
        )
        incoming = incoming.reshape(n_lvl, n_pcol * slots, block_rows, cols)[section]
        acc = acc.at[recv_block[section]].add(incoming.astype(jnp.float32), mode="clip")
    outer = acc[window_blocks:NT].reshape(ABOVE, cols)

    solved_blocks = solved.reshape(n_prow, rows_out, cols)
    final = jnp.concatenate(
        [
            solved_blocks.astype(jnp.bfloat16),
            jnp.broadcast_to(outer.astype(jnp.bfloat16)[None], (n_prow, ABOVE, cols)),
        ],
        axis=1,
    )
    final = lax.all_to_all(final, "prow", split_axis=0, concat_axis=0, tiled=True)
    final = final.astype(jnp.float32)
    solution_rows = jnp.transpose(final[:, :rows_out], (1, 0, 2)).reshape(rows_out, columns_all)
    solution_rows = jnp.where(level_index == 0, first_rows, solution_rows)
    outer_all = jnp.transpose(final[:, rows_out:], (1, 0, 2)).reshape(ABOVE, columns_all)
    return (solution_rows[None, None], outer_all[None, None])


def solution(mesh):
    placed = (
        P("lvl", "pcol", None, None),
        P("lvl", "pcol", "prow", None),
        P("lvl", "pcol", "prow", None, None),
        P("lvl", "pcol", None),
        P("lvl", "pcol", "prow"),
        P("lvl", "pcol", "prow"),
        P("lvl", "pcol", "prow"),
    )
    return jax.shard_map(
        per_device,
        mesh=mesh,
        in_specs=placed,
        out_specs=(P("lvl", "pcol", "prow", None), P("lvl", "pcol", None, None)),
        check_vma=False,
    )
```

```python
import jax
import jax.numpy as jnp
from jax import lax
from jax.sharding import PartitionSpec as P

CAP = 2
ABOVE = 512
NT = 48


def per_device(
    rhs, diag_inverse, off_tiles, panel_super, off_device, off_block, offdiag_block_panel
):
    n_lvl = lax.axis_size("lvl")
    n_pcol = lax.axis_size("pcol")
    n_prow = lax.axis_size("prow")
    groups = n_lvl * n_pcol
    level_index = lax.axis_index("lvl")
    row_index = lax.axis_index("prow")
    col_index = lax.axis_index("pcol")
    my_group = level_index * n_pcol + col_index
    width = rhs.shape[2]
    columns_all = rhs.shape[3]
    cols = columns_all // n_prow
    row_count = diag_inverse.shape[2]
    tile_count = off_tiles.shape[2]
    block_rows = off_tiles.shape[3]
    group_tiles = n_prow * tile_count
    slots = n_prow * CAP

    panels = panel_super[0, 0]
    panel_count = panels.shape[0]
    panel_cols = width // panel_count
    panel_ids = jnp.arange(panel_count, dtype=jnp.int32)

    def super_of(panel):
        hit = panel[..., None] == panel_ids
        return jnp.sum(jnp.where(hit, panels, 0), axis=-1)

    col_super = super_of(jnp.arange(width, dtype=jnp.int32) // panel_cols)
    row_ids = row_index * row_count + jnp.arange(row_count, dtype=jnp.int32)
    row_super = super_of(row_ids // panel_cols)
    inverse = jnp.where(
        row_super[:, None] == col_super[None, :], diag_inverse[0, 0], jnp.zeros((), jnp.bfloat16)
    )
    tile_supernode = super_of(offdiag_block_panel[0, 0])
    tiles_used = jnp.where(
        col_super[None, None, :] == tile_supernode[:, None, None],
        off_tiles[0, 0],
        jnp.zeros((), jnp.bfloat16),
    ).reshape(tile_count * block_rows, width)

    raw = jnp.concatenate(
        [diag_inverse[0, 0], off_tiles[0, 0].reshape(tile_count * block_rows, width)], axis=0
    )
    gathered = lax.all_gather(raw, "prow", axis=0)
    zero = jnp.zeros((), jnp.bfloat16)
    inv_full = jnp.where(
        col_super[:, None] == col_super[None, :],
        gathered[:, :row_count].reshape(n_prow * row_count, width),
        zero,
    )

    all_axes = ("lvl", "prow", "pcol")

    def level0_shift(x, shift):
        pairs = [
            (p * n_pcol + c, ((p + shift) % n_prow) * n_pcol + c)
            for p in range(n_prow)
            for c in range(n_pcol)
        ]
        return lax.ppermute(x, all_axes, pairs)

    def by_source(chunks):
        stacked = jnp.stack(chunks)
        order = (row_index - jnp.arange(n_prow, dtype=jnp.int32)) % n_prow
        return jnp.take(stacked, order, axis=0, mode="clip")

    rows_out = width // n_prow
    first_rows = jnp.dot(
        inverse, rhs[0, 0].astype(jnp.bfloat16), preferred_element_type=jnp.float32
    )
    first_half = first_rows.astype(jnp.bfloat16)
    first_all = by_source(
        [first_half] + [level0_shift(first_half, k) for k in range(1, n_prow)]
    ).reshape(width, columns_all)
    first_updates = jnp.dot(
        tiles_used, first_all, preferred_element_type=jnp.float32
    ).astype(jnp.bfloat16)

    def column_block(k):
        start = ((row_index + k) % n_prow) * cols
        return lax.dynamic_slice_in_dim(first_updates, start, cols, axis=1)

    first_cols = by_source(
        [column_block(0)] + [level0_shift(column_block(k), k) for k in range(1, n_prow)]
    ).reshape(group_tiles * block_rows, cols)
    first_cols = jnp.concatenate(
        [first_cols, jnp.zeros((block_rows, cols), jnp.bfloat16)], axis=0
    )

    meta = jnp.stack([off_device[0, 0], off_block[0, 0], offdiag_block_panel[0, 0]], axis=0)
    devices = n_lvl * n_prow * n_pcol
    meta = lax.all_to_all(
        jnp.broadcast_to(meta[None], (devices,) + meta.shape),
        ("lvl", "prow", "pcol"),
        split_axis=0,
        concat_axis=0,
        tiled=True,
    )
    meta = meta.reshape(n_lvl, n_prow, n_pcol, 3, tile_count)
    meta = jnp.transpose(meta, (0, 2, 1, 3, 4)).reshape(groups, n_prow, 3, tile_count)
    target = meta[:, :, 0, :].reshape(groups, group_tiles)
    group_panels = jnp.take(meta[:, :, 2, :].reshape(groups, group_tiles), my_group, axis=0)
    tiles_full = jnp.where(
        col_super[None, None, :] == super_of(group_panels)[:, None, None],
        gathered[:, row_count:].reshape(group_tiles, block_rows, width),
        zero,
    ).reshape(group_tiles * block_rows, width)
    tiles_full = jnp.concatenate(
        [tiles_full, jnp.zeros((block_rows, width), jnp.bfloat16)], axis=0
    )
    block = meta[:, :, 1, :].reshape(groups, group_tiles)
    tile_ids = jnp.arange(group_tiles, dtype=jnp.int32)
    source_row = tile_ids // tile_count
    earlier = (
        (target[:, :, None] == target[:, None, :])
        & (source_row[:, None] == source_row[None, :])[None]
        & (tile_ids[:, None] > tile_ids[None, :])[None]
    )
    position = jnp.sum(earlier.astype(jnp.int32), axis=2)
    local_slot = source_row[None, :] * CAP + position

    my_target = jnp.take(target, my_group, axis=0)
    my_slot = my_target * slots + jnp.take(local_slot, my_group, axis=0)
    send_match = my_slot[None, :] == jnp.arange(groups * slots, dtype=jnp.int32)[:, None]
    send_index = jnp.where(
        jnp.any(send_match, axis=1),
        jnp.sum(jnp.where(send_match, tile_ids[None, :], 0), axis=1),
        group_tiles,
    )

    to_me = target == my_group
    slot_ids = jnp.arange(slots, dtype=jnp.int32)
    pick = to_me[:, None, :] & (local_slot[:, None, :] == slot_ids[None, :, None])
    recv_block = jnp.where(
        jnp.any(pick, axis=2), jnp.sum(jnp.where(pick, block[:, None, :], 0), axis=2), NT
    )
    recv_block = recv_block.reshape(n_lvl, n_pcol * slots)

    rhs_cols = lax.dynamic_slice_in_dim(rhs[0, 0], row_index * cols, cols, axis=1)
    window_blocks = width // block_rows
    acc = jnp.zeros((NT + 1, block_rows, cols), jnp.float32)
    solved = jnp.zeros((width, cols), jnp.float32)
    for section in range(n_lvl):
        if section == 0:
            updates = first_cols
        else:
            right = rhs_cols - acc[:window_blocks].reshape(width, cols)
            solved_now = jnp.dot(
                inv_full, right.astype(jnp.bfloat16), preferred_element_type=jnp.float32
            )
            solved = jnp.where(level_index == section, solved_now, solved)
            updates = jnp.dot(
                tiles_full, solved_now.astype(jnp.bfloat16), preferred_element_type=jnp.float32
            ).astype(jnp.bfloat16)
        updates = updates.reshape(group_tiles + 1, block_rows, cols)
        sending = updates.at[send_index].get(mode="promise_in_bounds")
        incoming = lax.all_to_all(
            sending, ("lvl", "pcol"), split_axis=0, concat_axis=0, tiled=True
        )
        incoming = incoming.reshape(n_lvl, n_pcol * slots, block_rows, cols)[section]
        acc = acc.at[recv_block[section]].add(incoming.astype(jnp.float32), mode="promise_in_bounds")
    outer = acc[window_blocks:NT].reshape(ABOVE, cols)

    solved_blocks = solved.reshape(n_prow, rows_out, cols)
    final = jnp.concatenate(
        [
            solved_blocks.astype(jnp.bfloat16),
            jnp.broadcast_to(outer.astype(jnp.bfloat16)[None], (n_prow, ABOVE, cols)),
        ],
        axis=1,
    )
    final = lax.all_to_all(final, "prow", split_axis=0, concat_axis=0, tiled=True)
    final = final.astype(jnp.float32)
    solution_rows = jnp.transpose(final[:, :rows_out], (1, 0, 2)).reshape(rows_out, columns_all)
    solution_rows = jnp.where(level_index == 0, first_rows, solution_rows)
    outer_all = jnp.transpose(final[:, rows_out:], (1, 0, 2)).reshape(ABOVE, columns_all)
    return (solution_rows[None, None], outer_all[None, None])


def solution(mesh):
    placed = (
        P("lvl", "pcol", None, None),
        P("lvl", "pcol", "prow", None),
        P("lvl", "pcol", "prow", None, None),
        P("lvl", "pcol", None),
        P("lvl", "pcol", "prow"),
        P("lvl", "pcol", "prow"),
        P("lvl", "pcol", "prow"),
    )
    return jax.shard_map(
        per_device,
        mesh=mesh,
        in_specs=placed,
        out_specs=(P("lvl", "pcol", "prow", None), P("lvl", "pcol", None, None)),
        check_vma=False,
    )
```

```python
import jax
import jax.numpy as jnp
from jax import lax
from jax.sharding import PartitionSpec as P

CAP = 2
ABOVE = 512
NT = 48


def per_device(
    rhs, diag_inverse, off_tiles, panel_super, off_device, off_block, offdiag_block_panel
):
    n_lvl = lax.axis_size("lvl")
    n_pcol = lax.axis_size("pcol")
    n_prow = lax.axis_size("prow")
    groups = n_lvl * n_pcol
    level_index = lax.axis_index("lvl")
    row_index = lax.axis_index("prow")
    col_index = lax.axis_index("pcol")
    my_group = level_index * n_pcol + col_index
    width = rhs.shape[2]
    columns_all = rhs.shape[3]
    cols = columns_all // n_prow
    row_count = diag_inverse.shape[2]
    tile_count = off_tiles.shape[2]
    block_rows = off_tiles.shape[3]
    group_tiles = n_prow * tile_count
    slots = n_prow * CAP

    panels = panel_super[0, 0]
    panel_count = panels.shape[0]
    panel_cols = width // panel_count
    panel_ids = jnp.arange(panel_count, dtype=jnp.int32)

    def super_of(panel):
        hit = panel[..., None] == panel_ids
        return jnp.sum(jnp.where(hit, panels, 0), axis=-1)

    col_super = super_of(jnp.arange(width, dtype=jnp.int32) // panel_cols)
    row_ids = row_index * row_count + jnp.arange(row_count, dtype=jnp.int32)
    row_super = super_of(row_ids // panel_cols)
    inverse = jnp.where(
        row_super[:, None] == col_super[None, :], diag_inverse[0, 0], jnp.zeros((), jnp.bfloat16)
    )
    tile_supernode = super_of(offdiag_block_panel[0, 0])
    tiles_used = jnp.where(
        col_super[None, None, :] == tile_supernode[:, None, None],
        off_tiles[0, 0],
        jnp.zeros((), jnp.bfloat16),
    ).reshape(tile_count * block_rows, width)

    raw = jnp.concatenate(
        [diag_inverse[0, 0], off_tiles[0, 0].reshape(tile_count * block_rows, width)], axis=0
    )
    gathered = lax.all_gather(raw, "prow", axis=0)
    zero = jnp.zeros((), jnp.bfloat16)
    inv_full = jnp.where(
        col_super[:, None] == col_super[None, :],
        gathered[:, :row_count].reshape(n_prow * row_count, width),
        zero,
    )

    all_axes = ("lvl", "prow", "pcol")

    def level0_shift(x, shift):
        pairs = [
            (p * n_pcol + c, ((p + shift) % n_prow) * n_pcol + c)
            for p in range(n_prow)
            for c in range(n_pcol)
        ]
        return lax.ppermute(x, all_axes, pairs)

    def by_source(chunks):
        stacked = jnp.stack(chunks)
        order = (row_index - jnp.arange(n_prow, dtype=jnp.int32)) % n_prow
        return jnp.take(stacked, order, axis=0, mode="clip")

    rows_out = width // n_prow
    first_rows = jnp.dot(
        inverse, rhs[0, 0].astype(jnp.bfloat16), preferred_element_type=jnp.float32
    )
    first_half = first_rows.astype(jnp.bfloat16)
    first_all = by_source(
        [first_half] + [level0_shift(first_half, k) for k in range(1, n_prow)]
    ).reshape(width, columns_all)
    first_updates = jnp.dot(
        tiles_used, first_all, preferred_element_type=jnp.float32
    ).astype(jnp.bfloat16)

    def column_block(k):
        start = ((row_index + k) % n_prow) * cols
        return lax.dynamic_slice_in_dim(first_updates, start, cols, axis=1)

    first_cols = by_source(
        [column_block(0)] + [level0_shift(column_block(k), k) for k in range(1, n_prow)]
    ).reshape(group_tiles * block_rows, cols)
    first_cols = jnp.concatenate(
        [first_cols, jnp.zeros((block_rows, cols), jnp.bfloat16)], axis=0
    )

    meta = jnp.stack([off_device[0, 0], off_block[0, 0], offdiag_block_panel[0, 0]], axis=0)
    devices = n_lvl * n_prow * n_pcol
    meta = lax.all_to_all(
        jnp.broadcast_to(meta[None], (devices,) + meta.shape),
        ("lvl", "prow", "pcol"),
        split_axis=0,
        concat_axis=0,
        tiled=True,
    )
    meta = meta.reshape(n_lvl, n_prow, n_pcol, 3, tile_count)
    meta = jnp.transpose(meta, (0, 2, 1, 3, 4)).reshape(groups, n_prow, 3, tile_count)
    target = meta[:, :, 0, :].reshape(groups, group_tiles)
    group_panels = jnp.take(meta[:, :, 2, :].reshape(groups, group_tiles), my_group, axis=0)
    tiles_full = jnp.where(
        col_super[None, None, :] == super_of(group_panels)[:, None, None],
        gathered[:, row_count:].reshape(group_tiles, block_rows, width),
        zero,
    ).reshape(group_tiles * block_rows, width)
    tiles_full = jnp.concatenate(
        [tiles_full, jnp.zeros((block_rows, width), jnp.bfloat16)], axis=0
    )
    block = meta[:, :, 1, :].reshape(groups, group_tiles)
    tile_ids = jnp.arange(group_tiles, dtype=jnp.int32)
    source_row = tile_ids // tile_count
    earlier = (
        (target[:, :, None] == target[:, None, :])
        & (source_row[:, None] == source_row[None, :])[None]
        & (tile_ids[:, None] > tile_ids[None, :])[None]
    )
    position = jnp.sum(earlier.astype(jnp.int32), axis=2)
    local_slot = source_row[None, :] * CAP + position

    my_target = jnp.take(target, my_group, axis=0)
    my_slot = my_target * slots + jnp.take(local_slot, my_group, axis=0)
    send_match = my_slot[None, :] == jnp.arange(groups * slots, dtype=jnp.int32)[:, None]
    send_index = jnp.where(
        jnp.any(send_match, axis=1),
        jnp.sum(jnp.where(send_match, tile_ids[None, :], 0), axis=1),
        group_tiles,
    )

    to_me = target == my_group
    slot_ids = jnp.arange(slots, dtype=jnp.int32)
    pick = to_me[:, None, :] & (local_slot[:, None, :] == slot_ids[None, :, None])
    recv_block = jnp.where(
        jnp.any(pick, axis=2), jnp.sum(jnp.where(pick, block[:, None, :], 0), axis=2), NT
    )
    recv_block = recv_block.reshape(n_lvl, n_pcol * slots)

    rhs_cols = lax.dynamic_slice_in_dim(rhs[0, 0], row_index * cols, cols, axis=1)
    window_blocks = width // block_rows
    acc = jnp.zeros((NT + 1, block_rows, cols), jnp.float32)
    solved = jnp.zeros((width, cols), jnp.float32)
    for section in range(n_lvl):
        if section == 0:
            updates = first_cols
        else:
            right = rhs_cols - acc[:window_blocks].reshape(width, cols)
            solved_now = jnp.dot(
                inv_full, right.astype(jnp.bfloat16), preferred_element_type=jnp.float32
            )
            solved = jnp.where(level_index == section, solved_now, solved)
            updates = jnp.dot(
                tiles_full, solved_now.astype(jnp.bfloat16), preferred_element_type=jnp.float32
            ).astype(jnp.bfloat16)
        updates = updates.reshape(group_tiles + 1, block_rows // 2, 2 * cols)
        sending = jnp.take(updates, send_index, axis=0, mode="clip")
        incoming = lax.all_to_all(
            sending, ("lvl", "pcol"), split_axis=0, concat_axis=0, tiled=True
        )
        incoming = incoming.reshape(n_lvl, n_pcol * slots, block_rows // 2, 2 * cols)[section]
        incoming = incoming.reshape(n_pcol * slots, block_rows, cols)
        acc = acc.at[recv_block[section]].add(incoming.astype(jnp.float32), mode="clip")
    outer = acc[window_blocks:NT].reshape(ABOVE, cols)

    solved_blocks = solved.reshape(n_prow, rows_out, cols)
    final = jnp.concatenate(
        [
            solved_blocks.astype(jnp.bfloat16),
            jnp.broadcast_to(outer.astype(jnp.bfloat16)[None], (n_prow, ABOVE, cols)),
        ],
        axis=1,
    )
    final = lax.all_to_all(final, "prow", split_axis=0, concat_axis=0, tiled=True)
    final = final.astype(jnp.float32)
    solution_rows = jnp.transpose(final[:, :rows_out], (1, 0, 2)).reshape(rows_out, columns_all)
    solution_rows = jnp.where(level_index == 0, first_rows, solution_rows)
    outer_all = jnp.transpose(final[:, rows_out:], (1, 0, 2)).reshape(ABOVE, columns_all)
    return (solution_rows[None, None], outer_all[None, None])


def solution(mesh):
    placed = (
        P("lvl", "pcol", None, None),
        P("lvl", "pcol", "prow", None),
        P("lvl", "pcol", "prow", None, None),
        P("lvl", "pcol", None),
        P("lvl", "pcol", "prow"),
        P("lvl", "pcol", "prow"),
        P("lvl", "pcol", "prow"),
    )
    return jax.shard_map(
        per_device,
        mesh=mesh,
        in_specs=placed,
        out_specs=(P("lvl", "pcol", "prow", None), P("lvl", "pcol", None, None)),
        check_vma=False,
    )
```

```python
import jax
import jax.numpy as jnp
from jax import lax
from jax.sharding import PartitionSpec as P

CAP = 2
ABOVE = 512
NT = 48


def per_device(
    rhs, diag_inverse, off_tiles, panel_super, off_device, off_block, offdiag_block_panel
):
    n_lvl = lax.axis_size("lvl")
    n_pcol = lax.axis_size("pcol")
    n_prow = lax.axis_size("prow")
    groups = n_lvl * n_pcol
    level_index = lax.axis_index("lvl")
    row_index = lax.axis_index("prow")
    col_index = lax.axis_index("pcol")
    my_group = level_index * n_pcol + col_index
    width = rhs.shape[2]
    columns_all = rhs.shape[3]
    cols = columns_all // n_prow
    row_count = diag_inverse.shape[2]
    tile_count = off_tiles.shape[2]
    block_rows = off_tiles.shape[3]
    group_tiles = n_prow * tile_count
    slots = n_prow * CAP

    panels = panel_super[0, 0]
    panel_count = panels.shape[0]
    panel_cols = width // panel_count
    panel_ids = jnp.arange(panel_count, dtype=jnp.int32)

    def super_of(panel):
        hit = panel[..., None] == panel_ids
        return jnp.sum(jnp.where(hit, panels, 0), axis=-1)

    col_super = super_of(jnp.arange(width, dtype=jnp.int32) // panel_cols)
    row_ids = row_index * row_count + jnp.arange(row_count, dtype=jnp.int32)
    row_super = super_of(row_ids // panel_cols)
    inverse = jnp.where(
        row_super[:, None] == col_super[None, :], diag_inverse[0, 0], jnp.zeros((), jnp.bfloat16)
    )
    tile_supernode = super_of(offdiag_block_panel[0, 0])
    tiles_used = jnp.where(
        col_super[None, None, :] == tile_supernode[:, None, None],
        off_tiles[0, 0],
        jnp.zeros((), jnp.bfloat16),
    ).reshape(tile_count * block_rows, width)

    raw = jnp.concatenate(
        [diag_inverse[0, 0], off_tiles[0, 0].reshape(tile_count * block_rows, width)], axis=0
    )
    gathered = lax.all_gather(raw, "prow", axis=0)
    zero = jnp.zeros((), jnp.bfloat16)
    inv_full = jnp.where(
        col_super[:, None] == col_super[None, :],
        gathered[:, :row_count].reshape(n_prow * row_count, width),
        zero,
    )

    all_axes = ("lvl", "prow", "pcol")

    def level0_shift(x, shift):
        pairs = [
            (p * n_pcol + c, ((p + shift) % n_prow) * n_pcol + c)
            for p in range(n_prow)
            for c in range(n_pcol)
        ]
        return lax.ppermute(x, all_axes, pairs)

    def by_source(chunks):
        stacked = jnp.stack(chunks)
        order = (row_index - jnp.arange(n_prow, dtype=jnp.int32)) % n_prow
        return jnp.take(stacked, order, axis=0, mode="clip")

    rows_out = width // n_prow
    first_rows = jnp.dot(
        inverse, rhs[0, 0].astype(jnp.bfloat16), preferred_element_type=jnp.float32
    )
    first_half = first_rows.astype(jnp.bfloat16)
    first_all = by_source(
        [first_half] + [level0_shift(first_half, k) for k in range(1, n_prow)]
    ).reshape(width, columns_all)
    first_updates = jnp.dot(
        tiles_used, first_all, preferred_element_type=jnp.float32
    ).astype(jnp.bfloat16)

    def column_block(k):
        start = ((row_index + k) % n_prow) * cols
        return lax.dynamic_slice_in_dim(first_updates, start, cols, axis=1)

    first_cols = by_source(
        [column_block(0)] + [level0_shift(column_block(k), k) for k in range(1, n_prow)]
    ).reshape(group_tiles * block_rows, cols)
    first_cols = jnp.concatenate(
        [first_cols, jnp.zeros((block_rows, cols), jnp.bfloat16)], axis=0
    )

    meta = jnp.stack([off_device[0, 0], off_block[0, 0], offdiag_block_panel[0, 0]], axis=0)
    devices = n_lvl * n_prow * n_pcol
    meta = lax.all_to_all(
        jnp.broadcast_to(meta[None], (devices,) + meta.shape),
        ("lvl", "prow", "pcol"),
        split_axis=0,
        concat_axis=0,
        tiled=True,
    )
    meta = meta.reshape(n_lvl, n_prow, n_pcol, 3, tile_count)
    meta = jnp.transpose(meta, (0, 2, 1, 3, 4)).reshape(groups, n_prow, 3, tile_count)
    target = meta[:, :, 0, :].reshape(groups, group_tiles)
    group_panels = jnp.take(meta[:, :, 2, :].reshape(groups, group_tiles), my_group, axis=0)
    tiles_full = jnp.where(
        col_super[None, None, :] == super_of(group_panels)[:, None, None],
        gathered[:, row_count:].reshape(group_tiles, block_rows, width),
        zero,
    ).reshape(group_tiles * block_rows, width)
    tiles_full = jnp.concatenate(
        [tiles_full, jnp.zeros((block_rows, width), jnp.bfloat16)], axis=0
    )
    block = meta[:, :, 1, :].reshape(groups, group_tiles)
    tile_ids = jnp.arange(group_tiles, dtype=jnp.int32)
    source_row = tile_ids // tile_count
    earlier = (
        (target[:, :, None] == target[:, None, :])
        & (source_row[:, None] == source_row[None, :])[None]
        & (tile_ids[:, None] > tile_ids[None, :])[None]
    )
    position = jnp.sum(earlier.astype(jnp.int32), axis=2)
    local_slot = source_row[None, :] * CAP + position

    my_target = jnp.take(target, my_group, axis=0)
    my_slot = my_target * slots + jnp.take(local_slot, my_group, axis=0)
    send_match = my_slot[None, :] == jnp.arange(groups * slots, dtype=jnp.int32)[:, None]
    send_index = jnp.where(
        jnp.any(send_match, axis=1),
        jnp.sum(jnp.where(send_match, tile_ids[None, :], 0), axis=1),
        group_tiles,
    )

    to_me = target == my_group
    slot_ids = jnp.arange(slots, dtype=jnp.int32)
    pick = to_me[:, None, :] & (local_slot[:, None, :] == slot_ids[None, :, None])
    recv_block = jnp.where(
        jnp.any(pick, axis=2), jnp.sum(jnp.where(pick, block[:, None, :], 0), axis=2), NT
    )
    recv_block = recv_block.reshape(n_lvl, n_pcol * slots)

    rhs_cols = lax.dynamic_slice_in_dim(rhs[0, 0], row_index * cols, cols, axis=1)
    window_blocks = width // block_rows
    acc = jnp.zeros((NT + 1, block_rows, cols), jnp.float32)
    solved = jnp.zeros((width, cols), jnp.float32)
    for section in range(n_lvl):
        if section == 0:
            updates = first_cols
        else:
            right = rhs_cols - acc[:window_blocks].reshape(width, cols)
            solved_now = jnp.dot(
                inv_full, right.astype(jnp.bfloat16), preferred_element_type=jnp.float32
            )
            solved = jnp.where(level_index == section, solved_now, solved)
            updates = jnp.dot(
                tiles_full, solved_now.astype(jnp.bfloat16), preferred_element_type=jnp.float32
            ).astype(jnp.bfloat16)
        updates = updates.reshape(group_tiles + 1, block_rows // 2, 2 * cols)
        sending = jnp.take(updates, send_index, axis=0, mode="clip")
        incoming = lax.all_to_all(
            sending, ("lvl", "pcol"), split_axis=0, concat_axis=0, tiled=True
        )
        incoming = incoming.reshape(n_lvl, n_pcol * slots, block_rows // 2, 2 * cols)[section]
        incoming = incoming.reshape(n_pcol * slots, block_rows, cols)
        acc = acc.at[recv_block[section]].add(incoming.astype(jnp.float32), mode="clip")
    outer = acc[window_blocks:NT].reshape(ABOVE, cols)

    solved_blocks = solved.reshape(n_prow, rows_out, cols)
    final = jnp.concatenate(
        [
            solved_blocks.astype(jnp.bfloat16),
            jnp.broadcast_to(outer.astype(jnp.bfloat16)[None], (n_prow, ABOVE, cols)),
        ],
        axis=1,
    )
    final_shape = final.shape
    final = lax.all_to_all(
        final.reshape(n_prow, final_shape[1] // 2, 2 * cols),
        "prow",
        split_axis=0,
        concat_axis=0,
        tiled=True,
    ).reshape(final_shape)
    final = final.astype(jnp.float32)
    solution_rows = jnp.transpose(final[:, :rows_out], (1, 0, 2)).reshape(rows_out, columns_all)
    solution_rows = jnp.where(level_index == 0, first_rows, solution_rows)
    outer_all = jnp.transpose(final[:, rows_out:], (1, 0, 2)).reshape(ABOVE, columns_all)
    return (solution_rows[None, None], outer_all[None, None])


def solution(mesh):
    placed = (
        P("lvl", "pcol", None, None),
        P("lvl", "pcol", "prow", None),
        P("lvl", "pcol", "prow", None, None),
        P("lvl", "pcol", None),
        P("lvl", "pcol", "prow"),
        P("lvl", "pcol", "prow"),
        P("lvl", "pcol", "prow"),
    )
    return jax.shard_map(
        per_device,
        mesh=mesh,
        in_specs=placed,
        out_specs=(P("lvl", "pcol", "prow", None), P("lvl", "pcol", None, None)),
        check_vma=False,
    )
```

```python
import jax
import jax.numpy as jnp
from jax import lax
from jax.sharding import PartitionSpec as P

CAP = 2
ABOVE = 512
NT = 48


def per_device(
    rhs, diag_inverse, off_tiles, panel_super, off_device, off_block, offdiag_block_panel
):
    n_lvl = lax.axis_size("lvl")
    n_pcol = lax.axis_size("pcol")
    n_prow = lax.axis_size("prow")
    groups = n_lvl * n_pcol
    level_index = lax.axis_index("lvl")
    row_index = lax.axis_index("prow")
    col_index = lax.axis_index("pcol")
    my_group = level_index * n_pcol + col_index
    width = rhs.shape[2]
    columns_all = rhs.shape[3]
    cols = columns_all // n_prow
    row_count = diag_inverse.shape[2]
    tile_count = off_tiles.shape[2]
    block_rows = off_tiles.shape[3]
    group_tiles = n_prow * tile_count
    slots = n_prow * CAP

    panels = panel_super[0, 0]
    panel_count = panels.shape[0]
    panel_cols = width // panel_count
    panel_ids = jnp.arange(panel_count, dtype=jnp.int32)

    def super_of(panel):
        hit = panel[..., None] == panel_ids
        return jnp.sum(jnp.where(hit, panels, 0), axis=-1)

    col_super = super_of(jnp.arange(width, dtype=jnp.int32) // panel_cols)
    row_ids = row_index * row_count + jnp.arange(row_count, dtype=jnp.int32)
    row_super = super_of(row_ids // panel_cols)
    inverse = jnp.where(
        row_super[:, None] == col_super[None, :], diag_inverse[0, 0], jnp.zeros((), jnp.bfloat16)
    )
    tile_supernode = super_of(offdiag_block_panel[0, 0])
    tiles_used = jnp.where(
        col_super[None, None, :] == tile_supernode[:, None, None],
        off_tiles[0, 0],
        jnp.zeros((), jnp.bfloat16),
    ).reshape(tile_count * block_rows, width)

    raw = jnp.concatenate(
        [diag_inverse[0, 0], off_tiles[0, 0].reshape(tile_count * block_rows, width)], axis=0
    )
    gathered = lax.all_gather(raw, "prow", axis=0)
    zero = jnp.zeros((), jnp.bfloat16)
    inv_full = jnp.where(
        col_super[:, None] == col_super[None, :],
        gathered[:, :row_count].reshape(n_prow * row_count, width),
        zero,
    )

    all_axes = ("lvl", "prow", "pcol")

    def level0_shift(x, shift):
        pairs = [
            (p * n_pcol + c, ((p + shift) % n_prow) * n_pcol + c)
            for p in range(n_prow)
            for c in range(n_pcol)
        ]
        return lax.ppermute(x, all_axes, pairs)

    def by_source(chunks):
        stacked = jnp.stack(chunks)
        order = (row_index - jnp.arange(n_prow, dtype=jnp.int32)) % n_prow
        return jnp.take(stacked, order, axis=0, mode="clip")

    rows_out = width // n_prow
    first_rows = jnp.dot(
        inverse, rhs[0, 0].astype(jnp.bfloat16), preferred_element_type=jnp.float32
    )
    first_half = first_rows.astype(jnp.bfloat16)
    first_all = by_source(
        [first_half] + [level0_shift(first_half, k) for k in range(1, n_prow)]
    ).reshape(width, columns_all)
    first_updates = jnp.dot(
        tiles_used, first_all, preferred_element_type=jnp.float32
    ).astype(jnp.bfloat16)

    def column_block(k):
        start = ((row_index + k) % n_prow) * cols
        return lax.dynamic_slice_in_dim(first_updates, start, cols, axis=1)

    first_cols = by_source(
        [column_block(0)] + [level0_shift(column_block(k), k) for k in range(1, n_prow)]
    ).reshape(group_tiles * block_rows, cols)
    first_cols = jnp.concatenate(
        [first_cols, jnp.zeros((block_rows, cols), jnp.bfloat16)], axis=0
    )

    meta = jnp.stack([off_device[0, 0], off_block[0, 0], offdiag_block_panel[0, 0]], axis=0)
    devices = n_lvl * n_prow * n_pcol
    meta = lax.all_to_all(
        jnp.broadcast_to(meta[None], (devices,) + meta.shape),
        ("lvl", "prow", "pcol"),
        split_axis=0,
        concat_axis=0,
        tiled=True,
    )
    meta = meta.reshape(n_lvl, n_prow, n_pcol, 3, tile_count)
    meta = jnp.transpose(meta, (0, 2, 1, 3, 4)).reshape(groups, n_prow, 3, tile_count)
    target = meta[:, :, 0, :].reshape(groups, group_tiles)
    group_panels = jnp.take(meta[:, :, 2, :].reshape(groups, group_tiles), my_group, axis=0)
    tiles_full = jnp.where(
        col_super[None, None, :] == super_of(group_panels)[:, None, None],
        gathered[:, row_count:].reshape(group_tiles, block_rows, width),
        zero,
    ).reshape(group_tiles * block_rows, width)
    tiles_full = jnp.concatenate(
        [tiles_full, jnp.zeros((block_rows, width), jnp.bfloat16)], axis=0
    )
    block = meta[:, :, 1, :].reshape(groups, group_tiles)
    tile_ids = jnp.arange(group_tiles, dtype=jnp.int32)
    source_row = tile_ids // tile_count
    earlier = (
        (target[:, :, None] == target[:, None, :])
        & (source_row[:, None] == source_row[None, :])[None]
        & (tile_ids[:, None] > tile_ids[None, :])[None]
    )
    position = jnp.sum(earlier.astype(jnp.int32), axis=2)
    local_slot = source_row[None, :] * CAP + position

    my_target = jnp.take(target, my_group, axis=0)
    my_slot = my_target * slots + jnp.take(local_slot, my_group, axis=0)
    send_match = my_slot[None, :] == jnp.arange(groups * slots, dtype=jnp.int32)[:, None]
    send_index = jnp.where(
        jnp.any(send_match, axis=1),
        jnp.sum(jnp.where(send_match, tile_ids[None, :], 0), axis=1),
        group_tiles,
    )

    to_me = target == my_group
    slot_ids = jnp.arange(slots, dtype=jnp.int32)
    pick = to_me[:, None, :] & (local_slot[:, None, :] == slot_ids[None, :, None])
    recv_block = jnp.where(
        jnp.any(pick, axis=2), jnp.sum(jnp.where(pick, block[:, None, :], 0), axis=2), NT
    )
    recv_block = recv_block.reshape(n_lvl, n_pcol * slots)

    rhs_cols = lax.dynamic_slice_in_dim(rhs[0, 0], row_index * cols, cols, axis=1)
    window_blocks = width // block_rows
    acc = jnp.zeros((NT + 1, block_rows // 2, 2 * cols), jnp.float32)
    solved = jnp.zeros((width, cols), jnp.float32)
    for section in range(n_lvl):
        if section == 0:
            updates = first_cols
        else:
            right = rhs_cols - acc[:window_blocks].reshape(width, cols)
            solved_now = jnp.dot(
                inv_full, right.astype(jnp.bfloat16), preferred_element_type=jnp.float32
            )
            solved = jnp.where(level_index == section, solved_now, solved)
            updates = jnp.dot(
                tiles_full, solved_now.astype(jnp.bfloat16), preferred_element_type=jnp.float32
            ).astype(jnp.bfloat16)
        updates = updates.reshape(group_tiles + 1, block_rows // 2, 2 * cols)
        sending = jnp.take(updates, send_index, axis=0, mode="clip")
        incoming = lax.all_to_all(
            sending, ("lvl", "pcol"), split_axis=0, concat_axis=0, tiled=True
        )
        incoming = incoming.reshape(n_lvl, n_pcol * slots, block_rows // 2, 2 * cols)[section]
        acc = acc.at[recv_block[section]].add(incoming.astype(jnp.float32), mode="clip")
    outer = acc[window_blocks:NT].reshape(ABOVE, cols)

    solved_blocks = solved.reshape(n_prow, rows_out, cols)
    final = jnp.concatenate(
        [
            solved_blocks.astype(jnp.bfloat16),
            jnp.broadcast_to(outer.astype(jnp.bfloat16)[None], (n_prow, ABOVE, cols)),
        ],
        axis=1,
    )
    final = lax.all_to_all(final, "prow", split_axis=0, concat_axis=0, tiled=True)
    final = final.astype(jnp.float32)
    solution_rows = jnp.transpose(final[:, :rows_out], (1, 0, 2)).reshape(rows_out, columns_all)
    solution_rows = jnp.where(level_index == 0, first_rows, solution_rows)
    outer_all = jnp.transpose(final[:, rows_out:], (1, 0, 2)).reshape(ABOVE, columns_all)
    return (solution_rows[None, None], outer_all[None, None])


def solution(mesh):
    placed = (
        P("lvl", "pcol", None, None),
        P("lvl", "pcol", "prow", None),
        P("lvl", "pcol", "prow", None, None),
        P("lvl", "pcol", None),
        P("lvl", "pcol", "prow"),
        P("lvl", "pcol", "prow"),
        P("lvl", "pcol", "prow"),
    )
    return jax.shard_map(
        per_device,
        mesh=mesh,
        in_specs=placed,
        out_specs=(P("lvl", "pcol", "prow", None), P("lvl", "pcol", None, None)),
        check_vma=False,
    )
```
